32 devices in a mesh: gx: 4 (over x, core), gy: 8 (over z, y).
Axes of the slice: x: 2, y: 2, z: 4, core: 2. Of those that a mesh axis runs over, the one named last changes fastest.
Arguments:
- right_side: float32 [4, 1024, 2048], P(None, 'gx', 'gy')
- prior_weight: float32 [4, 1024, 2048], P(None, 'gx', 'gy'), may hold values from 0.5 to 4
- jacobi_inverse: float32 [4, 1024, 2048], P(None, 'gx', 'gy'), may hold values from 0.1 to 0.5
- interaction: float32 [2, 4, 128, 128], replicated, may hold values from -0.5 to 0.5
- footprint: int32 [2, 16, 16, 4], P(None, 'gx', 'gy'), may hold values from 0 to 255, as said below
Outputs:
- solution: float32 [4, 1024, 2048], P(None, 'gx', 'gy')
- residual: float32 [4, 1024, 2048], P(None, 'gx', 'gy')
The draws below stay inside these ranges and needn't reach their ends.
Inputs may be any that keep to these rules, and one draw needn't show every extreme that they name: `footprint`: each entry is bx * 16 + by of a block of the same 4 block rows along the first dimension as its ray block's tile. Of the 64 entries of one tile's ray blocks, between 7 and 9 fall in each tile of the same strip along the second dimension, exactly 9 in some; one tile of the second dimension receives exactly 9 entries from every tile of the strip.
All inputs are finite; a program needn't handle non-finite values.
Results may differ from the reference program's by a relative error of at most 0.0003.
Values sent between devices are 32-bit elements; how exact they have to be, the bound alone decides.
No kernel may reach another device: no remote copies, remote signals or barrier semaphores. Data moves between devices by JAX's collectives and lax.ppermute only.
A program may use at most 128 MiB of HBM per device.

```python
import math
import jax
import jax.numpy as jnp
from jax import lax

L = 4
S = 2
BX = 64
BY = 128
ITERS = 4
NX = 1024
NY = 2048
RBX = 4
RBY = 2
STRIPS = 4
OWNERS = 8
NBX = 16
NBY = 16
REQ = 64


def draw_right_side(key, part):
    rows_pos = jnp.arange(NX, dtype=jnp.float32) / NX
    cols_pos = jnp.arange(NY, dtype=jnp.float32) / NY
    scale = 10.0 ** (0.5 * (rows_pos[:, None] + cols_pos[None, :]))
    base_vals = jnp.clip(jax.random.normal(key, (L, NX, NY), jnp.float32), -6.0, 6.0)
    return base_vals * scale[None, :, :]


def draw_footprint(key, part):
    devices = STRIPS * OWNERS
    key_rank, key_order, key_local, key_common = jax.random.split(jax.random.fold_in(key, 7), 4)
    base_count = REQ // OWNERS
    quarter = OWNERS // 4
    owner_ids = jnp.arange(OWNERS, dtype=jnp.int32)
    common = jax.random.randint(key_common, (), 0, OWNERS)
    scores = jax.random.randint(key_rank, (devices, OWNERS), 0, 1 << 20) * OWNERS + owner_ids[None, :]
    scores = jnp.where(owner_ids[None, :] == common, -1, scores)
    ranking = jnp.argsort(jnp.argsort(scores, axis=1), axis=1)
    counts = base_count + (ranking < quarter).astype(jnp.int32) - ((ranking >= quarter) & (ranking < 2 * quarter)).astype(jnp.int32)
    ends = jnp.cumsum(counts, axis=1)
    position = jnp.arange(REQ, dtype=jnp.int32)
    target = jnp.sum((ends[:, None, :] <= position[None, :, None]).astype(jnp.int32), axis=2)
    shuffle = jax.random.randint(key_order, (devices, REQ), 0, 1 << 20) * REQ + position[None, :]
    order = jnp.argsort(shuffle, axis=1)
    target = jnp.take_along_axis(target, order, axis=1)
    local_block = jax.random.randint(key_local, (devices, REQ), 0, RBX * RBY)
    strip_of = jnp.arange(devices, dtype=jnp.int32) // OWNERS
    block_row = strip_of[:, None] * RBX + local_block // RBY
    block_col = target * RBY + local_block % RBY
    block_ids = block_row * NBY + block_col
    block_ids = block_ids.reshape(STRIPS, OWNERS, S, RBX, RBY, L).transpose(2, 0, 3, 1, 4, 5).reshape(S, NBX, NBY, L)
    return block_ids.astype(jnp.int32)


def shard_levels(stream_key, extent, pieces, least, largest):
    factor_of = 1.0
    for axis_at, shards_of in pieces:
        steps = jax.random.uniform(jax.random.fold_in(jax.random.fold_in(stream_key, 6), axis_at), (shards_of,), jnp.float32, least / len(pieces), largest / len(pieces))
        factor_of = factor_of * jnp.repeat(jnp.exp(steps), extent[axis_at] // shards_of).reshape((-1,) + (1,) * (len(extent) - 1 - axis_at))
    return factor_of


def normal_values(stream_key, extent, width, most, kind=jnp.bfloat16):
    entries = jax.random.normal(stream_key, extent, jnp.float32) * width
    return jnp.minimum(jnp.maximum(entries, -most), most).astype(kind)


def setup_inputs(seed: int = 0) -> dict:
    streams_of = jax.random.split(jax.random.key(seed), 6)
    right_side = draw_right_side(jax.random.fold_in(streams_of[5], 71), 0)
    prior_weight = jnp.clip(jnp.exp(math.log(4.0) - 2.0794415 * jax.random.uniform(streams_of[1], (L, NX, NY), jnp.float32) ** shard_levels(streams_of[1], (L, NX, NY), ((1, 4), (2, 8)), -0.2, 0.2)), 0.5, 4.0)
    jacobi_inverse = jnp.clip(jnp.exp(math.log(0.5) - 1.609438 * jax.random.uniform(streams_of[2], (L, NX, NY), jnp.float32) ** shard_levels(streams_of[2], (L, NX, NY), ((1, 4), (2, 8)), -0.2, 0.2)), 0.1, 0.5)
    interaction = normal_values(streams_of[3], (S, L, BY, BY), BY ** -0.5, 0.5, jnp.float32)
    footprint = draw_footprint(jax.random.fold_in(streams_of[5], 71), 0)
    return {"right_side": right_side, "prior_weight": prior_weight, "jacobi_inverse": jacobi_inverse, "interaction": interaction, "footprint": footprint}


DAUB_LOW = (0.3326705529509569, 0.8068915093133388, 0.4598775021193313, -0.13501102001039084, -0.08544127388224149, 0.035226291882100656)
DAUB_HIGH = tuple(((-1.0) ** tap_index) * DAUB_LOW[5 - tap_index] for tap_index in range(6))


def alternate(first_part, second_part, dimension):
    stacked = jnp.stack([first_part, second_part], axis=dimension + 1)
    new_shape = list(first_part.shape)
    new_shape[dimension] = 2 * first_part.shape[dimension]
    return stacked.reshape(new_shape)


def synth_axis(padded, dimension, coarse):
    length = 2 * coarse + 8
    even_part = lax.slice_in_dim(padded, 0, length, 2, dimension)
    odd_part = lax.slice_in_dim(padded, 1, length, 2, dimension)
    phases = []
    for phase in (0, 1):
        total = None
        for tap_num in range(3):
            low_cells = lax.slice_in_dim(even_part, 2 - tap_num, 2 - tap_num + coarse, 1, dimension)
            high_cells = lax.slice_in_dim(odd_part, 2 - tap_num, 2 - tap_num + coarse, 1, dimension)
            term = DAUB_LOW[2 * tap_num + phase] * low_cells + DAUB_HIGH[2 * tap_num + phase] * high_cells
            total = term if total is None else total + term
        phases.append(total)
    return alternate(phases[0], phases[1], dimension)


def analyze_axis(padded, dimension, coarse):
    length = 2 * coarse + 8
    even_part = lax.slice_in_dim(padded, 0, length, 2, dimension)
    odd_part = lax.slice_in_dim(padded, 1, length, 2, dimension)
    low_total = None
    high_total = None
    for tap_num in range(3):
        even_cells = lax.slice_in_dim(even_part, 2 + tap_num, 2 + tap_num + coarse, 1, dimension)
        odd_cells = lax.slice_in_dim(odd_part, 2 + tap_num, 2 + tap_num + coarse, 1, dimension)
        low_term = DAUB_LOW[2 * tap_num] * even_cells + DAUB_LOW[2 * tap_num + 1] * odd_cells
        high_term = DAUB_HIGH[2 * tap_num] * even_cells + DAUB_HIGH[2 * tap_num + 1] * odd_cells
        low_total = low_term if low_total is None else low_total + low_term
        high_total = high_term if high_total is None else high_total + high_term
    return alternate(low_total, high_total, dimension)


def reference(right_side, prior_weight, jacobi_inverse, interaction, footprint):
    highest = lax.Precision.HIGHEST

    def synthesize(coef):
        padded = jnp.pad(coef, ((0, 0), (4, 4), (4, 4)))
        return synth_axis(synth_axis(padded, 1, NX // 2), 2, NY // 2)

    def analyze(field):
        padded = jnp.pad(field, ((0, 0), (4, 4), (4, 4)))
        return analyze_axis(analyze_axis(padded, 2, NY // 2), 1, NX // 2)

    def project_back(field):
        blocks = field.reshape(L, NBX, BX, NBY, BY).transpose(0, 1, 3, 2, 4).reshape(L, NBX * NBY, BX, BY)
        slopes = jnp.zeros((S, NBX, NBY, BX, BY), jnp.float32)
        for layer in range(L):
            seen = blocks[layer][footprint[:, :, :, layer]]
            slopes = slopes + jnp.einsum("snmxy,syz->snmxz", seen, interaction[:, layer], precision=highest)
        result = jnp.zeros((L, NBX * NBY, BX, BY), jnp.float32)
        for layer in range(L):
            back = jnp.einsum("snmxz,syz->snmxy", slopes, interaction[:, layer], precision=highest)
            result = result.at[layer, footprint[:, :, :, layer].reshape(-1)].add(back.reshape(-1, BX, BY))
        return result.reshape(L, NBX, NBY, BX, BY).transpose(0, 1, 3, 2, 4).reshape(L, NX, NY)

    def apply_op(coef):
        return analyze(project_back(synthesize(coef))) + prior_weight * coef

    solution = jnp.zeros_like(right_side)
    residual = right_side
    precond_res = jacobi_inverse * residual
    direction = precond_res
    rho_now = jnp.sum(residual * precond_res)
    for step in range(ITERS):
        image = apply_op(direction)
        step_size = rho_now / jnp.sum(direction * image)
        solution = solution + step_size * direction
        residual = residual - step_size * image
        precond_res = jacobi_inverse * residual
        rho_next = jnp.sum(residual * precond_res)
        direction = precond_res + (rho_next / rho_now) * direction
        rho_now = rho_next
    return solution, residual
```

```python
import jax
import jax.numpy as jnp
from jax import lax
from jax.sharding import PartitionSpec as P

ITERS = 4


DAUB_LOW = (
    0.3326705529509569,
    0.8068915093133388,
    0.4598775021193313,
    -0.13501102001039084,
    -0.08544127388224149,
    0.035226291882100656,
)
DAUB_HIGH = tuple(((-1.0) ** tap_index * DAUB_LOW[5 - tap_index] for tap_index in range(6)))


def extended(block, sides, width):
    for axis, dim in sides:
        count = lax.axis_size(axis)
        forward = [(i, i + 1) for i in range(count - 1)]
        backward = [(target, source) for source, target in forward]
        low = lax.ppermute(
            lax.slice_in_dim(block, block.shape[dim] - width, None, axis=dim), axis, forward
        )
        high = lax.ppermute(lax.slice_in_dim(block, 0, width, axis=dim), axis, backward)
        block = jnp.concatenate([low, block, high], axis=dim)
    return block


def synth_table(length):
    inputs = jnp.arange(length + 8, dtype=jnp.int32)[:, None]
    outputs = jnp.arange(length, dtype=jnp.int32)[None, :]
    half = outputs // 2
    phase = outputs % 2
    table = jnp.zeros((length + 8, length), jnp.float32)
    for tap_num in range(3):
        low_coef = jnp.where(phase == 0, DAUB_LOW[2 * tap_num], DAUB_LOW[2 * tap_num + 1])
        high_coef = jnp.where(phase == 0, DAUB_HIGH[2 * tap_num], DAUB_HIGH[2 * tap_num + 1])
        table = table + jnp.where(inputs == 2 * (half - tap_num) + 4, low_coef, 0.0)
        table = table + jnp.where(inputs == 2 * (half - tap_num) + 5, high_coef, 0.0)
    return table


def analysis_table(length):
    inputs = jnp.arange(length + 8, dtype=jnp.int32)[:, None]
    outputs = jnp.arange(length, dtype=jnp.int32)[None, :]
    half = outputs // 2
    phase = outputs % 2
    table = jnp.zeros((length + 8, length), jnp.float32)
    for tap_num in range(3):
        for offset in (0, 1):
            coef = jnp.where(
                phase == 0, DAUB_LOW[2 * tap_num + offset], DAUB_HIGH[2 * tap_num + offset]
            )
            table = table + jnp.where(inputs == 2 * (half + tap_num) + offset + 4, coef, 0.0)
    return table


def butterfly_sum(value, axis):
    count = lax.axis_size(axis)
    if count & (count - 1):
        return lax.psum(value, axis)
    stride = 1
    while stride < count:
        value = value + lax.ppermute(value, axis, [(i, i ^ stride) for i in range(count)])
        stride *= 2
    return value


def global_sum(local_value):
    return butterfly_sum(butterfly_sum(local_value, "gx"), "gy")


def with_rim(field):
    return extended(field, (("gx", 1), ("gy", 2)), 4)


def shards(right_side, prior_weight, jacobi_inverse, interaction, footprint):
    highest = lax.Precision.HIGHEST
    layers, tile_rows, tile_cols = right_side.shape
    sensors, rows_blocks, cols_blocks = (footprint.shape[0], footprint.shape[1], footprint.shape[2])
    block_rows = tile_rows // rows_blocks
    block_cols = tile_cols // cols_blocks
    owners = lax.axis_size("gy")
    layer_blocks_cols = cols_blocks * owners
    requests = sensors * rows_blocks * cols_blocks * layers
    capacity = requests // owners + 1
    own_blocks = layers * rows_blocks * cols_blocks
    synth_rows = synth_table(tile_rows)
    synth_cols = synth_table(tile_cols)
    analysis_rows = analysis_table(tile_rows)
    analysis_cols = analysis_table(tile_cols)
    flat_ids = footprint.reshape(requests)
    request_num = jnp.arange(requests, dtype=jnp.int32)
    layer_of = request_num % layers
    sensor_of = request_num // (requests // sensors)
    target = flat_ids % layer_blocks_cols // cols_blocks
    owned_index = (
        layer_of * (rows_blocks * cols_blocks)
        + flat_ids // layer_blocks_cols % rows_blocks * cols_blocks
        + flat_ids % layer_blocks_cols % cols_blocks
    )
    picks = (target[:, None] == jnp.arange(owners, dtype=jnp.int32)[None, :]).astype(jnp.int32)
    slot = jnp.sum(picks * (jnp.cumsum(picks, axis=0) - 1), axis=1)
    send_ids = jnp.full((owners, capacity), own_blocks, jnp.int32).at[target, slot].set(owned_index)
    send_pairs = (
        jnp.zeros((owners, capacity), jnp.int32).at[target, slot].set(sensor_of * layers + layer_of)
    )
    wanted_ids, wanted_pairs = (
        lax.all_to_all(send_ids, "gy", split_axis=0, concat_axis=0, tiled=True),
        lax.all_to_all(send_pairs, "gy", split_axis=0, concat_axis=0, tiled=True),
    )
    slot_source = (
        jnp.full((owners, capacity), requests, jnp.int32).at[target, slot].set(request_num)
    )
    landing = (
        wanted_ids.reshape(-1)[None, :] == jnp.arange(own_blocks, dtype=jnp.int32)[:, None]
    ).astype(jnp.float32)
    def apply_op(direction):
        synthesize_padded = with_rim(direction)
        along_rows = jnp.einsum("lab,ac->lcb", synthesize_padded, synth_rows, precision=highest)
        blocks = (
            jnp.einsum("lab,bc->lac", along_rows, synth_cols, precision=highest)
            .reshape(layers, rows_blocks, block_rows, cols_blocks, block_cols)
            .transpose(0, 1, 3, 2, 4)
            .reshape(own_blocks, block_rows, block_cols)
        )
        outgoing = jnp.take(blocks, wanted_ids, axis=0, mode="fill", fill_value=0.0)
        arrived = lax.all_to_all(outgoing, "gy", split_axis=0, concat_axis=0, tiled=True)
        seen = arrived[target, slot].reshape(
            sensors, rows_blocks * cols_blocks, layers, block_rows, block_cols
        )
        slopes = jnp.einsum("sklxy,slyz->skxz", seen, interaction, precision=highest)
        back = jnp.einsum("skxz,slyz->sklxy", slopes, interaction, precision=highest).reshape(
            requests, block_rows, block_cols
        )
        returning = jnp.take(back, slot_source, axis=0, mode="fill", fill_value=0.0)
        landed = lax.all_to_all(returning, "gy", split_axis=0, concat_axis=0, tiled=True)
        summed = jnp.dot(
            landing, landed.reshape(owners * capacity, block_rows * block_cols), precision=highest
        )
        padded = with_rim(
            summed.reshape(layers, rows_blocks, cols_blocks, block_rows, block_cols)
            .transpose(0, 1, 3, 2, 4)
            .reshape(layers, tile_rows, tile_cols)
        )
        along_cols = jnp.einsum("lab,bc->lac", padded, analysis_cols, precision=highest)
        return (
            jnp.einsum("lab,ac->lcb", along_cols, analysis_rows, precision=highest)
            + prior_weight * direction
        )

    solution = jnp.zeros_like(right_side)
    residual = right_side
    precond_res = jacobi_inverse * residual
    direction = precond_res
    rho_now = global_sum(jnp.sum(residual * precond_res))
    image = apply_op(direction)
    for step in range(ITERS):
        step_size = rho_now / global_sum(jnp.sum(direction * image))
        solution = solution + step_size * direction
        residual = residual - step_size * image
        if step + 1 < ITERS:
            precond_res = jacobi_inverse * residual
            rho_next = global_sum(jnp.sum(residual * precond_res))
            applied = apply_op(precond_res)
            ratio = rho_next / rho_now
            direction = precond_res + ratio * direction
            image = applied + ratio * image
            rho_now = rho_next
    return (solution, residual)


def solution(mesh):
    return jax.shard_map(
        shards,
        mesh=mesh,
        in_specs=(
            P(None, "gx", "gy"),
            P(None, "gx", "gy"),
            P(None, "gx", "gy"),
            P(),
            P(None, "gx", "gy", None),
        ),
        out_specs=(P(None, "gx", "gy"), P(None, "gx", "gy")),
        check_vma=False,
    )
```

```python
import jax
import jax.numpy as jnp
from jax import lax
from jax.sharding import PartitionSpec as P

ITERS = 4


DAUB_LOW = (
    0.3326705529509569,
    0.8068915093133388,
    0.4598775021193313,
    -0.13501102001039084,
    -0.08544127388224149,
    0.035226291882100656,
)
DAUB_HIGH = tuple(((-1.0) ** tap_index * DAUB_LOW[5 - tap_index] for tap_index in range(6)))


def extended(block, sides, width):
    for axis, dim in sides:
        count = lax.axis_size(axis)
        forward = [(i, i + 1) for i in range(count - 1)]
        backward = [(target, source) for source, target in forward]
        low = lax.ppermute(
            lax.slice_in_dim(block, block.shape[dim] - width, None, axis=dim), axis, forward
        )
        high = lax.ppermute(lax.slice_in_dim(block, 0, width, axis=dim), axis, backward)
        block = jnp.concatenate([low, block, high], axis=dim)
    return block


def synth_table(length):
    inputs = jnp.arange(length + 8, dtype=jnp.int32)[:, None]
    outputs = jnp.arange(length, dtype=jnp.int32)[None, :]
    half = outputs // 2
    phase = outputs % 2
    table = jnp.zeros((length + 8, length), jnp.float32)
    for tap_num in range(3):
        low_coef = jnp.where(phase == 0, DAUB_LOW[2 * tap_num], DAUB_LOW[2 * tap_num + 1])
        high_coef = jnp.where(phase == 0, DAUB_HIGH[2 * tap_num], DAUB_HIGH[2 * tap_num + 1])
        table = table + jnp.where(inputs == 2 * (half - tap_num) + 4, low_coef, 0.0)
        table = table + jnp.where(inputs == 2 * (half - tap_num) + 5, high_coef, 0.0)
    return table


def analysis_table(length):
    inputs = jnp.arange(length + 8, dtype=jnp.int32)[:, None]
    outputs = jnp.arange(length, dtype=jnp.int32)[None, :]
    half = outputs // 2
    phase = outputs % 2
    table = jnp.zeros((length + 8, length), jnp.float32)
    for tap_num in range(3):
        for offset in (0, 1):
            coef = jnp.where(
                phase == 0, DAUB_LOW[2 * tap_num + offset], DAUB_HIGH[2 * tap_num + offset]
            )
            table = table + jnp.where(inputs == 2 * (half + tap_num) + offset + 4, coef, 0.0)
    return table


def butterfly_sum(value, axis):
    count = lax.axis_size(axis)
    if count & (count - 1):
        return lax.psum(value, axis)
    stride = 1
    while stride < count:
        value = value + lax.ppermute(value, axis, [(i, i ^ stride) for i in range(count)])
        stride *= 2
    return value


def sum_steps(axes):
    steps = []
    for axis in axes:
        count = lax.axis_size(axis)
        if count & (count - 1):
            steps.append(lambda value, axis=axis: lax.psum(value, axis))
            continue
        stride = 1
        while stride < count:
            pairs = [(i, i ^ stride) for i in range(count)]
            steps.append(lambda value, axis=axis, pairs=pairs: value + lax.ppermute(value, axis, pairs))
            stride *= 2
    return steps


def global_sum(local_value):
    for step in sum_steps(("gx", "gy")):
        local_value = step(local_value)
    return local_value


def advance(carry, value):
    total, steps = carry
    if steps:
        total = steps[0](total)
        steps = steps[1:]
    total, value = lax.optimization_barrier((total, value))
    return (total, steps), value


def finish(carry):
    total, steps = carry
    for step in steps:
        total = step(total)
    return total


def with_rim(field):
    return extended(field, (("gx", 1), ("gy", 2)), 4)


def shards(right_side, prior_weight, jacobi_inverse, interaction, footprint):
    highest = lax.Precision.HIGHEST
    layers, tile_rows, tile_cols = right_side.shape
    sensors, rows_blocks, cols_blocks = (footprint.shape[0], footprint.shape[1], footprint.shape[2])
    block_rows = tile_rows // rows_blocks
    block_cols = tile_cols // cols_blocks
    owners = lax.axis_size("gy")
    layer_blocks_cols = cols_blocks * owners
    requests = sensors * rows_blocks * cols_blocks * layers
    capacity = requests // owners + 1
    own_blocks = layers * rows_blocks * cols_blocks
    synth_rows = synth_table(tile_rows)
    synth_cols = synth_table(tile_cols)
    analysis_rows = analysis_table(tile_rows)
    analysis_cols = analysis_table(tile_cols)
    flat_ids = footprint.reshape(requests)
    request_num = jnp.arange(requests, dtype=jnp.int32)
    layer_of = request_num % layers
    sensor_of = request_num // (requests // sensors)
    target = flat_ids % layer_blocks_cols // cols_blocks
    owned_index = (
        layer_of * (rows_blocks * cols_blocks)
        + flat_ids // layer_blocks_cols % rows_blocks * cols_blocks
        + flat_ids % layer_blocks_cols % cols_blocks
    )
    picks = (target[:, None] == jnp.arange(owners, dtype=jnp.int32)[None, :]).astype(jnp.int32)
    slot = jnp.sum(picks * (jnp.cumsum(picks, axis=0) - 1), axis=1)
    send_ids = jnp.full((owners, capacity), own_blocks, jnp.int32).at[target, slot].set(owned_index)
    send_pairs = (
        jnp.zeros((owners, capacity), jnp.int32).at[target, slot].set(sensor_of * layers + layer_of)
    )
    wanted_ids, wanted_pairs = (
        lax.all_to_all(send_ids, "gy", split_axis=0, concat_axis=0, tiled=True),
        lax.all_to_all(send_pairs, "gy", split_axis=0, concat_axis=0, tiled=True),
    )
    slot_source = (
        jnp.full((owners, capacity), requests, jnp.int32).at[target, slot].set(request_num)
    )
    landing = (
        wanted_ids.reshape(-1)[None, :] == jnp.arange(own_blocks, dtype=jnp.int32)[:, None]
    ).astype(jnp.float32)
    def apply_op(direction, carry):
        synthesize_padded = with_rim(direction)
        carry, synthesize_padded = advance(carry, synthesize_padded)
        along_rows = jnp.einsum("lab,ac->lcb", synthesize_padded, synth_rows, precision=highest)
        blocks = (
            jnp.einsum("lab,bc->lac", along_rows, synth_cols, precision=highest)
            .reshape(layers, rows_blocks, block_rows, cols_blocks, block_cols)
            .transpose(0, 1, 3, 2, 4)
            .reshape(own_blocks, block_rows, block_cols)
        )
        outgoing = jnp.take(blocks, wanted_ids, axis=0, mode="fill", fill_value=0.0)
        carry, outgoing = advance(carry, outgoing)
        arrived = lax.all_to_all(outgoing, "gy", split_axis=0, concat_axis=0, tiled=True)
        carry, arrived = advance(carry, arrived)
        seen = arrived[target, slot].reshape(
            sensors, rows_blocks * cols_blocks, layers, block_rows, block_cols
        )
        slopes = jnp.einsum("sklxy,slyz->skxz", seen, interaction, precision=highest)
        back = jnp.einsum("skxz,slyz->sklxy", slopes, interaction, precision=highest).reshape(
            requests, block_rows, block_cols
        )
        returning = jnp.take(back, slot_source, axis=0, mode="fill", fill_value=0.0)
        carry, returning = advance(carry, returning)
        landed = lax.all_to_all(returning, "gy", split_axis=0, concat_axis=0, tiled=True)
        carry, landed = advance(carry, landed)
        summed = jnp.dot(
            landing, landed.reshape(owners * capacity, block_rows * block_cols), precision=highest
        )
        padded = with_rim(
            summed.reshape(layers, rows_blocks, cols_blocks, block_rows, block_cols)
            .transpose(0, 1, 3, 2, 4)
            .reshape(layers, tile_rows, tile_cols)
        )
        along_cols = jnp.einsum("lab,bc->lac", padded, analysis_cols, precision=highest)
        return (
            jnp.einsum("lab,ac->lcb", along_cols, analysis_rows, precision=highest)
            + prior_weight * direction
        ), finish(carry)

    solution = jnp.zeros_like(right_side)
    residual = right_side
    precond_res = jacobi_inverse * residual
    direction = precond_res
    image, rho_now = apply_op(direction, (jnp.sum(residual * precond_res), sum_steps(("gx", "gy"))))
    for step in range(ITERS):
        step_size = rho_now / global_sum(jnp.sum(direction * image))
        solution = solution + step_size * direction
        residual = residual - step_size * image
        if step + 1 < ITERS:
            precond_res = jacobi_inverse * residual
            applied, rho_next = apply_op(
                precond_res, (jnp.sum(residual * precond_res), sum_steps(("gx", "gy")))
            )
            ratio = rho_next / rho_now
            direction = precond_res + ratio * direction
            image = applied + ratio * image
            rho_now = rho_next
    return (solution, residual)


def solution(mesh):
    return jax.shard_map(
        shards,
        mesh=mesh,
        in_specs=(
            P(None, "gx", "gy"),
            P(None, "gx", "gy"),
            P(None, "gx", "gy"),
            P(),
            P(None, "gx", "gy", None),
        ),
        out_specs=(P(None, "gx", "gy"), P(None, "gx", "gy")),
        check_vma=False,
    )
```

```python
import jax
import jax.numpy as jnp
from jax import lax
from jax.sharding import PartitionSpec as P

ITERS = 4


DAUB_LOW = (
    0.3326705529509569,
    0.8068915093133388,
    0.4598775021193313,
    -0.13501102001039084,
    -0.08544127388224149,
    0.035226291882100656,
)
DAUB_HIGH = tuple(((-1.0) ** tap_index * DAUB_LOW[5 - tap_index] for tap_index in range(6)))


def extended(block, sides, width):
    for axis, dim in sides:
        count = lax.axis_size(axis)
        forward = [(i, i + 1) for i in range(count - 1)]
        backward = [(target, source) for source, target in forward]
        low = lax.ppermute(
            lax.slice_in_dim(block, block.shape[dim] - width, None, axis=dim), axis, forward
        )
        high = lax.ppermute(lax.slice_in_dim(block, 0, width, axis=dim), axis, backward)
        block = jnp.concatenate([low, block, high], axis=dim)
    return block


def synth_table(length):
    inputs = jnp.arange(length + 8, dtype=jnp.int32)[:, None]
    outputs = jnp.arange(length, dtype=jnp.int32)[None, :]
    half = outputs // 2
    phase = outputs % 2
    table = jnp.zeros((length + 8, length), jnp.float32)
    for tap_num in range(3):
        low_coef = jnp.where(phase == 0, DAUB_LOW[2 * tap_num], DAUB_LOW[2 * tap_num + 1])
        high_coef = jnp.where(phase == 0, DAUB_HIGH[2 * tap_num], DAUB_HIGH[2 * tap_num + 1])
        table = table + jnp.where(inputs == 2 * (half - tap_num) + 4, low_coef, 0.0)
        table = table + jnp.where(inputs == 2 * (half - tap_num) + 5, high_coef, 0.0)
    return table


def analysis_table(length):
    inputs = jnp.arange(length + 8, dtype=jnp.int32)[:, None]
    outputs = jnp.arange(length, dtype=jnp.int32)[None, :]
    half = outputs // 2
    phase = outputs % 2
    table = jnp.zeros((length + 8, length), jnp.float32)
    for tap_num in range(3):
        for offset in (0, 1):
            coef = jnp.where(
                phase == 0, DAUB_LOW[2 * tap_num + offset], DAUB_HIGH[2 * tap_num + offset]
            )
            table = table + jnp.where(inputs == 2 * (half + tap_num) + offset + 4, coef, 0.0)
    return table


def butterfly_sum(value, axis):
    count = lax.axis_size(axis)
    if count & (count - 1):
        return lax.psum(value, axis)
    stride = 1
    while stride < count:
        value = value + lax.ppermute(value, axis, [(i, i ^ stride) for i in range(count)])
        stride *= 2
    return value


def sum_steps(axes):
    steps = []
    for axis in axes:
        count = lax.axis_size(axis)
        if count & (count - 1):
            steps.append(lambda value, axis=axis: lax.psum(value, axis))
            continue
        stride = 1
        while stride < count:
            pairs = [(i, i ^ stride) for i in range(count)]
            steps.append(lambda value, axis=axis, pairs=pairs: value + lax.ppermute(value, axis, pairs))
            stride *= 2
    return steps


def global_sum(local_value):
    for step in sum_steps(("gx", "gy")):
        local_value = step(local_value)
    return local_value


def advance(carry, value, step=True):
    total, steps = carry
    if step and steps:
        total = steps[0](total)
        steps = steps[1:]
    total, value = lax.optimization_barrier((total, value))
    return (total, steps), value


def finish(carry):
    total, steps = carry
    for step in steps:
        total = step(total)
    return total


def with_rim(field):
    return extended(field, (("gx", 1), ("gy", 2)), 4)


def shards(right_side, prior_weight, jacobi_inverse, interaction, footprint):
    highest = lax.Precision.HIGHEST
    layers, tile_rows, tile_cols = right_side.shape
    sensors, rows_blocks, cols_blocks = (footprint.shape[0], footprint.shape[1], footprint.shape[2])
    block_rows = tile_rows // rows_blocks
    block_cols = tile_cols // cols_blocks
    owners = lax.axis_size("gy")
    layer_blocks_cols = cols_blocks * owners
    requests = sensors * rows_blocks * cols_blocks * layers
    capacity = requests // owners + 1
    own_blocks = layers * rows_blocks * cols_blocks
    synth_rows = synth_table(tile_rows)
    synth_cols = synth_table(tile_cols)
    analysis_rows = analysis_table(tile_rows)
    analysis_cols = analysis_table(tile_cols)
    flat_ids = footprint.reshape(requests)
    request_num = jnp.arange(requests, dtype=jnp.int32)
    layer_of = request_num % layers
    sensor_of = request_num // (requests // sensors)
    target = flat_ids % layer_blocks_cols // cols_blocks
    owned_index = (
        layer_of * (rows_blocks * cols_blocks)
        + flat_ids // layer_blocks_cols % rows_blocks * cols_blocks
        + flat_ids % layer_blocks_cols % cols_blocks
    )
    picks = (target[:, None] == jnp.arange(owners, dtype=jnp.int32)[None, :]).astype(jnp.int32)
    slot = jnp.sum(picks * (jnp.cumsum(picks, axis=0) - 1), axis=1)
    send_ids = jnp.full((owners, capacity), own_blocks, jnp.int32).at[target, slot].set(owned_index)
    send_pairs = (
        jnp.zeros((owners, capacity), jnp.int32).at[target, slot].set(sensor_of * layers + layer_of)
    )
    wanted_ids, wanted_pairs = (
        lax.all_to_all(send_ids, "gy", split_axis=0, concat_axis=0, tiled=True),
        lax.all_to_all(send_pairs, "gy", split_axis=0, concat_axis=0, tiled=True),
    )
    slot_source = (
        jnp.full((owners, capacity), requests, jnp.int32).at[target, slot].set(request_num)
    )
    landing = (
        wanted_ids.reshape(-1)[None, :] == jnp.arange(own_blocks, dtype=jnp.int32)[:, None]
    ).astype(jnp.float32)
    def apply_op(direction, carry):
        synthesize_padded = with_rim(direction)
        carry, synthesize_padded = advance(carry, synthesize_padded)
        along_rows = jnp.einsum("lab,ac->lcb", synthesize_padded, synth_rows, precision=highest)
        blocks = (
            jnp.einsum("lab,bc->lac", along_rows, synth_cols, precision=highest)
            .reshape(layers, rows_blocks, block_rows, cols_blocks, block_cols)
            .transpose(0, 1, 3, 2, 4)
            .reshape(own_blocks, block_rows, block_cols)
        )
        blocks = jnp.concatenate([blocks, jnp.zeros((1, block_rows, block_cols), blocks.dtype)])
        outgoing = jnp.take(blocks, wanted_ids, axis=0, mode="clip")
        carry, outgoing = advance(carry, outgoing)
        arrived = lax.all_to_all(outgoing, "gy", split_axis=0, concat_axis=0, tiled=True)
        carry, arrived = advance(carry, arrived, step=False)
        seen = arrived[target, slot].reshape(
            sensors, rows_blocks * cols_blocks, layers, block_rows, block_cols
        )
        slopes = jnp.einsum("sklxy,slyz->skxz", seen, interaction, precision=highest)
        back = jnp.einsum("skxz,slyz->sklxy", slopes, interaction, precision=highest).reshape(
            requests, block_rows, block_cols
        )
        back = jnp.concatenate([back, jnp.zeros((1, block_rows, block_cols), back.dtype)])
        returning = jnp.take(back, slot_source, axis=0, mode="clip")
        carry, returning = advance(carry, returning)
        landed = lax.all_to_all(returning, "gy", split_axis=0, concat_axis=0, tiled=True)
        carry, landed = advance(carry, landed, step=False)
        summed = jnp.dot(
            landing, landed.reshape(owners * capacity, block_rows * block_cols), precision=highest
        )
        padded = with_rim(
            summed.reshape(layers, rows_blocks, cols_blocks, block_rows, block_cols)
            .transpose(0, 1, 3, 2, 4)
            .reshape(layers, tile_rows, tile_cols)
        )
        carry, padded = advance(carry, padded)
        along_cols = jnp.einsum("lab,bc->lac", padded, analysis_cols, precision=highest)
        return (
            jnp.einsum("lab,ac->lcb", along_cols, analysis_rows, precision=highest)
            + prior_weight * direction
        ), finish(carry)

    solution = jnp.zeros_like(right_side)
    residual = right_side
    precond_res = jacobi_inverse * residual
    direction = precond_res
    image, rho_now = apply_op(direction, (jnp.sum(residual * precond_res), sum_steps(("gx", "gy"))))
    for step in range(ITERS):
        step_size = rho_now / global_sum(jnp.sum(direction * image))
        solution = solution + step_size * direction
        residual = residual - step_size * image
        if step + 1 < ITERS:
            precond_res = jacobi_inverse * residual
            applied, rho_next = apply_op(
                precond_res, (jnp.sum(residual * precond_res), sum_steps(("gx", "gy")))
            )
            ratio = rho_next / rho_now
            direction = precond_res + ratio * direction
            image = applied + ratio * image
            rho_now = rho_next
    return (solution, residual)


def solution(mesh):
    return jax.shard_map(
        shards,
        mesh=mesh,
        in_specs=(
            P(None, "gx", "gy"),
            P(None, "gx", "gy"),
            P(None, "gx", "gy"),
            P(),
            P(None, "gx", "gy", None),
        ),
        out_specs=(P(None, "gx", "gy"), P(None, "gx", "gy")),
        check_vma=False,
    )
```

```python
import jax
import jax.numpy as jnp
from jax import lax
from jax.sharding import PartitionSpec as P

ITERS = 4


DAUB_LOW = (
    0.3326705529509569,
    0.8068915093133388,
    0.4598775021193313,
    -0.13501102001039084,
    -0.08544127388224149,
    0.035226291882100656,
)
DAUB_HIGH = tuple(((-1.0) ** tap_index * DAUB_LOW[5 - tap_index] for tap_index in range(6)))


def extended(block, sides, width):
    for axis, dim in sides:
        count = lax.axis_size(axis)
        forward = [(i, i + 1) for i in range(count - 1)]
        backward = [(target, source) for source, target in forward]
        low = lax.ppermute(
            lax.slice_in_dim(block, block.shape[dim] - width, None, axis=dim), axis, forward
        )
        high = lax.ppermute(lax.slice_in_dim(block, 0, width, axis=dim), axis, backward)
        block = jnp.concatenate([low, block, high], axis=dim)
    return block


def synth_table(length):
    inputs = jnp.arange(length + 8, dtype=jnp.int32)[:, None]
    outputs = jnp.arange(length, dtype=jnp.int32)[None, :]
    half = outputs // 2
    phase = outputs % 2
    table = jnp.zeros((length + 8, length), jnp.float32)
    for tap_num in range(3):
        low_coef = jnp.where(phase == 0, DAUB_LOW[2 * tap_num], DAUB_LOW[2 * tap_num + 1])
        high_coef = jnp.where(phase == 0, DAUB_HIGH[2 * tap_num], DAUB_HIGH[2 * tap_num + 1])
        table = table + jnp.where(inputs == 2 * (half - tap_num) + 4, low_coef, 0.0)
        table = table + jnp.where(inputs == 2 * (half - tap_num) + 5, high_coef, 0.0)
    return table


def analysis_table(length):
    inputs = jnp.arange(length + 8, dtype=jnp.int32)[:, None]
    outputs = jnp.arange(length, dtype=jnp.int32)[None, :]
    half = outputs // 2
    phase = outputs % 2
    table = jnp.zeros((length + 8, length), jnp.float32)
    for tap_num in range(3):
        for offset in (0, 1):
            coef = jnp.where(
                phase == 0, DAUB_LOW[2 * tap_num + offset], DAUB_HIGH[2 * tap_num + offset]
            )
            table = table + jnp.where(inputs == 2 * (half + tap_num) + offset + 4, coef, 0.0)
    return table


def butterfly_sum(value, axis):
    count = lax.axis_size(axis)
    if count & (count - 1):
        return lax.psum(value, axis)
    stride = 1
    while stride < count:
        value = value + lax.ppermute(value, axis, [(i, i ^ stride) for i in range(count)])
        stride *= 2
    return value


def sum_steps(axes):
    steps = []
    for axis in axes:
        count = lax.axis_size(axis)
        if count & (count - 1):
            steps.append(lambda value, axis=axis: lax.psum(value, axis))
            continue
        stride = 1
        while stride < count:
            pairs = [(i, i ^ stride) for i in range(count)]
            steps.append(lambda value, axis=axis, pairs=pairs: value + lax.ppermute(value, axis, pairs))
            stride *= 2
    return steps


def global_sum(local_value):
    for step in sum_steps(("gx", "gy")):
        local_value = step(local_value)
    return local_value


def advance(carry, value, step=True):
    total, steps = carry
    if step and steps:
        total = steps[0](total)
        steps = steps[1:]
    total, value = lax.optimization_barrier((total, value))
    return (total, steps), value


def finish(carry):
    total, steps = carry
    for step in steps:
        total = step(total)
    return total


def with_rim(field, width=4):
    return extended(field, (("gx", 1), ("gy", 2)), width)


def interior(field):
    return field[:, 4:-4, 4:-4]


def shards(right_side, prior_weight, jacobi_inverse, interaction, footprint):
    highest = lax.Precision.HIGHEST
    layers, tile_rows, tile_cols = right_side.shape
    sensors, rows_blocks, cols_blocks = (footprint.shape[0], footprint.shape[1], footprint.shape[2])
    block_rows = tile_rows // rows_blocks
    block_cols = tile_cols // cols_blocks
    owners = lax.axis_size("gy")
    layer_blocks_cols = cols_blocks * owners
    requests = sensors * rows_blocks * cols_blocks * layers
    capacity = requests // owners + 1
    own_blocks = layers * rows_blocks * cols_blocks
    synth_rows = synth_table(tile_rows)
    synth_cols = synth_table(tile_cols)
    analysis_rows = analysis_table(tile_rows + 8)
    analysis_cols = analysis_table(tile_cols + 8)
    flat_ids = footprint.reshape(requests)
    request_num = jnp.arange(requests, dtype=jnp.int32)
    layer_of = request_num % layers
    sensor_of = request_num // (requests // sensors)
    target = flat_ids % layer_blocks_cols // cols_blocks
    owned_index = (
        layer_of * (rows_blocks * cols_blocks)
        + flat_ids // layer_blocks_cols % rows_blocks * cols_blocks
        + flat_ids % layer_blocks_cols % cols_blocks
    )
    picks = (target[:, None] == jnp.arange(owners, dtype=jnp.int32)[None, :]).astype(jnp.int32)
    slot = jnp.sum(picks * (jnp.cumsum(picks, axis=0) - 1), axis=1)
    send_ids = jnp.full((owners, capacity), own_blocks, jnp.int32).at[target, slot].set(owned_index)
    send_pairs = (
        jnp.zeros((owners, capacity), jnp.int32).at[target, slot].set(sensor_of * layers + layer_of)
    )
    wanted_ids, wanted_pairs = (
        lax.all_to_all(send_ids, "gy", split_axis=0, concat_axis=0, tiled=True),
        lax.all_to_all(send_pairs, "gy", split_axis=0, concat_axis=0, tiled=True),
    )
    slot_source = (
        jnp.full((owners, capacity), requests, jnp.int32).at[target, slot].set(request_num)
    )
    landing = (
        wanted_ids.reshape(-1)[None, :] == jnp.arange(own_blocks, dtype=jnp.int32)[:, None]
    ).astype(jnp.float32)
    def apply_op(direction, carry):
        carry, synthesize_padded = advance(carry, direction)
        along_rows = jnp.einsum("lab,ac->lcb", synthesize_padded, synth_rows, precision=highest)
        blocks = (
            jnp.einsum("lab,bc->lac", along_rows, synth_cols, precision=highest)
            .reshape(layers, rows_blocks, block_rows, cols_blocks, block_cols)
            .transpose(0, 1, 3, 2, 4)
            .reshape(own_blocks, block_rows, block_cols)
        )
        blocks = jnp.concatenate([blocks, jnp.zeros((1, block_rows, block_cols), blocks.dtype)])
        outgoing = jnp.take(blocks, wanted_ids, axis=0, mode="clip")
        carry, outgoing = advance(carry, outgoing)
        arrived = lax.all_to_all(outgoing, "gy", split_axis=0, concat_axis=0, tiled=True)
        carry, arrived = advance(carry, arrived, step=False)
        seen = arrived[target, slot].reshape(
            sensors, rows_blocks * cols_blocks, layers, block_rows, block_cols
        )
        slopes = jnp.einsum("sklxy,slyz->skxz", seen, interaction, precision=highest)
        back = jnp.einsum("skxz,slyz->sklxy", slopes, interaction, precision=highest).reshape(
            requests, block_rows, block_cols
        )
        back = jnp.concatenate([back, jnp.zeros((1, block_rows, block_cols), back.dtype)])
        returning = jnp.take(back, slot_source, axis=0, mode="clip")
        carry, returning = advance(carry, returning)
        landed = lax.all_to_all(returning, "gy", split_axis=0, concat_axis=0, tiled=True)
        carry, landed = advance(carry, landed, step=False)
        summed = jnp.dot(
            landing, landed.reshape(owners * capacity, block_rows * block_cols), precision=highest
        )
        padded = with_rim(
            summed.reshape(layers, rows_blocks, cols_blocks, block_rows, block_cols)
            .transpose(0, 1, 3, 2, 4)
            .reshape(layers, tile_rows, tile_cols),
            8,
        )
        carry, padded = advance(carry, padded)
        along_cols = jnp.einsum("lab,bc->lac", padded, analysis_cols, precision=highest)
        return (
            jnp.einsum("lab,ac->lcb", along_cols, analysis_rows, precision=highest)
            + prior_weight * direction
        ), finish(carry)

    rims = with_rim(jnp.concatenate([right_side, jacobi_inverse, prior_weight]))
    residual, jacobi_inverse, prior_weight = jnp.split(rims, 3)
    solution = jnp.zeros_like(right_side)
    precond_res = jacobi_inverse * residual
    direction = interior(precond_res)
    image, rho_now = apply_op(
        precond_res,
        (jnp.sum(interior(residual) * direction), sum_steps(("gx", "gy"))),
    )
    for step in range(ITERS):
        step_size = rho_now / global_sum(jnp.sum(direction * interior(image)))
        solution = solution + step_size * direction
        residual = residual - step_size * image
        if step + 1 < ITERS:
            precond_res = jacobi_inverse * residual
            applied, rho_next = apply_op(
                precond_res,
                (
                    jnp.sum(interior(residual) * interior(precond_res)),
                    sum_steps(("gx", "gy")),
                ),
            )
            ratio = rho_next / rho_now
            direction = interior(precond_res) + ratio * direction
            image = applied + ratio * image
            rho_now = rho_next
    residual = interior(residual)
    return (solution, residual)


def solution(mesh):
    return jax.shard_map(
        shards,
        mesh=mesh,
        in_specs=(
            P(None, "gx", "gy"),
            P(None, "gx", "gy"),
            P(None, "gx", "gy"),
            P(),
            P(None, "gx", "gy", None),
        ),
        out_specs=(P(None, "gx", "gy"), P(None, "gx", "gy")),
        check_vma=False,
    )
```

```python
import jax
import jax.numpy as jnp
from jax import lax
from jax.sharding import PartitionSpec as P

ITERS = 4


DAUB_LOW = (
    0.3326705529509569,
    0.8068915093133388,
    0.4598775021193313,
    -0.13501102001039084,
    -0.08544127388224149,
    0.035226291882100656,
)
DAUB_HIGH = tuple(((-1.0) ** tap_index * DAUB_LOW[5 - tap_index] for tap_index in range(6)))


def extended(block, sides, width):
    for axis, dim in sides:
        count = lax.axis_size(axis)
        forward = [(i, i + 1) for i in range(count - 1)]
        backward = [(target, source) for source, target in forward]
        low = lax.ppermute(
            lax.slice_in_dim(block, block.shape[dim] - width, None, axis=dim), axis, forward
        )
        high = lax.ppermute(lax.slice_in_dim(block, 0, width, axis=dim), axis, backward)
        block = jnp.concatenate([low, block, high], axis=dim)
    return block


def synth_table(length):
    inputs = jnp.arange(length + 8, dtype=jnp.int32)[:, None]
    outputs = jnp.arange(length, dtype=jnp.int32)[None, :]
    half = outputs // 2
    phase = outputs % 2
    table = jnp.zeros((length + 8, length), jnp.float32)
    for tap_num in range(3):
        low_coef = jnp.where(phase == 0, DAUB_LOW[2 * tap_num], DAUB_LOW[2 * tap_num + 1])
        high_coef = jnp.where(phase == 0, DAUB_HIGH[2 * tap_num], DAUB_HIGH[2 * tap_num + 1])
        table = table + jnp.where(inputs == 2 * (half - tap_num) + 4, low_coef, 0.0)
        table = table + jnp.where(inputs == 2 * (half - tap_num) + 5, high_coef, 0.0)
    return table


def analysis_table(length):
    inputs = jnp.arange(length + 8, dtype=jnp.int32)[:, None]
    outputs = jnp.arange(length, dtype=jnp.int32)[None, :]
    half = outputs // 2
    phase = outputs % 2
    table = jnp.zeros((length + 8, length), jnp.float32)
    for tap_num in range(3):
        for offset in (0, 1):
            coef = jnp.where(
                phase == 0, DAUB_LOW[2 * tap_num + offset], DAUB_HIGH[2 * tap_num + offset]
            )
            table = table + jnp.where(inputs == 2 * (half + tap_num) + offset + 4, coef, 0.0)
    return table


def butterfly_sum(value, axis):
    count = lax.axis_size(axis)
    if count & (count - 1):
        return lax.psum(value, axis)
    stride = 1
    while stride < count:
        value = value + lax.ppermute(value, axis, [(i, i ^ stride) for i in range(count)])
        stride *= 2
    return value


def sum_steps(axes):
    steps = []
    for axis in axes:
        count = lax.axis_size(axis)
        if count & (count - 1):
            steps.append(lambda value, axis=axis: lax.psum(value, axis))
            continue
        stride = 1
        while stride < count:
            pairs = [(i, i ^ stride) for i in range(count)]
            steps.append(lambda value, axis=axis, pairs=pairs: value + lax.ppermute(value, axis, pairs))
            stride *= 2
    return steps


def global_sum(local_value):
    for step in sum_steps(("gx", "gy")):
        local_value = step(local_value)
    return local_value


def advance(carry, value, step=True):
    total, steps = carry
    if step and steps:
        total = steps[0](total)
        steps = steps[1:]
    total, value = lax.optimization_barrier((total, value))
    return (total, steps), value


def finish(carry):
    total, steps = carry
    for step in steps:
        total = step(total)
    return total


def with_rim(field, width=4):
    return extended(field, (("gx", 1), ("gy", 2)), width)


def interior(field):
    return field[:, 4:-4, 4:-4]


def shards(right_side, prior_weight, jacobi_inverse, interaction, footprint):
    highest = lax.Precision.HIGHEST
    layers, tile_rows, tile_cols = right_side.shape
    sensors, rows_blocks, cols_blocks = (footprint.shape[0], footprint.shape[1], footprint.shape[2])
    block_rows = tile_rows // rows_blocks
    block_cols = tile_cols // cols_blocks
    owners = lax.axis_size("gy")
    layer_blocks_cols = cols_blocks * owners
    requests = sensors * rows_blocks * cols_blocks * layers
    capacity = requests // owners + 1
    own_blocks = layers * rows_blocks * cols_blocks
    synth_rows = synth_table(tile_rows)
    synth_cols = synth_table(tile_cols)
    analysis_rows = analysis_table(tile_rows + 8)
    analysis_cols = analysis_table(tile_cols + 8)
    flat_ids = footprint.reshape(requests)
    request_num = jnp.arange(requests, dtype=jnp.int32)
    layer_of = request_num % layers
    sensor_of = request_num // (requests // sensors)
    target = flat_ids % layer_blocks_cols // cols_blocks
    owned_index = (
        layer_of * (rows_blocks * cols_blocks)
        + flat_ids // layer_blocks_cols % rows_blocks * cols_blocks
        + flat_ids % layer_blocks_cols % cols_blocks
    )
    picks = (target[:, None] == jnp.arange(owners, dtype=jnp.int32)[None, :]).astype(jnp.int32)
    slot = jnp.sum(picks * (jnp.cumsum(picks, axis=0) - 1), axis=1)
    send_ids = jnp.full((owners, capacity), own_blocks, jnp.int32).at[target, slot].set(owned_index)
    send_pairs = (
        jnp.zeros((owners, capacity), jnp.int32).at[target, slot].set(sensor_of * layers + layer_of)
    )
    wanted_ids, wanted_pairs = (
        lax.all_to_all(send_ids, "gy", split_axis=0, concat_axis=0, tiled=True),
        lax.all_to_all(send_pairs, "gy", split_axis=0, concat_axis=0, tiled=True),
    )
    slot_source = (
        jnp.full((owners, capacity), requests, jnp.int32).at[target, slot].set(request_num)
    )
    landing = (
        wanted_ids.reshape(-1)[None, :] == jnp.arange(own_blocks, dtype=jnp.int32)[:, None]
    ).astype(jnp.float32)
    def apply_op(direction, partials):
        along_rows = jnp.einsum("lab,ac->lcb", direction, synth_rows, precision=highest)
        blocks = (
            jnp.einsum("lab,bc->lac", along_rows, synth_cols, precision=highest)
            .reshape(layers, rows_blocks, block_rows, cols_blocks, block_cols)
            .transpose(0, 1, 3, 2, 4)
            .reshape(own_blocks, block_rows, block_cols)
        )
        blocks = jnp.concatenate([blocks, jnp.zeros((1, block_rows, block_cols), blocks.dtype)])
        outgoing = jnp.take(blocks, wanted_ids, axis=0, mode="clip")
        arrived = lax.all_to_all(outgoing, "gy", split_axis=0, concat_axis=0, tiled=True)
        seen = arrived[target, slot].reshape(
            sensors, rows_blocks * cols_blocks, layers, block_rows, block_cols
        )
        slopes = jnp.einsum("sklxy,slyz->skxz", seen, interaction, precision=highest)
        carry = (partials(slopes), sum_steps(("gx", "gy")))
        back = jnp.einsum("skxz,slyz->sklxy", slopes, interaction, precision=highest).reshape(
            requests, block_rows, block_cols
        )
        back = jnp.concatenate([back, jnp.zeros((1, block_rows, block_cols), back.dtype)])
        returning = jnp.take(back, slot_source, axis=0, mode="clip")
        carry, returning = advance(carry, returning)
        landed = lax.all_to_all(returning, "gy", split_axis=0, concat_axis=0, tiled=True)
        carry, landed = advance(carry, landed, step=False)
        summed = jnp.dot(
            landing, landed.reshape(owners * capacity, block_rows * block_cols), precision=highest
        )
        carry, summed = advance(carry, summed)
        padded = with_rim(
            summed.reshape(layers, rows_blocks, cols_blocks, block_rows, block_cols)
            .transpose(0, 1, 3, 2, 4)
            .reshape(layers, tile_rows, tile_cols),
            8,
        )
        carry, padded = advance(carry, padded)
        along_cols = jnp.einsum("lab,bc->lac", padded, analysis_cols, precision=highest)
        carry, along_cols = advance(carry, along_cols)
        return (
            jnp.einsum("lab,ac->lcb", along_cols, analysis_rows, precision=highest)
            + prior_weight * direction
        ), slopes, finish(carry)

    rims = with_rim(jnp.concatenate([right_side, jacobi_inverse, prior_weight]))
    residual, jacobi_inverse, prior_weight = jnp.split(rims, 3)
    solution = jnp.zeros_like(right_side)
    prior_inner = interior(prior_weight)
    precond_res = jacobi_inverse * residual
    direction = interior(precond_res)
    image, direction_slopes, totals = apply_op(
        precond_res,
        lambda slopes: jnp.stack(
            [
                jnp.sum(interior(residual) * direction),
                jnp.sum(slopes * slopes),
                jnp.sum(prior_inner * direction * direction),
            ]
        ),
    )
    rho_now = totals[0]
    step_size = rho_now / (totals[1] + totals[2])
    for step in range(ITERS):
        solution = solution + step_size * direction
        residual = residual - step_size * image
        if step + 1 < ITERS:
            precond_res = jacobi_inverse * residual
            inner = interior(precond_res)
            applied, slopes_now, totals = apply_op(
                precond_res,
                lambda slopes: jnp.stack(
                    [
                        jnp.sum(interior(residual) * inner),
                        jnp.sum(slopes * slopes),
                        jnp.sum(slopes * direction_slopes),
                        jnp.sum(direction_slopes * direction_slopes),
                        jnp.sum(prior_inner * inner * inner),
                        jnp.sum(prior_inner * inner * direction),
                        jnp.sum(prior_inner * direction * direction),
                    ]
                ),
            )
            rho_next = totals[0]
            ratio = rho_next / rho_now
            curvature = (totals[1] + 2.0 * ratio * totals[2] + ratio * ratio * totals[3]) + (
                totals[4] + 2.0 * ratio * totals[5] + ratio * ratio * totals[6]
            )
            step_size = rho_next / curvature
            direction = inner + ratio * direction
            direction_slopes = slopes_now + ratio * direction_slopes
            image = applied + ratio * image
            rho_now = rho_next
    residual = interior(residual)
    return (solution, residual)


def solution(mesh):
    return jax.shard_map(
        shards,
        mesh=mesh,
        in_specs=(
            P(None, "gx", "gy"),
            P(None, "gx", "gy"),
            P(None, "gx", "gy"),
            P(),
            P(None, "gx", "gy", None),
        ),
        out_specs=(P(None, "gx", "gy"), P(None, "gx", "gy")),
        check_vma=False,
    )
```

```python
import jax
import jax.numpy as jnp
from jax import lax
from jax.sharding import PartitionSpec as P

ITERS = 4


DAUB_LOW = (
    0.3326705529509569,
    0.8068915093133388,
    0.4598775021193313,
    -0.13501102001039084,
    -0.08544127388224149,
    0.035226291882100656,
)
DAUB_HIGH = tuple(((-1.0) ** tap_index * DAUB_LOW[5 - tap_index] for tap_index in range(6)))


def extended(block, sides, width):
    for axis, dim in sides:
        count = lax.axis_size(axis)
        forward = [(i, i + 1) for i in range(count - 1)]
        backward = [(target, source) for source, target in forward]
        low = lax.ppermute(
            lax.slice_in_dim(block, block.shape[dim] - width, None, axis=dim), axis, forward
        )
        high = lax.ppermute(lax.slice_in_dim(block, 0, width, axis=dim), axis, backward)
        block = jnp.concatenate([low, block, high], axis=dim)
    return block


def synth_table(length):
    inputs = jnp.arange(length + 8, dtype=jnp.int32)[:, None]
    outputs = jnp.arange(length, dtype=jnp.int32)[None, :]
    half = outputs // 2
    phase = outputs % 2
    table = jnp.zeros((length + 8, length), jnp.float32)
    for tap_num in range(3):
        low_coef = jnp.where(phase == 0, DAUB_LOW[2 * tap_num], DAUB_LOW[2 * tap_num + 1])
        high_coef = jnp.where(phase == 0, DAUB_HIGH[2 * tap_num], DAUB_HIGH[2 * tap_num + 1])
        table = table + jnp.where(inputs == 2 * (half - tap_num) + 4, low_coef, 0.0)
        table = table + jnp.where(inputs == 2 * (half - tap_num) + 5, high_coef, 0.0)
    return table


def analysis_table(length):
    inputs = jnp.arange(length + 8, dtype=jnp.int32)[:, None]
    outputs = jnp.arange(length, dtype=jnp.int32)[None, :]
    half = outputs // 2
    phase = outputs % 2
    table = jnp.zeros((length + 8, length), jnp.float32)
    for tap_num in range(3):
        for offset in (0, 1):
            coef = jnp.where(
                phase == 0, DAUB_LOW[2 * tap_num + offset], DAUB_HIGH[2 * tap_num + offset]
            )
            table = table + jnp.where(inputs == 2 * (half + tap_num) + offset + 4, coef, 0.0)
    return table


def butterfly_sum(value, axis):
    count = lax.axis_size(axis)
    if count & (count - 1):
        return lax.psum(value, axis)
    stride = 1
    while stride < count:
        value = value + lax.ppermute(value, axis, [(i, i ^ stride) for i in range(count)])
        stride *= 2
    return value


def sum_steps(axes):
    steps = []
    for axis in axes:
        count = lax.axis_size(axis)
        if count & (count - 1):
            steps.append(lambda value, axis=axis: lax.psum(value, axis))
            continue
        stride = 1
        while stride < count:
            pairs = [(i, i ^ stride) for i in range(count)]
            steps.append(lambda value, axis=axis, pairs=pairs: value + lax.ppermute(value, axis, pairs))
            stride *= 2
    return steps


def global_sum(local_value):
    for step in sum_steps(("gx", "gy")):
        local_value = step(local_value)
    return local_value


def advance(carry, value, step=True):
    total, steps = carry
    if step and steps:
        total = steps[0](total)
        steps = steps[1:]
    total, value = lax.optimization_barrier((total, value))
    return (total, steps), value


def finish(carry):
    total, steps = carry
    for step in steps:
        total = step(total)
    return total


def with_rim(field, width=4):
    return extended(field, (("gx", 1), ("gy", 2)), width)


def interior(field):
    return field[:, 4:-4, 4:-4]


def shards(right_side, prior_weight, jacobi_inverse, interaction, footprint):
    highest = lax.Precision.HIGH
    layers, tile_rows, tile_cols = right_side.shape
    sensors, rows_blocks, cols_blocks = (footprint.shape[0], footprint.shape[1], footprint.shape[2])
    block_rows = tile_rows // rows_blocks
    block_cols = tile_cols // cols_blocks
    owners = lax.axis_size("gy")
    layer_blocks_cols = cols_blocks * owners
    requests = sensors * rows_blocks * cols_blocks * layers
    capacity = requests // owners + 1
    own_blocks = layers * rows_blocks * cols_blocks
    synth_rows = synth_table(tile_rows)
    synth_cols = synth_table(tile_cols)
    analysis_rows = analysis_table(tile_rows + 8)
    analysis_cols = analysis_table(tile_cols + 8)
    flat_ids = footprint.reshape(requests)
    request_num = jnp.arange(requests, dtype=jnp.int32)
    layer_of = request_num % layers
    sensor_of = request_num // (requests // sensors)
    target = flat_ids % layer_blocks_cols // cols_blocks
    owned_index = (
        layer_of * (rows_blocks * cols_blocks)
        + flat_ids // layer_blocks_cols % rows_blocks * cols_blocks
        + flat_ids % layer_blocks_cols % cols_blocks
    )
    picks = (target[:, None] == jnp.arange(owners, dtype=jnp.int32)[None, :]).astype(jnp.int32)
    slot = jnp.sum(picks * (jnp.cumsum(picks, axis=0) - 1), axis=1)
    send_ids = jnp.full((owners, capacity), own_blocks, jnp.int32).at[target, slot].set(owned_index)
    send_pairs = (
        jnp.zeros((owners, capacity), jnp.int32).at[target, slot].set(sensor_of * layers + layer_of)
    )
    wanted_ids, wanted_pairs = (
        lax.all_to_all(send_ids, "gy", split_axis=0, concat_axis=0, tiled=True),
        lax.all_to_all(send_pairs, "gy", split_axis=0, concat_axis=0, tiled=True),
    )
    slot_source = (
        jnp.full((owners, capacity), requests, jnp.int32).at[target, slot].set(request_num)
    )
    landing = (
        wanted_ids.reshape(-1)[None, :] == jnp.arange(own_blocks, dtype=jnp.int32)[:, None]
    ).astype(jnp.float32)
    def apply_op(direction, partials):
        along_rows = jnp.einsum("lab,ac->lcb", direction, synth_rows, precision=highest)
        blocks = (
            jnp.einsum("lab,bc->lac", along_rows, synth_cols, precision=highest)
            .reshape(layers, rows_blocks, block_rows, cols_blocks, block_cols)
            .transpose(0, 1, 3, 2, 4)
            .reshape(own_blocks, block_rows, block_cols)
        )
        blocks = jnp.concatenate([blocks, jnp.zeros((1, block_rows, block_cols), blocks.dtype)])
        outgoing = jnp.take(blocks, wanted_ids, axis=0, mode="clip")
        arrived = lax.all_to_all(outgoing, "gy", split_axis=0, concat_axis=0, tiled=True)
        seen = arrived[target, slot].reshape(
            sensors, rows_blocks * cols_blocks, layers, block_rows, block_cols
        )
        slopes = jnp.einsum("sklxy,slyz->skxz", seen, interaction, precision=highest)
        carry = (partials(slopes), sum_steps(("gx", "gy")))
        back = jnp.einsum("skxz,slyz->sklxy", slopes, interaction, precision=highest).reshape(
            requests, block_rows, block_cols
        )
        back = jnp.concatenate([back, jnp.zeros((1, block_rows, block_cols), back.dtype)])
        returning = jnp.take(back, slot_source, axis=0, mode="clip")
        carry, returning = advance(carry, returning)
        landed = lax.all_to_all(returning, "gy", split_axis=0, concat_axis=0, tiled=True)
        carry, landed = advance(carry, landed, step=False)
        summed = jnp.dot(
            landing, landed.reshape(owners * capacity, block_rows * block_cols), precision=highest
        )
        carry, summed = advance(carry, summed)
        padded = with_rim(
            summed.reshape(layers, rows_blocks, cols_blocks, block_rows, block_cols)
            .transpose(0, 1, 3, 2, 4)
            .reshape(layers, tile_rows, tile_cols),
            8,
        )
        carry, padded = advance(carry, padded)
        along_cols = jnp.einsum("lab,bc->lac", padded, analysis_cols, precision=highest)
        carry, along_cols = advance(carry, along_cols)
        return (
            jnp.einsum("lab,ac->lcb", along_cols, analysis_rows, precision=highest)
            + prior_weight * direction
        ), slopes, finish(carry)

    rims = with_rim(jnp.concatenate([right_side, jacobi_inverse, prior_weight]))
    residual, jacobi_inverse, prior_weight = jnp.split(rims, 3)
    solution = jnp.zeros_like(right_side)
    prior_inner = interior(prior_weight)
    precond_res = jacobi_inverse * residual
    direction = interior(precond_res)
    image, direction_slopes, totals = apply_op(
        precond_res,
        lambda slopes: jnp.stack(
            [
                jnp.sum(interior(residual) * direction),
                jnp.sum(slopes * slopes),
                jnp.sum(prior_inner * direction * direction),
            ]
        ),
    )
    rho_now = totals[0]
    step_size = rho_now / (totals[1] + totals[2])
    for step in range(ITERS):
        solution = solution + step_size * direction
        residual = residual - step_size * image
        if step + 1 < ITERS:
            precond_res = jacobi_inverse * residual
            inner = interior(precond_res)
            applied, slopes_now, totals = apply_op(
                precond_res,
                lambda slopes: jnp.stack(
                    [
                        jnp.sum(interior(residual) * inner),
                        jnp.sum(slopes * slopes),
                        jnp.sum(slopes * direction_slopes),
                        jnp.sum(direction_slopes * direction_slopes),
                        jnp.sum(prior_inner * inner * inner),
                        jnp.sum(prior_inner * inner * direction),
                        jnp.sum(prior_inner * direction * direction),
                    ]
                ),
            )
            rho_next = totals[0]
            ratio = rho_next / rho_now
            curvature = (totals[1] + 2.0 * ratio * totals[2] + ratio * ratio * totals[3]) + (
                totals[4] + 2.0 * ratio * totals[5] + ratio * ratio * totals[6]
            )
            step_size = rho_next / curvature
            direction = inner + ratio * direction
            direction_slopes = slopes_now + ratio * direction_slopes
            image = applied + ratio * image
            rho_now = rho_next
    residual = interior(residual)
    return (solution, residual)


def solution(mesh):
    return jax.shard_map(
        shards,
        mesh=mesh,
        in_specs=(
            P(None, "gx", "gy"),
            P(None, "gx", "gy"),
            P(None, "gx", "gy"),
            P(),
            P(None, "gx", "gy", None),
        ),
        out_specs=(P(None, "gx", "gy"), P(None, "gx", "gy")),
        check_vma=False,
    )
```

```python
import jax
import jax.numpy as jnp
from jax import lax
from jax.sharding import PartitionSpec as P

ITERS = 4


DAUB_LOW = (
    0.3326705529509569,
    0.8068915093133388,
    0.4598775021193313,
    -0.13501102001039084,
    -0.08544127388224149,
    0.035226291882100656,
)
DAUB_HIGH = tuple(((-1.0) ** tap_index * DAUB_LOW[5 - tap_index] for tap_index in range(6)))


def extended(block, sides, width):
    for axis, dim in sides:
        count = lax.axis_size(axis)
        forward = [(i, i + 1) for i in range(count - 1)]
        backward = [(target, source) for source, target in forward]
        low = lax.ppermute(
            lax.slice_in_dim(block, block.shape[dim] - width, None, axis=dim), axis, forward
        )
        high = lax.ppermute(lax.slice_in_dim(block, 0, width, axis=dim), axis, backward)
        block = jnp.concatenate([low, block, high], axis=dim)
    return block


def synth_table(length):
    inputs = jnp.arange(length + 8, dtype=jnp.int32)[:, None]
    outputs = jnp.arange(length, dtype=jnp.int32)[None, :]
    half = outputs // 2
    phase = outputs % 2
    table = jnp.zeros((length + 8, length), jnp.float32)
    for tap_num in range(3):
        low_coef = jnp.where(phase == 0, DAUB_LOW[2 * tap_num], DAUB_LOW[2 * tap_num + 1])
        high_coef = jnp.where(phase == 0, DAUB_HIGH[2 * tap_num], DAUB_HIGH[2 * tap_num + 1])
        table = table + jnp.where(inputs == 2 * (half - tap_num) + 4, low_coef, 0.0)
        table = table + jnp.where(inputs == 2 * (half - tap_num) + 5, high_coef, 0.0)
    return table


def analysis_table(length):
    inputs = jnp.arange(length + 8, dtype=jnp.int32)[:, None]
    outputs = jnp.arange(length, dtype=jnp.int32)[None, :]
    half = outputs // 2
    phase = outputs % 2
    table = jnp.zeros((length + 8, length), jnp.float32)
    for tap_num in range(3):
        for offset in (0, 1):
            coef = jnp.where(
                phase == 0, DAUB_LOW[2 * tap_num + offset], DAUB_HIGH[2 * tap_num + offset]
            )
            table = table + jnp.where(inputs == 2 * (half + tap_num) + offset + 4, coef, 0.0)
    return table


def butterfly_sum(value, axis):
    count = lax.axis_size(axis)
    if count & (count - 1):
        return lax.psum(value, axis)
    stride = 1
    while stride < count:
        value = value + lax.ppermute(value, axis, [(i, i ^ stride) for i in range(count)])
        stride *= 2
    return value


def sum_steps(axes):
    steps = []
    for axis in axes:
        count = lax.axis_size(axis)
        if count & (count - 1):
            steps.append(lambda value, axis=axis: lax.psum(value, axis))
            continue
        stride = 1
        while stride < count:
            pairs = [(i, i ^ stride) for i in range(count)]
            steps.append(lambda value, axis=axis, pairs=pairs: value + lax.ppermute(value, axis, pairs))
            stride *= 2
    return steps


def global_sum(local_value):
    for step in sum_steps(("gx", "gy")):
        local_value = step(local_value)
    return local_value


def advance(carry, value, step=True):
    total, steps = carry
    if step and steps:
        total = steps[0](total)
        steps = steps[1:]
    total, value = lax.optimization_barrier((total, value))
    return (total, steps), value


def finish(carry):
    total, steps = carry
    for step in steps:
        total = step(total)
    return total


def with_rim(field, width=4):
    return extended(field, (("gx", 1), ("gy", 2)), width)


def interior(field):
    return field[:, 4:-4, 4:-4]


def shards(right_side, prior_weight, jacobi_inverse, interaction, footprint):
    highest = lax.Precision.HIGH
    layers, tile_rows, tile_cols = right_side.shape
    sensors, rows_blocks, cols_blocks = (footprint.shape[0], footprint.shape[1], footprint.shape[2])
    block_rows = tile_rows // rows_blocks
    block_cols = tile_cols // cols_blocks
    owners = lax.axis_size("gy")
    layer_blocks_cols = cols_blocks * owners
    requests = sensors * rows_blocks * cols_blocks * layers
    capacity = requests // owners + 1
    own_blocks = layers * rows_blocks * cols_blocks
    synth_rows = synth_table(tile_rows)
    synth_cols = synth_table(tile_cols)
    analysis_rows = analysis_table(tile_rows + 8)
    analysis_cols = analysis_table(tile_cols + 8)
    flat_ids = footprint.reshape(requests)
    request_num = jnp.arange(requests, dtype=jnp.int32)
    layer_of = request_num % layers
    sensor_of = request_num // (requests // sensors)
    target = flat_ids % layer_blocks_cols // cols_blocks
    owned_index = (
        layer_of * (rows_blocks * cols_blocks)
        + flat_ids // layer_blocks_cols % rows_blocks * cols_blocks
        + flat_ids % layer_blocks_cols % cols_blocks
    )
    picks = (target[:, None] == jnp.arange(owners, dtype=jnp.int32)[None, :]).astype(jnp.int32)
    slot = jnp.sum(picks * (jnp.cumsum(picks, axis=0) - 1), axis=1)
    send_ids = jnp.full((owners, capacity), own_blocks, jnp.int32).at[target, slot].set(owned_index)
    send_pairs = (
        jnp.zeros((owners, capacity), jnp.int32).at[target, slot].set(sensor_of * layers + layer_of)
    )
    wanted_ids, wanted_pairs = (
        lax.all_to_all(send_ids, "gy", split_axis=0, concat_axis=0, tiled=True),
        lax.all_to_all(send_pairs, "gy", split_axis=0, concat_axis=0, tiled=True),
    )
    slot_source = (
        jnp.full((owners, capacity), requests, jnp.int32).at[target, slot].set(request_num)
    )
    landing = (
        wanted_ids.reshape(-1)[None, :] == jnp.arange(own_blocks, dtype=jnp.int32)[:, None]
    ).astype(jnp.float32)
    def apply_op(direction, partials):
        along_rows = jnp.einsum("lab,ac->lcb", direction, synth_rows, precision=highest)
        blocks = (
            jnp.einsum("lab,bc->lac", along_rows, synth_cols, precision=highest)
            .reshape(layers, rows_blocks, block_rows, cols_blocks, block_cols)
            .transpose(0, 1, 3, 2, 4)
            .reshape(own_blocks, block_rows, block_cols)
        )
        blocks = jnp.concatenate([blocks, jnp.zeros((1, block_rows, block_cols), blocks.dtype)])
        outgoing = jnp.take(blocks, wanted_ids, axis=0, mode="clip")
        arrived = lax.all_to_all(outgoing, "gy", split_axis=0, concat_axis=0, tiled=True)
        seen = arrived[target, slot].reshape(
            sensors, rows_blocks * cols_blocks, layers, block_rows, block_cols
        )
        slopes = jnp.einsum("sklxy,slyz->skxz", seen, interaction, precision=highest)
        carry = (partials(slopes), sum_steps(("gx", "gy")))
        back = jnp.einsum("skxz,slyz->sklxy", slopes, interaction, precision=highest).reshape(
            requests, block_rows, block_cols
        )
        back = jnp.concatenate([back, jnp.zeros((1, block_rows, block_cols), back.dtype)])
        returning = jnp.take(back, slot_source, axis=0, mode="clip")
        carry, returning = advance(carry, returning)
        landed = lax.all_to_all(returning, "gy", split_axis=0, concat_axis=0, tiled=True)
        carry, landed = advance(carry, landed, step=False)
        summed = jnp.dot(
            landing, landed.reshape(owners * capacity, block_rows * block_cols), precision=highest
        )
        carry, summed = advance(carry, summed)
        padded = with_rim(
            summed.reshape(layers, rows_blocks, cols_blocks, block_rows, block_cols)
            .transpose(0, 1, 3, 2, 4)
            .reshape(layers, tile_rows, tile_cols),
            8,
        )
        carry, padded = advance(carry, padded)
        along_cols = jnp.einsum("lab,bc->lac", padded, analysis_cols, precision=highest)
        carry, along_cols = advance(carry, along_cols)
        return (
            jnp.einsum("lab,ac->lcb", along_cols, analysis_rows, precision=highest)
            + prior_weight * direction
        ), slopes, finish(carry)

    rims = with_rim(jnp.concatenate([right_side, jacobi_inverse, prior_weight]))
    residual, jacobi_inverse, prior_weight = jnp.split(rims, 3)
    prior_inner = interior(prior_weight)

    def iteration(step, state):
        solution, residual, direction, direction_slopes, image, rho_now = state
        precond_res = jacobi_inverse * residual
        inner = interior(precond_res)
        field_sums = jnp.stack(
            [
                jnp.sum(interior(residual) * inner),
                jnp.sum(prior_inner * inner * inner),
                jnp.sum(prior_inner * inner * direction),
                jnp.sum(prior_inner * direction * direction),
            ]
        )
        applied, slopes_now, totals = apply_op(
            precond_res,
            lambda slopes: jnp.concatenate(
                [
                    field_sums,
                    jnp.stack(
                        [
                            jnp.sum(slopes * slopes),
                            jnp.sum(slopes * direction_slopes),
                            jnp.sum(direction_slopes * direction_slopes),
                        ]
                    ),
                ]
            ),
        )
        rho_next = totals[0]
        ratio = jnp.where(step == 0, 0.0, rho_next / rho_now)
        curvature = (totals[4] + 2.0 * ratio * totals[5] + ratio * ratio * totals[6]) + (
            totals[1] + 2.0 * ratio * totals[2] + ratio * ratio * totals[3]
        )
        step_size = rho_next / curvature
        direction = inner + ratio * direction
        direction_slopes = slopes_now + ratio * direction_slopes
        image = applied + ratio * image
        solution = solution + step_size * direction
        residual = residual - step_size * image
        return solution, residual, direction, direction_slopes, image, rho_next

    zero_slopes = jnp.zeros((sensors, rows_blocks * cols_blocks, block_rows, block_cols), jnp.float32)
    state = (
        jnp.zeros_like(right_side),
        residual,
        jnp.zeros_like(right_side),
        zero_slopes,
        jnp.zeros_like(residual),
        jnp.ones((), jnp.float32),
    )
    solution, residual, _, _, _, _ = lax.fori_loop(0, ITERS, iteration, state)
    residual = interior(residual)
    return (solution, residual)


def solution(mesh):
    return jax.shard_map(
        shards,
        mesh=mesh,
        in_specs=(
            P(None, "gx", "gy"),
            P(None, "gx", "gy"),
            P(None, "gx", "gy"),
            P(),
            P(None, "gx", "gy", None),
        ),
        out_specs=(P(None, "gx", "gy"), P(None, "gx", "gy")),
        check_vma=False,
    )
```

```python
import jax
import jax.numpy as jnp
from jax import lax
from jax.sharding import PartitionSpec as P

ITERS = 4


DAUB_LOW = (
    0.3326705529509569,
    0.8068915093133388,
    0.4598775021193313,
    -0.13501102001039084,
    -0.08544127388224149,
    0.035226291882100656,
)
DAUB_HIGH = tuple(((-1.0) ** tap_index * DAUB_LOW[5 - tap_index] for tap_index in range(6)))


def extended(block, sides, width):
    for axis, dim in sides:
        count = lax.axis_size(axis)
        forward = [(i, i + 1) for i in range(count - 1)]
        backward = [(target, source) for source, target in forward]
        low = lax.ppermute(
            lax.slice_in_dim(block, block.shape[dim] - width, None, axis=dim), axis, forward
        )
        high = lax.ppermute(lax.slice_in_dim(block, 0, width, axis=dim), axis, backward)
        block = jnp.concatenate([low, block, high], axis=dim)
    return block


def synth_table(length):
    inputs = jnp.arange(length + 8, dtype=jnp.int32)[:, None]
    outputs = jnp.arange(length, dtype=jnp.int32)[None, :]
    half = outputs // 2
    phase = outputs % 2
    table = jnp.zeros((length + 8, length), jnp.float32)
    for tap_num in range(3):
        low_coef = jnp.where(phase == 0, DAUB_LOW[2 * tap_num], DAUB_LOW[2 * tap_num + 1])
        high_coef = jnp.where(phase == 0, DAUB_HIGH[2 * tap_num], DAUB_HIGH[2 * tap_num + 1])
        table = table + jnp.where(inputs == 2 * (half - tap_num) + 4, low_coef, 0.0)
        table = table + jnp.where(inputs == 2 * (half - tap_num) + 5, high_coef, 0.0)
    return table


def analysis_table(length):
    inputs = jnp.arange(length + 8, dtype=jnp.int32)[:, None]
    outputs = jnp.arange(length, dtype=jnp.int32)[None, :]
    half = outputs // 2
    phase = outputs % 2
    table = jnp.zeros((length + 8, length), jnp.float32)
    for tap_num in range(3):
        for offset in (0, 1):
            coef = jnp.where(
                phase == 0, DAUB_LOW[2 * tap_num + offset], DAUB_HIGH[2 * tap_num + offset]
            )
            table = table + jnp.where(inputs == 2 * (half + tap_num) + offset + 4, coef, 0.0)
    return table


def butterfly_sum(value, axis):
    count = lax.axis_size(axis)
    if count & (count - 1):
        return lax.psum(value, axis)
    stride = 1
    while stride < count:
        value = value + lax.ppermute(value, axis, [(i, i ^ stride) for i in range(count)])
        stride *= 2
    return value


def sum_steps(axes):
    steps = []
    for axis in axes:
        count = lax.axis_size(axis)
        if count & (count - 1):
            steps.append(lambda value, axis=axis: lax.psum(value, axis))
            continue
        stride = 1
        while stride < count:
            pairs = [(i, i ^ stride) for i in range(count)]
            steps.append(lambda value, axis=axis, pairs=pairs: value + lax.ppermute(value, axis, pairs))
            stride *= 2
    return steps


def global_sum(local_value):
    for step in sum_steps(("gx", "gy")):
        local_value = step(local_value)
    return local_value


def advance(carry, value, step=True):
    total, steps = carry
    if step and steps:
        total = steps[0](total)
        steps = steps[1:]
    total, value = lax.optimization_barrier((total, value))
    return (total, steps), value


def finish(carry):
    total, steps = carry
    for step in steps:
        total = step(total)
    return total


def with_rim(field, width=4):
    return extended(field, (("gx", 1), ("gy", 2)), width)


def interior(field):
    return field[:, 4:-4, 4:-4]


def shards(right_side, prior_weight, jacobi_inverse, interaction, footprint):
    highest = lax.Precision.HIGH
    layers, tile_rows, tile_cols = right_side.shape
    sensors, rows_blocks, cols_blocks = (footprint.shape[0], footprint.shape[1], footprint.shape[2])
    block_rows = tile_rows // rows_blocks
    block_cols = tile_cols // cols_blocks
    owners = lax.axis_size("gy")
    layer_blocks_cols = cols_blocks * owners
    requests = sensors * rows_blocks * cols_blocks * layers
    capacity = requests // owners + 1
    own_blocks = layers * rows_blocks * cols_blocks
    synth_rows = synth_table(tile_rows)
    synth_cols = synth_table(tile_cols)
    analysis_rows = analysis_table(tile_rows + 8)
    analysis_cols = analysis_table(tile_cols + 8)
    flat_ids = footprint.reshape(requests)
    request_num = jnp.arange(requests, dtype=jnp.int32)
    layer_of = request_num % layers
    sensor_of = request_num // (requests // sensors)
    target = flat_ids % layer_blocks_cols // cols_blocks
    owned_index = (
        layer_of * (rows_blocks * cols_blocks)
        + flat_ids // layer_blocks_cols % rows_blocks * cols_blocks
        + flat_ids % layer_blocks_cols % cols_blocks
    )
    picks = (target[:, None] == jnp.arange(owners, dtype=jnp.int32)[None, :]).astype(jnp.int32)
    slot = jnp.sum(picks * (jnp.cumsum(picks, axis=0) - 1), axis=1)
    hit = (target[:, None, None] == jnp.arange(owners, dtype=jnp.int32)[None, :, None]) & (
        slot[:, None, None] == jnp.arange(capacity, dtype=jnp.int32)[None, None, :]
    )
    used = jnp.any(hit, axis=0)
    send_ids = jnp.where(
        used, jnp.sum(jnp.where(hit, owned_index[:, None, None], 0), axis=0), own_blocks
    )
    wanted_ids = lax.all_to_all(send_ids, "gy", split_axis=0, concat_axis=0, tiled=True)
    slot_source = jnp.where(
        used, jnp.sum(jnp.where(hit, request_num[:, None, None], 0), axis=0), requests
    )
    landing = (
        wanted_ids.reshape(-1)[None, :] == jnp.arange(own_blocks, dtype=jnp.int32)[:, None]
    ).astype(jnp.float32)
    def apply_op(direction, partials):
        along_rows = jnp.einsum("lab,ac->lcb", direction, synth_rows, precision=highest)
        blocks = (
            jnp.einsum("lab,bc->lac", along_rows, synth_cols, precision=highest)
            .reshape(layers, rows_blocks, block_rows, cols_blocks, block_cols)
            .transpose(0, 1, 3, 2, 4)
            .reshape(own_blocks, block_rows, block_cols)
        )
        blocks = jnp.concatenate([blocks, jnp.zeros((1, block_rows, block_cols), blocks.dtype)])
        outgoing = jnp.take(blocks, wanted_ids, axis=0, mode="clip")
        arrived = lax.all_to_all(outgoing, "gy", split_axis=0, concat_axis=0, tiled=True)
        seen = arrived[target, slot].reshape(
            sensors, rows_blocks * cols_blocks, layers, block_rows, block_cols
        )
        slopes = jnp.einsum("sklxy,slyz->skxz", seen, interaction, precision=highest)
        carry = (partials(slopes), sum_steps(("gx", "gy")))
        back = jnp.einsum("skxz,slyz->sklxy", slopes, interaction, precision=highest).reshape(
            requests, block_rows, block_cols
        )
        back = jnp.concatenate([back, jnp.zeros((1, block_rows, block_cols), back.dtype)])
        returning = jnp.take(back, slot_source, axis=0, mode="clip")
        carry, returning = advance(carry, returning)
        landed = lax.all_to_all(returning, "gy", split_axis=0, concat_axis=0, tiled=True)
        carry, landed = advance(carry, landed, step=False)
        summed = jnp.dot(
            landing, landed.reshape(owners * capacity, block_rows * block_cols), precision=highest
        )
        carry, summed = advance(carry, summed)
        padded = with_rim(
            summed.reshape(layers, rows_blocks, cols_blocks, block_rows, block_cols)
            .transpose(0, 1, 3, 2, 4)
            .reshape(layers, tile_rows, tile_cols),
            8,
        )
        carry, padded = advance(carry, padded)
        along_cols = jnp.einsum("lab,bc->lac", padded, analysis_cols, precision=highest)
        carry, along_cols = advance(carry, along_cols)
        return (
            jnp.einsum("lab,ac->lcb", along_cols, analysis_rows, precision=highest)
            + prior_weight * direction
        ), slopes, finish(carry)

    rims = with_rim(jnp.concatenate([right_side, jacobi_inverse, prior_weight]))
    residual, jacobi_inverse, prior_weight = jnp.split(rims, 3)
    solution = jnp.zeros_like(right_side)
    prior_inner = interior(prior_weight)
    precond_res = jacobi_inverse * residual
    direction = interior(precond_res)
    image, direction_slopes, totals = apply_op(
        precond_res,
        lambda slopes: jnp.stack(
            [
                jnp.sum(interior(residual) * direction),
                jnp.sum(slopes * slopes),
                jnp.sum(prior_inner * direction * direction),
            ]
        ),
    )
    rho_now = totals[0]
    step_size = rho_now / (totals[1] + totals[2])
    for step in range(ITERS):
        solution = solution + step_size * direction
        residual = residual - step_size * image
        if step + 1 < ITERS:
            precond_res = jacobi_inverse * residual
            inner = interior(precond_res)
            applied, slopes_now, totals = apply_op(
                precond_res,
                lambda slopes: jnp.stack(
                    [
                        jnp.sum(interior(residual) * inner),
                        jnp.sum(slopes * slopes),
                        jnp.sum(slopes * direction_slopes),
                        jnp.sum(direction_slopes * direction_slopes),
                        jnp.sum(prior_inner * inner * inner),
                        jnp.sum(prior_inner * inner * direction),
                        jnp.sum(prior_inner * direction * direction),
                    ]
                ),
            )
            rho_next = totals[0]
            ratio = rho_next / rho_now
            curvature = (totals[1] + 2.0 * ratio * totals[2] + ratio * ratio * totals[3]) + (
                totals[4] + 2.0 * ratio * totals[5] + ratio * ratio * totals[6]
            )
            step_size = rho_next / curvature
            direction = inner + ratio * direction
            direction_slopes = slopes_now + ratio * direction_slopes
            image = applied + ratio * image
            rho_now = rho_next
    residual = interior(residual)
    return (solution, residual)


def solution(mesh):
    return jax.shard_map(
        shards,
        mesh=mesh,
        in_specs=(
            P(None, "gx", "gy"),
            P(None, "gx", "gy"),
            P(None, "gx", "gy"),
            P(),
            P(None, "gx", "gy", None),
        ),
        out_specs=(P(None, "gx", "gy"), P(None, "gx", "gy")),
        check_vma=False,
    )
```

```python
import jax
import jax.numpy as jnp
from jax import lax
from jax.sharding import PartitionSpec as P

ITERS = 4


DAUB_LOW = (
    0.3326705529509569,
    0.8068915093133388,
    0.4598775021193313,
    -0.13501102001039084,
    -0.08544127388224149,
    0.035226291882100656,
)
DAUB_HIGH = tuple(((-1.0) ** tap_index * DAUB_LOW[5 - tap_index] for tap_index in range(6)))


def extended(block, sides, width):
    for axis, dim in sides:
        count = lax.axis_size(axis)
        forward = [(i, i + 1) for i in range(count - 1)]
        backward = [(target, source) for source, target in forward]
        low = lax.ppermute(
            lax.slice_in_dim(block, block.shape[dim] - width, None, axis=dim), axis, forward
        )
        high = lax.ppermute(lax.slice_in_dim(block, 0, width, axis=dim), axis, backward)
        block = jnp.concatenate([low, block, high], axis=dim)
    return block


def synth_table(length):
    inputs = jnp.arange(length + 8, dtype=jnp.int32)[:, None]
    outputs = jnp.arange(length, dtype=jnp.int32)[None, :]
    half = outputs // 2
    phase = outputs % 2
    table = jnp.zeros((length + 8, length), jnp.float32)
    for tap_num in range(3):
        low_coef = jnp.where(phase == 0, DAUB_LOW[2 * tap_num], DAUB_LOW[2 * tap_num + 1])
        high_coef = jnp.where(phase == 0, DAUB_HIGH[2 * tap_num], DAUB_HIGH[2 * tap_num + 1])
        table = table + jnp.where(inputs == 2 * (half - tap_num) + 4, low_coef, 0.0)
        table = table + jnp.where(inputs == 2 * (half - tap_num) + 5, high_coef, 0.0)
    return table


def analysis_table(length):
    inputs = jnp.arange(length + 8, dtype=jnp.int32)[:, None]
    outputs = jnp.arange(length, dtype=jnp.int32)[None, :]
    half = outputs // 2
    phase = outputs % 2
    table = jnp.zeros((length + 8, length), jnp.float32)
    for tap_num in range(3):
        for offset in (0, 1):
            coef = jnp.where(
                phase == 0, DAUB_LOW[2 * tap_num + offset], DAUB_HIGH[2 * tap_num + offset]
            )
            table = table + jnp.where(inputs == 2 * (half + tap_num) + offset + 4, coef, 0.0)
    return table


def butterfly_sum(value, axis):
    count = lax.axis_size(axis)
    if count & (count - 1):
        return lax.psum(value, axis)
    stride = 1
    while stride < count:
        value = value + lax.ppermute(value, axis, [(i, i ^ stride) for i in range(count)])
        stride *= 2
    return value


def sum_steps(axes):
    steps = []
    for axis in axes:
        count = lax.axis_size(axis)
        if count & (count - 1):
            steps.append(lambda value, axis=axis: lax.psum(value, axis))
            continue
        stride = 1
        while stride < count:
            pairs = [(i, i ^ stride) for i in range(count)]
            steps.append(lambda value, axis=axis, pairs=pairs: value + lax.ppermute(value, axis, pairs))
            stride *= 2
    return steps


def global_sum(local_value):
    for step in sum_steps(("gx", "gy")):
        local_value = step(local_value)
    return local_value


def advance(carry, value, step=True):
    total, steps = carry
    if step and steps:
        total = steps[0](total)
        steps = steps[1:]
    total, value = lax.optimization_barrier((total, value))
    return (total, steps), value


def finish(carry):
    total, steps = carry
    for step in steps:
        total = step(total)
    return total


def with_rim(field, width=4):
    return extended(field, (("gx", 1), ("gy", 2)), width)


def lane_sum(values):
    return jnp.sum(values.reshape(-1, 128), axis=0)


def interior(field):
    return field[:, 4:-4, 4:-4]


def shards(right_side, prior_weight, jacobi_inverse, interaction, footprint):
    highest = lax.Precision.HIGH
    layers, tile_rows, tile_cols = right_side.shape
    sensors, rows_blocks, cols_blocks = (footprint.shape[0], footprint.shape[1], footprint.shape[2])
    block_rows = tile_rows // rows_blocks
    block_cols = tile_cols // cols_blocks
    owners = lax.axis_size("gy")
    layer_blocks_cols = cols_blocks * owners
    requests = sensors * rows_blocks * cols_blocks * layers
    capacity = requests // owners + 1
    own_blocks = layers * rows_blocks * cols_blocks
    synth_rows = synth_table(tile_rows)
    synth_cols = synth_table(tile_cols)
    analysis_rows = analysis_table(tile_rows + 8)
    analysis_cols = analysis_table(tile_cols + 8)
    flat_ids = footprint.reshape(requests)
    request_num = jnp.arange(requests, dtype=jnp.int32)
    layer_of = request_num % layers
    sensor_of = request_num // (requests // sensors)
    target = flat_ids % layer_blocks_cols // cols_blocks
    owned_index = (
        layer_of * (rows_blocks * cols_blocks)
        + flat_ids // layer_blocks_cols % rows_blocks * cols_blocks
        + flat_ids % layer_blocks_cols % cols_blocks
    )
    picks = (target[:, None] == jnp.arange(owners, dtype=jnp.int32)[None, :]).astype(jnp.int32)
    slot = jnp.sum(picks * (jnp.cumsum(picks, axis=0) - 1), axis=1)
    hit = (target[:, None, None] == jnp.arange(owners, dtype=jnp.int32)[None, :, None]) & (
        slot[:, None, None] == jnp.arange(capacity, dtype=jnp.int32)[None, None, :]
    )
    used = jnp.any(hit, axis=0)
    send_ids = jnp.where(
        used, jnp.sum(jnp.where(hit, owned_index[:, None, None], 0), axis=0), own_blocks
    )
    wanted_ids = lax.all_to_all(send_ids, "gy", split_axis=0, concat_axis=0, tiled=True)
    slot_source = jnp.where(
        used, jnp.sum(jnp.where(hit, request_num[:, None, None], 0), axis=0), requests
    )
    landing = (
        wanted_ids.reshape(-1)[None, :] == jnp.arange(own_blocks, dtype=jnp.int32)[:, None]
    ).astype(jnp.float32)
    def apply_op(direction, partials):
        along_rows = jnp.einsum("lab,ac->lcb", direction, synth_rows, precision=highest)
        blocks = (
            jnp.einsum("lab,bc->lac", along_rows, synth_cols, precision=highest)
            .reshape(layers, rows_blocks, block_rows, cols_blocks, block_cols)
            .transpose(0, 1, 3, 2, 4)
            .reshape(own_blocks, block_rows, block_cols)
        )
        blocks = jnp.concatenate([blocks, jnp.zeros((1, block_rows, block_cols), blocks.dtype)])
        outgoing = jnp.take(blocks, wanted_ids, axis=0, mode="clip")
        arrived = lax.all_to_all(outgoing, "gy", split_axis=0, concat_axis=0, tiled=True)
        seen = arrived[target, slot].reshape(
            sensors, rows_blocks * cols_blocks, layers, block_rows, block_cols
        )
        slopes = jnp.einsum("sklxy,slyz->skxz", seen, interaction, precision=highest)
        carry = (partials(slopes), sum_steps(("gx", "gy")))
        back = jnp.einsum("skxz,slyz->sklxy", slopes, interaction, precision=highest).reshape(
            requests, block_rows, block_cols
        )
        back = jnp.concatenate([back, jnp.zeros((1, block_rows, block_cols), back.dtype)])
        returning = jnp.take(back, slot_source, axis=0, mode="clip")
        carry, returning = advance(carry, returning)
        landed = lax.all_to_all(returning, "gy", split_axis=0, concat_axis=0, tiled=True)
        carry, landed = advance(carry, landed, step=False)
        summed = jnp.dot(
            landing, landed.reshape(owners * capacity, block_rows * block_cols), precision=highest
        )
        carry, summed = advance(carry, summed)
        padded = with_rim(
            summed.reshape(layers, rows_blocks, cols_blocks, block_rows, block_cols)
            .transpose(0, 1, 3, 2, 4)
            .reshape(layers, tile_rows, tile_cols),
            8,
        )
        carry, padded = advance(carry, padded)
        along_cols = jnp.einsum("lab,bc->lac", padded, analysis_cols, precision=highest)
        carry, along_cols = advance(carry, along_cols)
        return (
            jnp.einsum("lab,ac->lcb", along_cols, analysis_rows, precision=highest)
            + prior_weight * direction
        ), slopes, jnp.sum(finish(carry), axis=1)

    rims = with_rim(jnp.concatenate([right_side, jacobi_inverse, prior_weight]))
    residual, jacobi_inverse, prior_weight = jnp.split(rims, 3)
    solution = jnp.zeros_like(right_side)
    prior_inner = interior(prior_weight)
    precond_res = jacobi_inverse * residual
    direction = interior(precond_res)
    image, direction_slopes, totals = apply_op(
        precond_res,
        lambda slopes: jnp.stack(
            [
                lane_sum(interior(residual) * direction),
                lane_sum(slopes * slopes),
                lane_sum(prior_inner * direction * direction),
            ]
        ),
    )
    rho_now = totals[0]
    step_size = rho_now / (totals[1] + totals[2])
    for step in range(ITERS):
        solution = solution + step_size * direction
        residual = residual - step_size * image
        if step + 1 < ITERS:
            precond_res = jacobi_inverse * residual
            inner = interior(precond_res)
            applied, slopes_now, totals = apply_op(
                precond_res,
                lambda slopes: jnp.stack(
                    [
                        lane_sum(interior(residual) * inner),
                        lane_sum(slopes * slopes),
                        lane_sum(slopes * direction_slopes),
                        lane_sum(direction_slopes * direction_slopes),
                        lane_sum(prior_inner * inner * inner),
                        lane_sum(prior_inner * inner * direction),
                        lane_sum(prior_inner * direction * direction),
                    ]
                ),
            )
            rho_next = totals[0]
            ratio = rho_next / rho_now
            curvature = (totals[1] + 2.0 * ratio * totals[2] + ratio * ratio * totals[3]) + (
                totals[4] + 2.0 * ratio * totals[5] + ratio * ratio * totals[6]
            )
            step_size = rho_next / curvature
            direction = inner + ratio * direction
            direction_slopes = slopes_now + ratio * direction_slopes
            image = applied + ratio * image
            rho_now = rho_next
    residual = interior(residual)
    return (solution, residual)


def solution(mesh):
    return jax.shard_map(
        shards,
        mesh=mesh,
        in_specs=(
            P(None, "gx", "gy"),
            P(None, "gx", "gy"),
            P(None, "gx", "gy"),
            P(),
            P(None, "gx", "gy", None),
        ),
        out_specs=(P(None, "gx", "gy"), P(None, "gx", "gy")),
        check_vma=False,
    )
```

```python
import jax
import jax.numpy as jnp
from jax import lax
from jax.sharding import PartitionSpec as P

ITERS = 4


DAUB_LOW = (
    0.3326705529509569,
    0.8068915093133388,
    0.4598775021193313,
    -0.13501102001039084,
    -0.08544127388224149,
    0.035226291882100656,
)
DAUB_HIGH = tuple(((-1.0) ** tap_index * DAUB_LOW[5 - tap_index] for tap_index in range(6)))


def extended(block, sides, width):
    for axis, dim in sides:
        count = lax.axis_size(axis)
        forward = [(i, i + 1) for i in range(count - 1)]
        backward = [(target, source) for source, target in forward]
        low = lax.ppermute(
            lax.slice_in_dim(block, block.shape[dim] - width, None, axis=dim), axis, forward
        )
        high = lax.ppermute(lax.slice_in_dim(block, 0, width, axis=dim), axis, backward)
        block = jnp.concatenate([low, block, high], axis=dim)
    return block


def synth_table(length):
    inputs = jnp.arange(length + 8, dtype=jnp.int32)[:, None]
    outputs = jnp.arange(length, dtype=jnp.int32)[None, :]
    half = outputs // 2
    phase = outputs % 2
    table = jnp.zeros((length + 8, length), jnp.float32)
    for tap_num in range(3):
        low_coef = jnp.where(phase == 0, DAUB_LOW[2 * tap_num], DAUB_LOW[2 * tap_num + 1])
        high_coef = jnp.where(phase == 0, DAUB_HIGH[2 * tap_num], DAUB_HIGH[2 * tap_num + 1])
        table = table + jnp.where(inputs == 2 * (half - tap_num) + 4, low_coef, 0.0)
        table = table + jnp.where(inputs == 2 * (half - tap_num) + 5, high_coef, 0.0)
    return table


def analysis_table(length):
    inputs = jnp.arange(length + 8, dtype=jnp.int32)[:, None]
    outputs = jnp.arange(length, dtype=jnp.int32)[None, :]
    half = outputs // 2
    phase = outputs % 2
    table = jnp.zeros((length + 8, length), jnp.float32)
    for tap_num in range(3):
        for offset in (0, 1):
            coef = jnp.where(
                phase == 0, DAUB_LOW[2 * tap_num + offset], DAUB_HIGH[2 * tap_num + offset]
            )
            table = table + jnp.where(inputs == 2 * (half + tap_num) + offset + 4, coef, 0.0)
    return table


def butterfly_sum(value, axis):
    count = lax.axis_size(axis)
    if count & (count - 1):
        return lax.psum(value, axis)
    stride = 1
    while stride < count:
        value = value + lax.ppermute(value, axis, [(i, i ^ stride) for i in range(count)])
        stride *= 2
    return value


def sum_steps(axes):
    steps = []
    for axis in axes:
        count = lax.axis_size(axis)
        if count & (count - 1):
            steps.append(lambda value, axis=axis: lax.psum(value, axis))
            continue
        stride = 1
        while stride < count:
            pairs = [(i, i ^ stride) for i in range(count)]
            steps.append(lambda value, axis=axis, pairs=pairs: value + lax.ppermute(value, axis, pairs))
            stride *= 2
    return steps


def global_sum(local_value):
    for step in sum_steps(("gx", "gy")):
        local_value = step(local_value)
    return local_value


def advance(carry, value, step=True):
    total, steps = carry
    if step and steps:
        total = steps[0](total)
        steps = steps[1:]
    total, value = lax.optimization_barrier((total, value))
    return (total, steps), value


def finish(carry):
    total, steps = carry
    for step in steps:
        total = step(total)
    return total


def with_rim(field, width=4):
    return extended(field, (("gx", 1), ("gy", 2)), width)


def lane_sum(values):
    return jnp.sum(values.reshape(-1, 128), axis=0)


def interior(field):
    return field[:, 4:-4, 4:-4]


def shards(right_side, prior_weight, jacobi_inverse, interaction, footprint):
    highest = lax.Precision.HIGH
    layers, tile_rows, tile_cols = right_side.shape
    sensors, rows_blocks, cols_blocks = (footprint.shape[0], footprint.shape[1], footprint.shape[2])
    block_rows = tile_rows // rows_blocks
    block_cols = tile_cols // cols_blocks
    owners = lax.axis_size("gy")
    layer_blocks_cols = cols_blocks * owners
    requests = sensors * rows_blocks * cols_blocks * layers
    capacity = requests // owners + 1
    own_blocks = layers * rows_blocks * cols_blocks
    synth_rows = synth_table(tile_rows)
    synth_cols = synth_table(tile_cols)
    analysis_rows = analysis_table(tile_rows + 8)
    analysis_cols = analysis_table(tile_cols + 8)
    flat_ids = footprint.reshape(requests)
    request_num = jnp.arange(requests, dtype=jnp.int32)
    layer_of = request_num % layers
    sensor_of = request_num // (requests // sensors)
    target = flat_ids % layer_blocks_cols // cols_blocks
    owned_index = (
        layer_of * (rows_blocks * cols_blocks)
        + flat_ids // layer_blocks_cols % rows_blocks * cols_blocks
        + flat_ids % layer_blocks_cols % cols_blocks
    )
    picks = (target[:, None] == jnp.arange(owners, dtype=jnp.int32)[None, :]).astype(jnp.int32)
    slot = jnp.sum(picks * (jnp.cumsum(picks, axis=0) - 1), axis=1)
    hit = (target[:, None, None] == jnp.arange(owners, dtype=jnp.int32)[None, :, None]) & (
        slot[:, None, None] == jnp.arange(capacity, dtype=jnp.int32)[None, None, :]
    )
    used = jnp.any(hit, axis=0)
    send_ids = jnp.where(
        used, jnp.sum(jnp.where(hit, owned_index[:, None, None], 0), axis=0), own_blocks
    )
    wanted_ids = lax.all_to_all(send_ids, "gy", split_axis=0, concat_axis=0, tiled=True)
    slot_source = jnp.where(
        used, jnp.sum(jnp.where(hit, request_num[:, None, None], 0), axis=0), requests
    )
    exact = lax.Precision.HIGHEST
    landing = (
        wanted_ids.reshape(-1)[None, :] == jnp.arange(own_blocks, dtype=jnp.int32)[:, None]
    ).astype(jnp.float32)
    picking = (
        (target * capacity + slot)[:, None]
        == jnp.arange(owners * capacity, dtype=jnp.int32)[None, :]
    ).astype(jnp.float32)
    block_size = block_rows * block_cols
    def apply_op(direction, partials):
        along_rows = jnp.einsum("lab,ac->lcb", direction, synth_rows, precision=highest)
        blocks = (
            jnp.einsum("lab,bc->lac", along_rows, synth_cols, precision=highest)
            .reshape(layers, rows_blocks, block_rows, cols_blocks, block_cols)
            .transpose(0, 1, 3, 2, 4)
            .reshape(own_blocks, block_rows, block_cols)
        )
        outgoing = jnp.dot(landing.T, blocks.reshape(own_blocks, block_size), precision=exact)
        arrived = lax.all_to_all(
            outgoing.reshape(owners, capacity, block_rows, block_cols),
            "gy",
            split_axis=0,
            concat_axis=0,
            tiled=True,
        )
        seen = jnp.dot(
            picking, arrived.reshape(owners * capacity, block_size), precision=exact
        ).reshape(sensors, rows_blocks * cols_blocks, layers, block_rows, block_cols)
        slopes = jnp.einsum("sklxy,slyz->skxz", seen, interaction, precision=highest)
        carry = (partials(slopes), sum_steps(("gx", "gy")))
        back = jnp.einsum("skxz,slyz->sklxy", slopes, interaction, precision=highest).reshape(
            requests, block_rows, block_cols
        )
        returning = jnp.dot(
            picking.T, back.reshape(requests, block_size), precision=exact
        ).reshape(owners, capacity, block_rows, block_cols)
        carry, returning = advance(carry, returning)
        landed = lax.all_to_all(returning, "gy", split_axis=0, concat_axis=0, tiled=True)
        carry, landed = advance(carry, landed, step=False)
        summed = jnp.dot(
            landing, landed.reshape(owners * capacity, block_size), precision=exact
        )
        carry, summed = advance(carry, summed)
        padded = with_rim(
            summed.reshape(layers, rows_blocks, cols_blocks, block_rows, block_cols)
            .transpose(0, 1, 3, 2, 4)
            .reshape(layers, tile_rows, tile_cols),
            8,
        )
        carry, padded = advance(carry, padded)
        along_cols = jnp.einsum("lab,bc->lac", padded, analysis_cols, precision=highest)
        carry, along_cols = advance(carry, along_cols)
        return (
            jnp.einsum("lab,ac->lcb", along_cols, analysis_rows, precision=highest)
            + prior_weight * direction
        ), slopes, jnp.sum(finish(carry), axis=1)

    rims = with_rim(jnp.concatenate([right_side, jacobi_inverse, prior_weight]))
    residual, jacobi_inverse, prior_weight = jnp.split(rims, 3)
    solution = jnp.zeros_like(right_side)
    prior_inner = interior(prior_weight)
    precond_res = jacobi_inverse * residual
    direction = interior(precond_res)
    image, direction_slopes, totals = apply_op(
        precond_res,
        lambda slopes: jnp.stack(
            [
                lane_sum(interior(residual) * direction),
                lane_sum(slopes * slopes),
                lane_sum(prior_inner * direction * direction),
            ]
        ),
    )
    rho_now = totals[0]
    step_size = rho_now / (totals[1] + totals[2])
    for step in range(ITERS):
        solution = solution + step_size * direction
        residual = residual - step_size * image
        if step + 1 < ITERS:
            precond_res = jacobi_inverse * residual
            inner = interior(precond_res)
            applied, slopes_now, totals = apply_op(
                precond_res,
                lambda slopes: jnp.stack(
                    [
                        lane_sum(interior(residual) * inner),
                        lane_sum(slopes * slopes),
                        lane_sum(slopes * direction_slopes),
                        lane_sum(direction_slopes * direction_slopes),
                        lane_sum(prior_inner * inner * inner),
                        lane_sum(prior_inner * inner * direction),
                        lane_sum(prior_inner * direction * direction),
                    ]
                ),
            )
            rho_next = totals[0]
            ratio = rho_next / rho_now
            curvature = (totals[1] + 2.0 * ratio * totals[2] + ratio * ratio * totals[3]) + (
                totals[4] + 2.0 * ratio * totals[5] + ratio * ratio * totals[6]
            )
            step_size = rho_next / curvature
            direction = inner + ratio * direction
            direction_slopes = slopes_now + ratio * direction_slopes
            image = applied + ratio * image
            rho_now = rho_next
    residual = interior(residual)
    return (solution, residual)


def solution(mesh):
    return jax.shard_map(
        shards,
        mesh=mesh,
        in_specs=(
            P(None, "gx", "gy"),
            P(None, "gx", "gy"),
            P(None, "gx", "gy"),
            P(),
            P(None, "gx", "gy", None),
        ),
        out_specs=(P(None, "gx", "gy"), P(None, "gx", "gy")),
        check_vma=False,
    )
```

```python
import jax
import jax.numpy as jnp
from jax import lax
from jax.sharding import PartitionSpec as P

ITERS = 4


DAUB_LOW = (
    0.3326705529509569,
    0.8068915093133388,
    0.4598775021193313,
    -0.13501102001039084,
    -0.08544127388224149,
    0.035226291882100656,
)
DAUB_HIGH = tuple(((-1.0) ** tap_index * DAUB_LOW[5 - tap_index] for tap_index in range(6)))


def extended(block, sides, width):
    for axis, dim in sides:
        count = lax.axis_size(axis)
        forward = [(i, i + 1) for i in range(count - 1)]
        backward = [(target, source) for source, target in forward]
        low = lax.ppermute(
            lax.slice_in_dim(block, block.shape[dim] - width, None, axis=dim), axis, forward
        )
        high = lax.ppermute(lax.slice_in_dim(block, 0, width, axis=dim), axis, backward)
        block = jnp.concatenate([low, block, high], axis=dim)
    return block


def synth_table(length):
    inputs = jnp.arange(length + 8, dtype=jnp.int32)[:, None]
    outputs = jnp.arange(length, dtype=jnp.int32)[None, :]
    half = outputs // 2
    phase = outputs % 2
    table = jnp.zeros((length + 8, length), jnp.float32)
    for tap_num in range(3):
        low_coef = jnp.where(phase == 0, DAUB_LOW[2 * tap_num], DAUB_LOW[2 * tap_num + 1])
        high_coef = jnp.where(phase == 0, DAUB_HIGH[2 * tap_num], DAUB_HIGH[2 * tap_num + 1])
        table = table + jnp.where(inputs == 2 * (half - tap_num) + 4, low_coef, 0.0)
        table = table + jnp.where(inputs == 2 * (half - tap_num) + 5, high_coef, 0.0)
    return table


def analysis_table(length):
    inputs = jnp.arange(length + 8, dtype=jnp.int32)[:, None]
    outputs = jnp.arange(length, dtype=jnp.int32)[None, :]
    half = outputs // 2
    phase = outputs % 2
    table = jnp.zeros((length + 8, length), jnp.float32)
    for tap_num in range(3):
        for offset in (0, 1):
            coef = jnp.where(
                phase == 0, DAUB_LOW[2 * tap_num + offset], DAUB_HIGH[2 * tap_num + offset]
            )
            table = table + jnp.where(inputs == 2 * (half + tap_num) + offset + 4, coef, 0.0)
    return table


def butterfly_sum(value, axis):
    count = lax.axis_size(axis)
    if count & (count - 1):
        return lax.psum(value, axis)
    stride = 1
    while stride < count:
        value = value + lax.ppermute(value, axis, [(i, i ^ stride) for i in range(count)])
        stride *= 2
    return value


def sum_steps(axes):
    steps = []
    for axis in axes:
        count = lax.axis_size(axis)
        if count & (count - 1):
            steps.append(lambda value, axis=axis: lax.psum(value, axis))
            continue
        stride = 1
        while stride < count:
            pairs = [(i, i ^ stride) for i in range(count)]
            steps.append(lambda value, axis=axis, pairs=pairs: value + lax.ppermute(value, axis, pairs))
            stride *= 2
    return steps


def global_sum(local_value):
    for step in sum_steps(("gx", "gy")):
        local_value = step(local_value)
    return local_value


def advance(carry, value, step=True):
    total, steps = carry
    if step and steps:
        total = steps[0](total)
        steps = steps[1:]
    total, value = lax.optimization_barrier((total, value))
    return (total, steps), value


def finish(carry):
    total, steps = carry
    for step in steps:
        total = step(total)
    return total


def with_rim(field, width=4):
    return extended(field, (("gx", 1), ("gy", 2)), width)


def lane_sum(values):
    return jnp.sum(values.reshape(-1, 128), axis=0)


def interior(field):
    return field[:, 4:-4, 4:-4]


def shards(right_side, prior_weight, jacobi_inverse, interaction, footprint):
    highest = lax.Precision.HIGH
    layers, tile_rows, tile_cols = right_side.shape
    sensors, rows_blocks, cols_blocks = (footprint.shape[0], footprint.shape[1], footprint.shape[2])
    block_rows = tile_rows // rows_blocks
    block_cols = tile_cols // cols_blocks
    owners = lax.axis_size("gy")
    layer_blocks_cols = cols_blocks * owners
    requests = sensors * rows_blocks * cols_blocks * layers
    capacity = requests // owners + 1
    own_blocks = layers * rows_blocks * cols_blocks
    synth_rows = synth_table(tile_rows)
    synth_cols = synth_table(tile_cols)
    analysis_rows = analysis_table(tile_rows + 8)
    analysis_cols = analysis_table(tile_cols + 8)
    flat_ids = footprint.reshape(requests)
    request_num = jnp.arange(requests, dtype=jnp.int32)
    layer_of = request_num % layers
    sensor_of = request_num // (requests // sensors)
    target = flat_ids % layer_blocks_cols // cols_blocks
    owned_index = (
        layer_of * (rows_blocks * cols_blocks)
        + flat_ids // layer_blocks_cols % rows_blocks * cols_blocks
        + flat_ids % layer_blocks_cols % cols_blocks
    )
    picks = (target[:, None] == jnp.arange(owners, dtype=jnp.int32)[None, :]).astype(jnp.int32)
    slot = jnp.sum(picks * (jnp.cumsum(picks, axis=0) - 1), axis=1)
    hit = (target[:, None, None] == jnp.arange(owners, dtype=jnp.int32)[None, :, None]) & (
        slot[:, None, None] == jnp.arange(capacity, dtype=jnp.int32)[None, None, :]
    )
    used = jnp.any(hit, axis=0)
    send_ids = jnp.where(
        used, jnp.sum(jnp.where(hit, owned_index[:, None, None], 0), axis=0), own_blocks
    )
    wanted_ids = lax.all_to_all(send_ids, "gy", split_axis=0, concat_axis=0, tiled=True)
    slot_source = jnp.where(
        used, jnp.sum(jnp.where(hit, request_num[:, None, None], 0), axis=0), requests
    )
    own_layer = wanted_ids // (rows_blocks * cols_blocks)
    own_row = wanted_ids % (rows_blocks * cols_blocks) // cols_blocks
    own_col = wanted_ids % cols_blocks
    gather_ids = jnp.where(
        wanted_ids < own_blocks,
        own_layer * (rows_blocks * cols_blocks) + own_col * rows_blocks + own_row,
        own_blocks,
    )
    landing = (
        wanted_ids.reshape(-1)[None, :] == jnp.arange(own_blocks, dtype=jnp.int32)[:, None]
    ).astype(jnp.float32)
    def apply_op(direction, partials):
        along_rows = jnp.einsum("lab,ac->lcb", direction, synth_rows, precision=highest)
        blocks = jnp.einsum(
            "lab,bjc->ljac",
            along_rows,
            synth_cols.reshape(-1, cols_blocks, block_cols),
            precision=highest,
        ).reshape(own_blocks, block_rows, block_cols)
        blocks = jnp.concatenate([blocks, jnp.zeros((1, block_rows, block_cols), blocks.dtype)])
        outgoing = jnp.take(blocks, gather_ids, axis=0, mode="clip")
        arrived = lax.all_to_all(outgoing, "gy", split_axis=0, concat_axis=0, tiled=True)
        seen = arrived[target, slot].reshape(
            sensors, rows_blocks * cols_blocks, layers, block_rows, block_cols
        )
        slopes = jnp.einsum("sklxy,slyz->skxz", seen, interaction, precision=highest)
        carry = (partials(slopes), sum_steps(("gx", "gy")))
        back = jnp.einsum("skxz,slyz->sklxy", slopes, interaction, precision=highest).reshape(
            requests, block_rows, block_cols
        )
        back = jnp.concatenate([back, jnp.zeros((1, block_rows, block_cols), back.dtype)])
        returning = jnp.take(back, slot_source, axis=0, mode="clip")
        carry, returning = advance(carry, returning)
        landed = lax.all_to_all(returning, "gy", split_axis=0, concat_axis=0, tiled=True)
        carry, landed = advance(carry, landed, step=False)
        summed = jnp.dot(
            landing, landed.reshape(owners * capacity, block_rows * block_cols), precision=highest
        )
        carry, summed = advance(carry, summed)
        padded = with_rim(
            summed.reshape(layers, rows_blocks, cols_blocks, block_rows, block_cols)
            .transpose(0, 1, 3, 2, 4)
            .reshape(layers, tile_rows, tile_cols),
            8,
        )
        carry, padded = advance(carry, padded)
        along_cols = jnp.einsum("lab,bc->lac", padded, analysis_cols, precision=highest)
        carry, along_cols = advance(carry, along_cols)
        return (
            jnp.einsum("lab,ac->lcb", along_cols, analysis_rows, precision=highest)
            + prior_weight * direction
        ), slopes, jnp.sum(finish(carry), axis=1)

    rims = with_rim(jnp.concatenate([right_side, jacobi_inverse, prior_weight]))
    residual, jacobi_inverse, prior_weight = jnp.split(rims, 3)
    solution = jnp.zeros_like(right_side)
    prior_inner = interior(prior_weight)
    precond_res = jacobi_inverse * residual
    direction = interior(precond_res)
    image, direction_slopes, totals = apply_op(
        precond_res,
        lambda slopes: jnp.stack(
            [
                lane_sum(interior(residual) * direction),
                lane_sum(slopes * slopes),
                lane_sum(prior_inner * direction * direction),
            ]
        ),
    )
    rho_now = totals[0]
    step_size = rho_now / (totals[1] + totals[2])
    for step in range(ITERS):
        solution = solution + step_size * direction
        residual = residual - step_size * image
        if step + 1 < ITERS:
            precond_res = jacobi_inverse * residual
            inner = interior(precond_res)
            applied, slopes_now, totals = apply_op(
                precond_res,
                lambda slopes: jnp.stack(
                    [
                        lane_sum(interior(residual) * inner),
                        lane_sum(slopes * slopes),
                        lane_sum(slopes * direction_slopes),
                        lane_sum(direction_slopes * direction_slopes),
                        lane_sum(prior_inner * inner * inner),
                        lane_sum(prior_inner * inner * direction),
                        lane_sum(prior_inner * direction * direction),
                    ]
                ),
            )
            rho_next = totals[0]
            ratio = rho_next / rho_now
            curvature = (totals[1] + 2.0 * ratio * totals[2] + ratio * ratio * totals[3]) + (
                totals[4] + 2.0 * ratio * totals[5] + ratio * ratio * totals[6]
            )
            step_size = rho_next / curvature
            direction = inner + ratio * direction
            direction_slopes = slopes_now + ratio * direction_slopes
            image = applied + ratio * image
            rho_now = rho_next
    residual = interior(residual)
    return (solution, residual)


def solution(mesh):
    return jax.shard_map(
        shards,
        mesh=mesh,
        in_specs=(
            P(None, "gx", "gy"),
            P(None, "gx", "gy"),
            P(None, "gx", "gy"),
            P(),
            P(None, "gx", "gy", None),
        ),
        out_specs=(P(None, "gx", "gy"), P(None, "gx", "gy")),
        check_vma=False,
    )
```

```python
import jax
import jax.numpy as jnp
from jax import lax
from jax.sharding import PartitionSpec as P

ITERS = 4


DAUB_LOW = (
    0.3326705529509569,
    0.8068915093133388,
    0.4598775021193313,
    -0.13501102001039084,
    -0.08544127388224149,
    0.035226291882100656,
)
DAUB_HIGH = tuple(((-1.0) ** tap_index * DAUB_LOW[5 - tap_index] for tap_index in range(6)))


def extended(block, sides, width):
    for axis, dim in sides:
        count = lax.axis_size(axis)
        forward = [(i, i + 1) for i in range(count - 1)]
        backward = [(target, source) for source, target in forward]
        low = lax.ppermute(
            lax.slice_in_dim(block, block.shape[dim] - width, None, axis=dim), axis, forward
        )
        high = lax.ppermute(lax.slice_in_dim(block, 0, width, axis=dim), axis, backward)
        block = jnp.concatenate([low, block, high], axis=dim)
    return block


def synth_table(length):
    inputs = jnp.arange(length + 8, dtype=jnp.int32)[:, None]
    outputs = jnp.arange(length, dtype=jnp.int32)[None, :]
    half = outputs // 2
    phase = outputs % 2
    table = jnp.zeros((length + 8, length), jnp.float32)
    for tap_num in range(3):
        low_coef = jnp.where(phase == 0, DAUB_LOW[2 * tap_num], DAUB_LOW[2 * tap_num + 1])
        high_coef = jnp.where(phase == 0, DAUB_HIGH[2 * tap_num], DAUB_HIGH[2 * tap_num + 1])
        table = table + jnp.where(inputs == 2 * (half - tap_num) + 4, low_coef, 0.0)
        table = table + jnp.where(inputs == 2 * (half - tap_num) + 5, high_coef, 0.0)
    return table


def analysis_table(length):
    inputs = jnp.arange(length + 8, dtype=jnp.int32)[:, None]
    outputs = jnp.arange(length, dtype=jnp.int32)[None, :]
    half = outputs // 2
    phase = outputs % 2
    table = jnp.zeros((length + 8, length), jnp.float32)
    for tap_num in range(3):
        for offset in (0, 1):
            coef = jnp.where(
                phase == 0, DAUB_LOW[2 * tap_num + offset], DAUB_HIGH[2 * tap_num + offset]
            )
            table = table + jnp.where(inputs == 2 * (half + tap_num) + offset + 4, coef, 0.0)
    return table


def butterfly_sum(value, axis):
    count = lax.axis_size(axis)
    if count & (count - 1):
        return lax.psum(value, axis)
    stride = 1
    while stride < count:
        value = value + lax.ppermute(value, axis, [(i, i ^ stride) for i in range(count)])
        stride *= 2
    return value


def sum_steps(axes):
    steps = []
    for axis in axes:
        count = lax.axis_size(axis)
        if count & (count - 1):
            steps.append(lambda value, axis=axis: lax.psum(value, axis))
            continue
        stride = 1
        while stride < count:
            pairs = [(i, i ^ stride) for i in range(count)]
            steps.append(lambda value, axis=axis, pairs=pairs: value + lax.ppermute(value, axis, pairs))
            stride *= 2
    return steps


def global_sum(local_value):
    for step in sum_steps(("gx", "gy")):
        local_value = step(local_value)
    return local_value


def advance(carry, value, step=True):
    total, steps = carry
    if step and steps:
        total = steps[0](total)
        steps = steps[1:]
    total, value = lax.optimization_barrier((total, value))
    return (total, steps), value


def finish(carry):
    total, steps = carry
    for step in steps:
        total = step(total)
    return total


def with_rim(field, width=4):
    return extended(field, (("gx", 1), ("gy", 2)), width)


def lane_sum(values):
    return jnp.sum(values.reshape(-1, 128), axis=0)


def interior(field):
    return field[:, 4:-4, 4:-4]


def shards(right_side, prior_weight, jacobi_inverse, interaction, footprint):
    highest = lax.Precision.HIGH
    layers, tile_rows, tile_cols = right_side.shape
    sensors, rows_blocks, cols_blocks = (footprint.shape[0], footprint.shape[1], footprint.shape[2])
    block_rows = tile_rows // rows_blocks
    block_cols = tile_cols // cols_blocks
    owners = lax.axis_size("gy")
    layer_blocks_cols = cols_blocks * owners
    requests = sensors * rows_blocks * cols_blocks * layers
    capacity = requests // owners + 1
    own_blocks = layers * rows_blocks * cols_blocks
    synth_rows = synth_table(tile_rows)
    synth_cols = synth_table(tile_cols)
    analysis_rows = analysis_table(tile_rows + 8)
    analysis_cols = analysis_table(tile_cols + 8)
    flat_ids = footprint.reshape(requests)
    request_num = jnp.arange(requests, dtype=jnp.int32)
    layer_of = request_num % layers
    sensor_of = request_num // (requests // sensors)
    target = flat_ids % layer_blocks_cols // cols_blocks
    owned_index = (
        layer_of * (rows_blocks * cols_blocks)
        + flat_ids // layer_blocks_cols % rows_blocks * cols_blocks
        + flat_ids % layer_blocks_cols % cols_blocks
    )
    picks = (target[:, None] == jnp.arange(owners, dtype=jnp.int32)[None, :]).astype(jnp.int32)
    slot = jnp.sum(picks * (jnp.cumsum(picks, axis=0) - 1), axis=1)
    hit = (target[:, None, None] == jnp.arange(owners, dtype=jnp.int32)[None, :, None]) & (
        slot[:, None, None] == jnp.arange(capacity, dtype=jnp.int32)[None, None, :]
    )
    used = jnp.any(hit, axis=0)
    send_ids = jnp.where(
        used, jnp.sum(jnp.where(hit, owned_index[:, None, None], 0), axis=0), own_blocks
    )
    wanted_ids = lax.all_to_all(send_ids, "gy", split_axis=0, concat_axis=0, tiled=True)
    slot_source = jnp.where(
        used, jnp.sum(jnp.where(hit, request_num[:, None, None], 0), axis=0), requests
    )
    own_layer = wanted_ids // (rows_blocks * cols_blocks)
    own_row = wanted_ids % (rows_blocks * cols_blocks) // cols_blocks
    own_col = wanted_ids % cols_blocks
    gather_ids = jnp.where(
        wanted_ids < own_blocks,
        own_layer * (rows_blocks * cols_blocks) + own_col * rows_blocks + own_row,
        own_blocks,
    )
    landing = (
        wanted_ids.reshape(-1)[None, :] == jnp.arange(own_blocks, dtype=jnp.int32)[:, None]
    ).astype(jnp.float32)
    def apply_op(direction, partials):
        along_rows = jnp.einsum("lab,ac->lcb", direction, synth_rows, precision=highest)
        blocks = jnp.einsum(
            "lab,bjc->ljac",
            along_rows,
            synth_cols.reshape(-1, cols_blocks, block_cols),
            precision=highest,
        ).reshape(own_blocks, block_rows, block_cols)
        blocks = jnp.concatenate([blocks, jnp.zeros((1, block_rows, block_cols), blocks.dtype)])
        outgoing = jnp.take(blocks, gather_ids, axis=0, mode="clip")
        arrived = lax.all_to_all(outgoing, "gy", split_axis=0, concat_axis=0, tiled=True)
        seen = arrived[target, slot].reshape(
            sensors, rows_blocks * cols_blocks, layers, block_rows, block_cols
        )
        slopes = jnp.einsum("sklxy,slyz->skxz", seen, interaction, precision=highest)
        carry = (partials(slopes), sum_steps(("gx", "gy")))
        back = jnp.einsum("skxz,slyz->sklxy", slopes, interaction, precision=highest).reshape(
            requests, block_rows, block_cols
        )
        back = jnp.concatenate([back, jnp.zeros((1, block_rows, block_cols), back.dtype)])
        returning = jnp.take(back, slot_source, axis=0, mode="clip")
        carry, returning = advance(carry, returning)
        landed = lax.all_to_all(returning, "gy", split_axis=0, concat_axis=0, tiled=True)
        carry, landed = advance(carry, landed, step=False)
        summed = jnp.dot(
            landing, landed.reshape(owners * capacity, block_rows * block_cols), precision=highest
        )
        carry, summed = advance(carry, summed)
        padded = extended(
            summed.reshape(layers, rows_blocks, cols_blocks, block_rows, block_cols)
            .transpose(0, 1, 3, 2, 4)
            .reshape(layers, tile_rows, tile_cols),
            (("gx", 1),),
            8,
        )
        carry, padded = advance(carry, padded)
        count = lax.axis_size("gy")
        forward = [(i, i + 1) for i in range(count - 1)]
        backward = [(target, source) for source, target in forward]
        left = lax.ppermute(padded[:, :, tile_cols - 8 :], "gy", forward)
        right = lax.ppermute(padded[:, :, :8], "gy", backward)
        along_cols = (
            jnp.einsum("lab,bc->lac", padded, analysis_cols[8 : 8 + tile_cols], precision=highest)
            + jnp.einsum("lab,bc->lac", left, analysis_cols[:8], precision=highest)
            + jnp.einsum("lab,bc->lac", right, analysis_cols[8 + tile_cols :], precision=highest)
        )
        carry, along_cols = advance(carry, along_cols)
        return (
            jnp.einsum("lab,ac->lcb", along_cols, analysis_rows, precision=highest)
            + prior_weight * direction
        ), slopes, jnp.sum(finish(carry), axis=1)

    rims = with_rim(jnp.concatenate([right_side, jacobi_inverse, prior_weight]))
    residual, jacobi_inverse, prior_weight = jnp.split(rims, 3)
    solution = jnp.zeros_like(right_side)
    prior_inner = interior(prior_weight)
    precond_res = jacobi_inverse * residual
    direction = interior(precond_res)
    image, direction_slopes, totals = apply_op(
        precond_res,
        lambda slopes: jnp.stack(
            [
                lane_sum(interior(residual) * direction),
                lane_sum(slopes * slopes),
                lane_sum(prior_inner * direction * direction),
            ]
        ),
    )
    rho_now = totals[0]
    step_size = rho_now / (totals[1] + totals[2])
    for step in range(ITERS):
        solution = solution + step_size * direction
        residual = residual - step_size * image
        if step + 1 < ITERS:
            precond_res = jacobi_inverse * residual
            inner = interior(precond_res)
            applied, slopes_now, totals = apply_op(
                precond_res,
                lambda slopes: jnp.stack(
                    [
                        lane_sum(interior(residual) * inner),
                        lane_sum(slopes * slopes),
                        lane_sum(slopes * direction_slopes),
                        lane_sum(direction_slopes * direction_slopes),
                        lane_sum(prior_inner * inner * inner),
                        lane_sum(prior_inner * inner * direction),
                        lane_sum(prior_inner * direction * direction),
                    ]
                ),
            )
            rho_next = totals[0]
            ratio = rho_next / rho_now
            curvature = (totals[1] + 2.0 * ratio * totals[2] + ratio * ratio * totals[3]) + (
                totals[4] + 2.0 * ratio * totals[5] + ratio * ratio * totals[6]
            )
            step_size = rho_next / curvature
            direction = inner + ratio * direction
            direction_slopes = slopes_now + ratio * direction_slopes
            image = applied + ratio * image
            rho_now = rho_next
    residual = interior(residual)
    return (solution, residual)


def solution(mesh):
    return jax.shard_map(
        shards,
        mesh=mesh,
        in_specs=(
            P(None, "gx", "gy"),
            P(None, "gx", "gy"),
            P(None, "gx", "gy"),
            P(),
            P(None, "gx", "gy", None),
        ),
        out_specs=(P(None, "gx", "gy"), P(None, "gx", "gy")),
        check_vma=False,
    )
```

```python
import jax
import jax.numpy as jnp
from jax import lax
from jax.sharding import PartitionSpec as P

ITERS = 4


DAUB_LOW = (
    0.3326705529509569,
    0.8068915093133388,
    0.4598775021193313,
    -0.13501102001039084,
    -0.08544127388224149,
    0.035226291882100656,
)
DAUB_HIGH = tuple(((-1.0) ** tap_index * DAUB_LOW[5 - tap_index] for tap_index in range(6)))


def extended(block, sides, width):
    for axis, dim in sides:
        count = lax.axis_size(axis)
        forward = [(i, i + 1) for i in range(count - 1)]
        backward = [(target, source) for source, target in forward]
        low = lax.ppermute(
            lax.slice_in_dim(block, block.shape[dim] - width, None, axis=dim), axis, forward
        )
        high = lax.ppermute(lax.slice_in_dim(block, 0, width, axis=dim), axis, backward)
        block = jnp.concatenate([low, block, high], axis=dim)
    return block


def synth_table(length):
    inputs = jnp.arange(length + 8, dtype=jnp.int32)[:, None]
    outputs = jnp.arange(length, dtype=jnp.int32)[None, :]
    half = outputs // 2
    phase = outputs % 2
    table = jnp.zeros((length + 8, length), jnp.float32)
    for tap_num in range(3):
        low_coef = jnp.where(phase == 0, DAUB_LOW[2 * tap_num], DAUB_LOW[2 * tap_num + 1])
        high_coef = jnp.where(phase == 0, DAUB_HIGH[2 * tap_num], DAUB_HIGH[2 * tap_num + 1])
        table = table + jnp.where(inputs == 2 * (half - tap_num) + 4, low_coef, 0.0)
        table = table + jnp.where(inputs == 2 * (half - tap_num) + 5, high_coef, 0.0)
    return table


def analysis_table(length):
    inputs = jnp.arange(length + 8, dtype=jnp.int32)[:, None]
    outputs = jnp.arange(length, dtype=jnp.int32)[None, :]
    half = outputs // 2
    phase = outputs % 2
    table = jnp.zeros((length + 8, length), jnp.float32)
    for tap_num in range(3):
        for offset in (0, 1):
            coef = jnp.where(
                phase == 0, DAUB_LOW[2 * tap_num + offset], DAUB_HIGH[2 * tap_num + offset]
            )
            table = table + jnp.where(inputs == 2 * (half + tap_num) + offset + 4, coef, 0.0)
    return table


def butterfly_sum(value, axis):
    count = lax.axis_size(axis)
    if count & (count - 1):
        return lax.psum(value, axis)
    stride = 1
    while stride < count:
        value = value + lax.ppermute(value, axis, [(i, i ^ stride) for i in range(count)])
        stride *= 2
    return value


def sum_steps(axes):
    steps = []
    for axis in axes:
        count = lax.axis_size(axis)
        if count & (count - 1):
            steps.append(lambda value, axis=axis: lax.psum(value, axis))
            continue
        stride = 1
        while stride < count:
            pairs = [(i, i ^ stride) for i in range(count)]
            steps.append(lambda value, axis=axis, pairs=pairs: value + lax.ppermute(value, axis, pairs))
            stride *= 2
    return steps


def global_sum(local_value):
    for step in sum_steps(("gx", "gy")):
        local_value = step(local_value)
    return local_value


def advance(carry, value, step=True):
    total, steps = carry
    if step and steps:
        total = steps[0](total)
        steps = steps[1:]
    total, value = lax.optimization_barrier((total, value))
    return (total, steps), value


def finish(carry):
    total, steps = carry
    for step in steps:
        total = step(total)
    return total


def with_rim(field, width=4):
    return extended(field, (("gx", 1), ("gy", 2)), width)


def lane_sum(values):
    return jnp.sum(values.reshape(-1, 128), axis=0)


def interior(field):
    return field[:, 4:-4, 4:-4]


def shards(right_side, prior_weight, jacobi_inverse, interaction, footprint):
    highest = lax.Precision.HIGH
    layers, tile_rows, tile_cols = right_side.shape
    sensors, rows_blocks, cols_blocks = (footprint.shape[0], footprint.shape[1], footprint.shape[2])
    block_rows = tile_rows // rows_blocks
    block_cols = tile_cols // cols_blocks
    owners = lax.axis_size("gy")
    layer_blocks_cols = cols_blocks * owners
    requests = sensors * rows_blocks * cols_blocks * layers
    capacity = requests // owners + 1
    own_blocks = layers * rows_blocks * cols_blocks
    synth_rows = synth_table(tile_rows)
    synth_cols = synth_table(tile_cols)
    analysis_rows = analysis_table(tile_rows + 8)
    analysis_cols = analysis_table(tile_cols + 8)
    flat_ids = footprint.reshape(requests)
    request_num = jnp.arange(requests, dtype=jnp.int32)
    layer_of = request_num % layers
    sensor_of = request_num // (requests // sensors)
    target = flat_ids % layer_blocks_cols // cols_blocks
    owned_index = (
        layer_of * (rows_blocks * cols_blocks)
        + flat_ids // layer_blocks_cols % rows_blocks * cols_blocks
        + flat_ids % layer_blocks_cols % cols_blocks
    )
    picks = (target[:, None] == jnp.arange(owners, dtype=jnp.int32)[None, :]).astype(jnp.int32)
    slot = jnp.sum(picks * (jnp.cumsum(picks, axis=0) - 1), axis=1)
    hit = (target[:, None, None] == jnp.arange(owners, dtype=jnp.int32)[None, :, None]) & (
        slot[:, None, None] == jnp.arange(capacity, dtype=jnp.int32)[None, None, :]
    )
    used = jnp.any(hit, axis=0)
    send_ids = jnp.where(
        used, jnp.sum(jnp.where(hit, owned_index[:, None, None], 0), axis=0), own_blocks
    )
    wanted_ids = lax.all_to_all(send_ids, "gy", split_axis=0, concat_axis=0, tiled=True)
    slot_source = jnp.where(
        used, jnp.sum(jnp.where(hit, request_num[:, None, None], 0), axis=0), requests
    )
    own_layer = wanted_ids // (rows_blocks * cols_blocks)
    own_row = wanted_ids % (rows_blocks * cols_blocks) // cols_blocks
    own_col = wanted_ids % cols_blocks
    gather_ids = jnp.where(
        wanted_ids < own_blocks,
        own_layer * (rows_blocks * cols_blocks) + own_col * rows_blocks + own_row,
        own_blocks,
    )
    landing = (
        gather_ids.reshape(-1)[None, :] == jnp.arange(own_blocks, dtype=jnp.int32)[:, None]
    ).astype(jnp.float32)
    def apply_op(direction, partials):
        along_rows = jnp.einsum("lab,ac->lcb", direction, synth_rows, precision=highest)
        blocks = jnp.einsum(
            "lab,bjc->ljac",
            along_rows,
            synth_cols.reshape(-1, cols_blocks, block_cols),
            precision=highest,
        ).reshape(own_blocks, block_rows, block_cols)
        blocks = jnp.concatenate([blocks, jnp.zeros((1, block_rows, block_cols), blocks.dtype)])
        outgoing = jnp.take(blocks, gather_ids, axis=0, mode="clip")
        arrived = lax.all_to_all(outgoing, "gy", split_axis=0, concat_axis=0, tiled=True)
        seen = arrived[target, slot].reshape(
            sensors, rows_blocks * cols_blocks, layers, block_rows, block_cols
        )
        slopes = jnp.einsum("sklxy,slyz->skxz", seen, interaction, precision=highest)
        carry = (partials(slopes), sum_steps(("gx", "gy")))
        back = jnp.einsum("skxz,slyz->sklxy", slopes, interaction, precision=highest).reshape(
            requests, block_rows, block_cols
        )
        back = jnp.concatenate([back, jnp.zeros((1, block_rows, block_cols), back.dtype)])
        returning = jnp.take(back, slot_source, axis=0, mode="clip")
        carry, returning = advance(carry, returning)
        landed = lax.all_to_all(returning, "gy", split_axis=0, concat_axis=0, tiled=True)
        carry, landed = advance(carry, landed, step=False)
        summed = jnp.dot(
            landing, landed.reshape(owners * capacity, block_rows * block_cols), precision=highest
        )
        carry, summed = advance(carry, summed)
        padded = extended(
            summed.reshape(layers, cols_blocks, tile_rows, block_cols), (("gx", 2),), 8
        )
        carry, padded = advance(carry, padded)
        count = lax.axis_size("gy")
        forward = [(i, i + 1) for i in range(count - 1)]
        backward = [(target, source) for source, target in forward]
        left = lax.ppermute(padded[:, cols_blocks - 1, :, block_cols - 8 :], "gy", forward)
        right = lax.ppermute(padded[:, 0, :, :8], "gy", backward)
        along_cols = (
            jnp.einsum(
                "ljac,jcd->lad",
                padded,
                analysis_cols[8 : 8 + tile_cols].reshape(cols_blocks, block_cols, -1),
                precision=highest,
            )
            + jnp.einsum("lab,bc->lac", left, analysis_cols[:8], precision=highest)
            + jnp.einsum("lab,bc->lac", right, analysis_cols[8 + tile_cols :], precision=highest)
        )
        carry, along_cols = advance(carry, along_cols)
        return (
            jnp.einsum("lab,ac->lcb", along_cols, analysis_rows, precision=highest)
            + prior_weight * direction
        ), slopes, jnp.sum(finish(carry), axis=1)

    rims = with_rim(jnp.concatenate([right_side, jacobi_inverse, prior_weight]))
    residual, jacobi_inverse, prior_weight = jnp.split(rims, 3)
    solution = jnp.zeros_like(right_side)
    prior_inner = interior(prior_weight)
    precond_res = jacobi_inverse * residual
    direction = interior(precond_res)
    image, direction_slopes, totals = apply_op(
        precond_res,
        lambda slopes: jnp.stack(
            [
                lane_sum(interior(residual) * direction),
                lane_sum(slopes * slopes),
                lane_sum(prior_inner * direction * direction),
            ]
        ),
    )
    rho_now = totals[0]
    step_size = rho_now / (totals[1] + totals[2])
    for step in range(ITERS):
        solution = solution + step_size * direction
        residual = residual - step_size * image
        if step + 1 < ITERS:
            precond_res = jacobi_inverse * residual
            inner = interior(precond_res)
            applied, slopes_now, totals = apply_op(
                precond_res,
                lambda slopes: jnp.stack(
                    [
                        lane_sum(interior(residual) * inner),
                        lane_sum(slopes * slopes),
                        lane_sum(slopes * direction_slopes),
                        lane_sum(direction_slopes * direction_slopes),
                        lane_sum(prior_inner * inner * inner),
                        lane_sum(prior_inner * inner * direction),
                        lane_sum(prior_inner * direction * direction),
                    ]
                ),
            )
            rho_next = totals[0]
            ratio = rho_next / rho_now
            curvature = (totals[1] + 2.0 * ratio * totals[2] + ratio * ratio * totals[3]) + (
                totals[4] + 2.0 * ratio * totals[5] + ratio * ratio * totals[6]
            )
            step_size = rho_next / curvature
            direction = inner + ratio * direction
            direction_slopes = slopes_now + ratio * direction_slopes
            image = applied + ratio * image
            rho_now = rho_next
    residual = interior(residual)
    return (solution, residual)


def solution(mesh):
    return jax.shard_map(
        shards,
        mesh=mesh,
        in_specs=(
            P(None, "gx", "gy"),
            P(None, "gx", "gy"),
            P(None, "gx", "gy"),
            P(),
            P(None, "gx", "gy", None),
        ),
        out_specs=(P(None, "gx", "gy"), P(None, "gx", "gy")),
        check_vma=False,
    )
```

```python
import jax
import jax.numpy as jnp
from jax import lax
from jax.sharding import PartitionSpec as P

ITERS = 4


DAUB_LOW = (
    0.3326705529509569,
    0.8068915093133388,
    0.4598775021193313,
    -0.13501102001039084,
    -0.08544127388224149,
    0.035226291882100656,
)
DAUB_HIGH = tuple(((-1.0) ** tap_index * DAUB_LOW[5 - tap_index] for tap_index in range(6)))


def extended(block, sides, width):
    for axis, dim in sides:
        count = lax.axis_size(axis)
        forward = [(i, i + 1) for i in range(count - 1)]
        backward = [(target, source) for source, target in forward]
        low = lax.ppermute(
            lax.slice_in_dim(block, block.shape[dim] - width, None, axis=dim), axis, forward
        )
        high = lax.ppermute(lax.slice_in_dim(block, 0, width, axis=dim), axis, backward)
        block = jnp.concatenate([low, block, high], axis=dim)
    return block


def synth_table(length):
    inputs = jnp.arange(length + 8, dtype=jnp.int32)[:, None]
    outputs = jnp.arange(length, dtype=jnp.int32)[None, :]
    half = outputs // 2
    phase = outputs % 2
    table = jnp.zeros((length + 8, length), jnp.float32)
    for tap_num in range(3):
        low_coef = jnp.where(phase == 0, DAUB_LOW[2 * tap_num], DAUB_LOW[2 * tap_num + 1])
        high_coef = jnp.where(phase == 0, DAUB_HIGH[2 * tap_num], DAUB_HIGH[2 * tap_num + 1])
        table = table + jnp.where(inputs == 2 * (half - tap_num) + 4, low_coef, 0.0)
        table = table + jnp.where(inputs == 2 * (half - tap_num) + 5, high_coef, 0.0)
    return table


def analysis_table(length):
    inputs = jnp.arange(length + 8, dtype=jnp.int32)[:, None]
    outputs = jnp.arange(length, dtype=jnp.int32)[None, :]
    half = outputs // 2
    phase = outputs % 2
    table = jnp.zeros((length + 8, length), jnp.float32)
    for tap_num in range(3):
        for offset in (0, 1):
            coef = jnp.where(
                phase == 0, DAUB_LOW[2 * tap_num + offset], DAUB_HIGH[2 * tap_num + offset]
            )
            table = table + jnp.where(inputs == 2 * (half + tap_num) + offset + 4, coef, 0.0)
    return table


def butterfly_sum(value, axis):
    count = lax.axis_size(axis)
    if count & (count - 1):
        return lax.psum(value, axis)
    stride = 1
    while stride < count:
        value = value + lax.ppermute(value, axis, [(i, i ^ stride) for i in range(count)])
        stride *= 2
    return value


def sum_steps(axes):
    steps = []
    for axis in axes:
        count = lax.axis_size(axis)
        if count & (count - 1):
            steps.append(lambda value, axis=axis: lax.psum(value, axis))
            continue
        stride = 1
        while stride < count:
            pairs = [(i, i ^ stride) for i in range(count)]
            steps.append(lambda value, axis=axis, pairs=pairs: value + lax.ppermute(value, axis, pairs))
            stride *= 2
    return steps


def global_sum(local_value):
    for step in sum_steps(("gx", "gy")):
        local_value = step(local_value)
    return local_value


def advance(carry, value, step=True):
    total, steps = carry
    if step and steps:
        total = steps[0](total)
        steps = steps[1:]
    total, value = lax.optimization_barrier((total, value))
    return (total, steps), value


def finish(carry):
    total, steps = carry
    for step in steps:
        total = step(total)
    return total


def with_rim(field, width=4):
    return extended(field, (("gx", 1), ("gy", 2)), width)


def lane_sum(values):
    return jnp.sum(values.reshape(-1, 128), axis=0)


def interior(field):
    return field[:, 4:-4, 4:-4]


def shards(right_side, prior_weight, jacobi_inverse, interaction, footprint):
    highest = lax.Precision.HIGH
    layers, tile_rows, tile_cols = right_side.shape
    sensors, rows_blocks, cols_blocks = (footprint.shape[0], footprint.shape[1], footprint.shape[2])
    block_rows = tile_rows // rows_blocks
    block_cols = tile_cols // cols_blocks
    owners = lax.axis_size("gy")
    layer_blocks_cols = cols_blocks * owners
    requests = sensors * rows_blocks * cols_blocks * layers
    capacity = requests // owners + 1
    own_blocks = layers * rows_blocks * cols_blocks
    synth_rows = synth_table(tile_rows)
    synth_cols = synth_table(tile_cols)
    analysis_rows = analysis_table(tile_rows + 8)
    analysis_cols = analysis_table(tile_cols + 8)
    flat_ids = footprint.reshape(requests)
    request_num = jnp.arange(requests, dtype=jnp.int32)
    layer_of = request_num % layers
    sensor_of = request_num // (requests // sensors)
    target = flat_ids % layer_blocks_cols // cols_blocks
    owned_index = (
        layer_of * (rows_blocks * cols_blocks)
        + flat_ids // layer_blocks_cols % rows_blocks * cols_blocks
        + flat_ids % layer_blocks_cols % cols_blocks
    )
    picks = (target[:, None] == jnp.arange(owners, dtype=jnp.int32)[None, :]).astype(jnp.int32)
    slot = jnp.sum(picks * (jnp.cumsum(picks, axis=0) - 1), axis=1)
    hit = (target[:, None, None] == jnp.arange(owners, dtype=jnp.int32)[None, :, None]) & (
        slot[:, None, None] == jnp.arange(capacity, dtype=jnp.int32)[None, None, :]
    )
    used = jnp.any(hit, axis=0)
    send_ids = jnp.where(
        used, jnp.sum(jnp.where(hit, owned_index[:, None, None], 0), axis=0), own_blocks
    )
    wanted_ids = lax.all_to_all(send_ids, "gy", split_axis=0, concat_axis=0, tiled=True)
    slot_source = jnp.where(
        used, jnp.sum(jnp.where(hit, request_num[:, None, None], 0), axis=0), requests
    )
    own_layer = wanted_ids // (rows_blocks * cols_blocks)
    own_row = wanted_ids % (rows_blocks * cols_blocks) // cols_blocks
    own_col = wanted_ids % cols_blocks
    gather_ids = jnp.where(
        wanted_ids < own_blocks,
        own_layer * (rows_blocks * cols_blocks) + own_col * rows_blocks + own_row,
        own_blocks,
    )
    landing = (
        gather_ids.reshape(-1)[None, :] == jnp.arange(own_blocks, dtype=jnp.int32)[:, None]
    ).astype(jnp.float32)
    def apply_op(direction, partials):
        along_rows = jnp.einsum("lab,ac->lcb", direction, synth_rows, precision=highest)
        blocks = jnp.einsum(
            "lab,bjc->ljac",
            along_rows,
            synth_cols.reshape(-1, cols_blocks, block_cols),
            precision=highest,
        ).reshape(own_blocks, block_rows, block_cols)
        outgoing = jnp.einsum(
            "bk,bxc->kxc", landing, blocks, precision=lax.Precision.HIGHEST
        ).reshape(owners, capacity, block_rows, block_cols)
        arrived = lax.all_to_all(outgoing, "gy", split_axis=0, concat_axis=0, tiled=True)
        seen = arrived[target, slot].reshape(
            sensors, rows_blocks * cols_blocks, layers, block_rows, block_cols
        )
        slopes = jnp.einsum("sklxy,slyz->skxz", seen, interaction, precision=highest)
        carry = (partials(slopes), sum_steps(("gx", "gy")))
        back = jnp.einsum("skxz,slyz->sklxy", slopes, interaction, precision=highest).reshape(
            requests, block_rows, block_cols
        )
        back = jnp.concatenate([back, jnp.zeros((1, block_rows, block_cols), back.dtype)])
        returning = jnp.take(back, slot_source, axis=0, mode="clip")
        carry, returning = advance(carry, returning)
        landed = lax.all_to_all(returning, "gy", split_axis=0, concat_axis=0, tiled=True)
        carry, landed = advance(carry, landed, step=False)
        summed = jnp.einsum(
            "bk,kxc->bxc",
            landing,
            landed.reshape(owners * capacity, block_rows, block_cols),
            precision=highest,
        )
        carry, summed = advance(carry, summed)
        padded = extended(
            summed.reshape(layers, cols_blocks, tile_rows, block_cols), (("gx", 2),), 8
        )
        carry, padded = advance(carry, padded)
        count = lax.axis_size("gy")
        forward = [(i, i + 1) for i in range(count - 1)]
        backward = [(target, source) for source, target in forward]
        left = lax.ppermute(padded[:, cols_blocks - 1, :, block_cols - 8 :], "gy", forward)
        right = lax.ppermute(padded[:, 0, :, :8], "gy", backward)
        along_cols = (
            jnp.einsum(
                "ljac,jcd->lad",
                padded,
                analysis_cols[8 : 8 + tile_cols].reshape(cols_blocks, block_cols, -1),
                precision=highest,
            )
            + jnp.einsum("lab,bc->lac", left, analysis_cols[:8], precision=highest)
            + jnp.einsum("lab,bc->lac", right, analysis_cols[8 + tile_cols :], precision=highest)
        )
        carry, along_cols = advance(carry, along_cols)
        return (
            jnp.einsum("lab,ac->lcb", along_cols, analysis_rows, precision=highest)
            + prior_weight * direction
        ), slopes, jnp.sum(finish(carry), axis=1)

    rims = with_rim(jnp.concatenate([right_side, jacobi_inverse, prior_weight]))
    residual, jacobi_inverse, prior_weight = jnp.split(rims, 3)
    solution = jnp.zeros_like(right_side)
    prior_inner = interior(prior_weight)
    precond_res = jacobi_inverse * residual
    direction = interior(precond_res)
    image, direction_slopes, totals = apply_op(
        precond_res,
        lambda slopes: jnp.stack(
            [
                lane_sum(interior(residual) * direction),
                lane_sum(slopes * slopes),
                lane_sum(prior_inner * direction * direction),
            ]
        ),
    )
    rho_now = totals[0]
    step_size = rho_now / (totals[1] + totals[2])
    for step in range(ITERS):
        solution = solution + step_size * direction
        residual = residual - step_size * image
        if step + 1 < ITERS:
            precond_res = jacobi_inverse * residual
            inner = interior(precond_res)
            applied, slopes_now, totals = apply_op(
                precond_res,
                lambda slopes: jnp.stack(
                    [
                        lane_sum(interior(residual) * inner),
                        lane_sum(slopes * slopes),
                        lane_sum(slopes * direction_slopes),
                        lane_sum(direction_slopes * direction_slopes),
                        lane_sum(prior_inner * inner * inner),
                        lane_sum(prior_inner * inner * direction),
                        lane_sum(prior_inner * direction * direction),
                    ]
                ),
            )
            rho_next = totals[0]
            ratio = rho_next / rho_now
            curvature = (totals[1] + 2.0 * ratio * totals[2] + ratio * ratio * totals[3]) + (
                totals[4] + 2.0 * ratio * totals[5] + ratio * ratio * totals[6]
            )
            step_size = rho_next / curvature
            direction = inner + ratio * direction
            direction_slopes = slopes_now + ratio * direction_slopes
            image = applied + ratio * image
            rho_now = rho_next
    residual = interior(residual)
    return (solution, residual)


def solution(mesh):
    return jax.shard_map(
        shards,
        mesh=mesh,
        in_specs=(
            P(None, "gx", "gy"),
            P(None, "gx", "gy"),
            P(None, "gx", "gy"),
            P(),
            P(None, "gx", "gy", None),
        ),
        out_specs=(P(None, "gx", "gy"), P(None, "gx", "gy")),
        check_vma=False,
    )
```

```python
import jax
import numpy as np
import jax.numpy as jnp
from jax import lax
from jax.sharding import PartitionSpec as P

ITERS = 4


DAUB_LOW = (
    0.3326705529509569,
    0.8068915093133388,
    0.4598775021193313,
    -0.13501102001039084,
    -0.08544127388224149,
    0.035226291882100656,
)
DAUB_HIGH = tuple(((-1.0) ** tap_index * DAUB_LOW[5 - tap_index] for tap_index in range(6)))


def extended(block, sides, width):
    for axis, dim in sides:
        count = lax.axis_size(axis)
        forward = [(i, i + 1) for i in range(count - 1)]
        backward = [(target, source) for source, target in forward]
        low = lax.ppermute(
            lax.slice_in_dim(block, block.shape[dim] - width, None, axis=dim), axis, forward
        )
        high = lax.ppermute(lax.slice_in_dim(block, 0, width, axis=dim), axis, backward)
        block = jnp.concatenate([low, block, high], axis=dim)
    return block


def synth_table(length):
    inputs = np.arange(length + 8, dtype=np.int64)[:, None]
    outputs = np.arange(length, dtype=np.int64)[None, :]
    half = outputs // 2
    phase = outputs % 2
    table = np.zeros((length + 8, length), np.float64)
    for tap_num in range(3):
        low_coef = np.where(phase == 0, DAUB_LOW[2 * tap_num], DAUB_LOW[2 * tap_num + 1])
        high_coef = np.where(phase == 0, DAUB_HIGH[2 * tap_num], DAUB_HIGH[2 * tap_num + 1])
        table = table + np.where(inputs == 2 * (half - tap_num) + 4, low_coef, 0.0)
        table = table + np.where(inputs == 2 * (half - tap_num) + 5, high_coef, 0.0)
    return table.astype(np.float32)


def analysis_table(length):
    inputs = np.arange(length + 8, dtype=np.int64)[:, None]
    outputs = np.arange(length, dtype=np.int64)[None, :]
    half = outputs // 2
    phase = outputs % 2
    table = np.zeros((length + 8, length), np.float64)
    for tap_num in range(3):
        for offset in (0, 1):
            coef = np.where(
                phase == 0, DAUB_LOW[2 * tap_num + offset], DAUB_HIGH[2 * tap_num + offset]
            )
            table = table + np.where(inputs == 2 * (half + tap_num) + offset + 4, coef, 0.0)
    return table.astype(np.float32)


def butterfly_sum(value, axis):
    count = lax.axis_size(axis)
    if count & (count - 1):
        return lax.psum(value, axis)
    stride = 1
    while stride < count:
        value = value + lax.ppermute(value, axis, [(i, i ^ stride) for i in range(count)])
        stride *= 2
    return value


def sum_steps(axes):
    steps = []
    for axis in axes:
        count = lax.axis_size(axis)
        if count & (count - 1):
            steps.append(lambda value, axis=axis: lax.psum(value, axis))
            continue
        stride = 1
        while stride < count:
            pairs = [(i, i ^ stride) for i in range(count)]
            steps.append(lambda value, axis=axis, pairs=pairs: value + lax.ppermute(value, axis, pairs))
            stride *= 2
    return steps


def global_sum(local_value):
    for step in sum_steps(("gx", "gy")):
        local_value = step(local_value)
    return local_value


def advance(carry, value, step=True):
    total, steps = carry
    if step and steps:
        total = steps[0](total)
        steps = steps[1:]
    total, value = lax.optimization_barrier((total, value))
    return (total, steps), value


def finish(carry):
    total, steps = carry
    for step in steps:
        total = step(total)
    return total


def with_rim(field, width=4):
    return extended(field, (("gx", 1), ("gy", 2)), width)


def lane_sum(values):
    return jnp.sum(values.reshape(-1, 128), axis=0)


def interior(field):
    return field[:, 4:-4, 4:-4]


def shards(right_side, prior_weight, jacobi_inverse, interaction, footprint):
    highest = lax.Precision.HIGH
    layers, tile_rows, tile_cols = right_side.shape
    sensors, rows_blocks, cols_blocks = (footprint.shape[0], footprint.shape[1], footprint.shape[2])
    block_rows = tile_rows // rows_blocks
    block_cols = tile_cols // cols_blocks
    owners = lax.axis_size("gy")
    layer_blocks_cols = cols_blocks * owners
    requests = sensors * rows_blocks * cols_blocks * layers
    capacity = requests // owners + 1
    own_blocks = layers * rows_blocks * cols_blocks
    synth_rows = synth_table(tile_rows)
    synth_cols = synth_table(tile_cols)
    analysis_rows = analysis_table(tile_rows + 8)
    analysis_cols = analysis_table(tile_cols + 8)
    flat_ids = footprint.reshape(requests)
    request_num = jnp.arange(requests, dtype=jnp.int32)
    layer_of = request_num % layers
    sensor_of = request_num // (requests // sensors)
    target = flat_ids % layer_blocks_cols // cols_blocks
    owned_index = (
        layer_of * (rows_blocks * cols_blocks)
        + flat_ids // layer_blocks_cols % rows_blocks * cols_blocks
        + flat_ids % layer_blocks_cols % cols_blocks
    )
    picks = (target[:, None] == jnp.arange(owners, dtype=jnp.int32)[None, :]).astype(jnp.int32)
    slot = jnp.sum(picks * (jnp.cumsum(picks, axis=0) - 1), axis=1)
    hit = (target[:, None, None] == jnp.arange(owners, dtype=jnp.int32)[None, :, None]) & (
        slot[:, None, None] == jnp.arange(capacity, dtype=jnp.int32)[None, None, :]
    )
    used = jnp.any(hit, axis=0)
    send_ids = jnp.where(
        used, jnp.sum(jnp.where(hit, owned_index[:, None, None], 0), axis=0), own_blocks
    )
    wanted_ids = lax.all_to_all(send_ids, "gy", split_axis=0, concat_axis=0, tiled=True)
    slot_source = jnp.where(
        used, jnp.sum(jnp.where(hit, request_num[:, None, None], 0), axis=0), requests
    )
    own_layer = wanted_ids // (rows_blocks * cols_blocks)
    own_row = wanted_ids % (rows_blocks * cols_blocks) // cols_blocks
    own_col = wanted_ids % cols_blocks
    gather_ids = jnp.where(
        wanted_ids < own_blocks,
        own_layer * (rows_blocks * cols_blocks) + own_col * rows_blocks + own_row,
        own_blocks,
    )
    landing = (
        gather_ids.reshape(-1)[None, :] == jnp.arange(own_blocks, dtype=jnp.int32)[:, None]
    ).astype(jnp.float32)
    def apply_op(direction, partials):
        along_rows = jnp.einsum("lab,ac->lcb", direction, synth_rows, precision=highest)
        blocks = jnp.einsum(
            "lab,bjc->ljac",
            along_rows,
            synth_cols.reshape(-1, cols_blocks, block_cols),
            precision=highest,
        ).reshape(own_blocks, block_rows, block_cols)
        outgoing = jnp.einsum(
            "bk,bxc->kxc", landing, blocks, precision=lax.Precision.HIGHEST
        ).reshape(owners, capacity, block_rows, block_cols)
        arrived = lax.all_to_all(outgoing, "gy", split_axis=0, concat_axis=0, tiled=True)
        seen = arrived[target, slot].reshape(
            sensors, rows_blocks * cols_blocks, layers, block_rows, block_cols
        )
        slopes = jnp.einsum("sklxy,slyz->skxz", seen, interaction, precision=highest)
        carry = (partials(slopes), sum_steps(("gx", "gy")))
        back = jnp.einsum("skxz,slyz->sklxy", slopes, interaction, precision=highest).reshape(
            requests, block_rows, block_cols
        )
        back = jnp.concatenate([back, jnp.zeros((1, block_rows, block_cols), back.dtype)])
        returning = jnp.take(back, slot_source, axis=0, mode="clip")
        carry, returning = advance(carry, returning)
        landed = lax.all_to_all(returning, "gy", split_axis=0, concat_axis=0, tiled=True)
        carry, landed = advance(carry, landed, step=False)
        summed = jnp.einsum(
            "bk,kxc->bxc",
            landing,
            landed.reshape(owners * capacity, block_rows, block_cols),
            precision=highest,
        )
        carry, summed = advance(carry, summed)
        padded = extended(
            summed.reshape(layers, cols_blocks, tile_rows, block_cols), (("gx", 2),), 8
        )
        carry, padded = advance(carry, padded)
        count = lax.axis_size("gy")
        forward = [(i, i + 1) for i in range(count - 1)]
        backward = [(target, source) for source, target in forward]
        left = lax.ppermute(padded[:, cols_blocks - 1, :, block_cols - 8 :], "gy", forward)
        right = lax.ppermute(padded[:, 0, :, :8], "gy", backward)
        along_cols = (
            jnp.einsum(
                "ljac,jcd->lad",
                padded,
                analysis_cols[8 : 8 + tile_cols].reshape(cols_blocks, block_cols, -1),
                precision=highest,
            )
            + jnp.einsum("lab,bc->lac", left, analysis_cols[:8], precision=highest)
            + jnp.einsum("lab,bc->lac", right, analysis_cols[8 + tile_cols :], precision=highest)
        )
        carry, along_cols = advance(carry, along_cols)
        return (
            jnp.einsum("lab,ac->lcb", along_cols, analysis_rows, precision=highest)
            + prior_weight * direction
        ), slopes, jnp.sum(finish(carry), axis=1)

    rims = with_rim(jnp.concatenate([right_side, jacobi_inverse, prior_weight]))
    residual, jacobi_inverse, prior_weight = jnp.split(rims, 3)
    solution = jnp.zeros_like(right_side)
    prior_inner = interior(prior_weight)
    precond_res = jacobi_inverse * residual
    direction = interior(precond_res)
    image, direction_slopes, totals = apply_op(
        precond_res,
        lambda slopes: jnp.stack(
            [
                lane_sum(interior(residual) * direction),
                lane_sum(slopes * slopes),
                lane_sum(prior_inner * direction * direction),
            ]
        ),
    )
    rho_now = totals[0]
    step_size = rho_now / (totals[1] + totals[2])
    for step in range(ITERS):
        solution = solution + step_size * direction
        residual = residual - step_size * image
        if step + 1 < ITERS:
            precond_res = jacobi_inverse * residual
            inner = interior(precond_res)
            applied, slopes_now, totals = apply_op(
                precond_res,
                lambda slopes: jnp.stack(
                    [
                        lane_sum(interior(residual) * inner),
                        lane_sum(slopes * slopes),
                        lane_sum(slopes * direction_slopes),
                        lane_sum(direction_slopes * direction_slopes),
                        lane_sum(prior_inner * inner * inner),
                        lane_sum(prior_inner * inner * direction),
                        lane_sum(prior_inner * direction * direction),
                    ]
                ),
            )
            rho_next = totals[0]
            ratio = rho_next / rho_now
            curvature = (totals[1] + 2.0 * ratio * totals[2] + ratio * ratio * totals[3]) + (
                totals[4] + 2.0 * ratio * totals[5] + ratio * ratio * totals[6]
            )
            step_size = rho_next / curvature
            direction = inner + ratio * direction
            direction_slopes = slopes_now + ratio * direction_slopes
            image = applied + ratio * image
            rho_now = rho_next
    residual = interior(residual)
    return (solution, residual)


def solution(mesh):
    return jax.shard_map(
        shards,
        mesh=mesh,
        in_specs=(
            P(None, "gx", "gy"),
            P(None, "gx", "gy"),
            P(None, "gx", "gy"),
            P(),
            P(None, "gx", "gy", None),
        ),
        out_specs=(P(None, "gx", "gy"), P(None, "gx", "gy")),
        check_vma=False,
    )
```

```python
import jax
import numpy as np
import jax.numpy as jnp
from jax import lax
from jax.sharding import PartitionSpec as P

ITERS = 4


DAUB_LOW = (
    0.3326705529509569,
    0.8068915093133388,
    0.4598775021193313,
    -0.13501102001039084,
    -0.08544127388224149,
    0.035226291882100656,
)
DAUB_HIGH = tuple(((-1.0) ** tap_index * DAUB_LOW[5 - tap_index] for tap_index in range(6)))


def extended(block, sides, width):
    for axis, dim in sides:
        count = lax.axis_size(axis)
        forward = [(i, i + 1) for i in range(count - 1)]
        backward = [(target, source) for source, target in forward]
        low = lax.ppermute(
            lax.slice_in_dim(block, block.shape[dim] - width, None, axis=dim), axis, forward
        )
        high = lax.ppermute(lax.slice_in_dim(block, 0, width, axis=dim), axis, backward)
        block = jnp.concatenate([low, block, high], axis=dim)
    return block


def synth_table(length):
    inputs = np.arange(length + 8, dtype=np.int64)[:, None]
    outputs = np.arange(length, dtype=np.int64)[None, :]
    half = outputs // 2
    phase = outputs % 2
    table = np.zeros((length + 8, length), np.float64)
    for tap_num in range(3):
        low_coef = np.where(phase == 0, DAUB_LOW[2 * tap_num], DAUB_LOW[2 * tap_num + 1])
        high_coef = np.where(phase == 0, DAUB_HIGH[2 * tap_num], DAUB_HIGH[2 * tap_num + 1])
        table = table + np.where(inputs == 2 * (half - tap_num) + 4, low_coef, 0.0)
        table = table + np.where(inputs == 2 * (half - tap_num) + 5, high_coef, 0.0)
    return table.astype(np.float32)


def analysis_table(length):
    inputs = np.arange(length + 8, dtype=np.int64)[:, None]
    outputs = np.arange(length, dtype=np.int64)[None, :]
    half = outputs // 2
    phase = outputs % 2
    table = np.zeros((length + 8, length), np.float64)
    for tap_num in range(3):
        for offset in (0, 1):
            coef = np.where(
                phase == 0, DAUB_LOW[2 * tap_num + offset], DAUB_HIGH[2 * tap_num + offset]
            )
            table = table + np.where(inputs == 2 * (half + tap_num) + offset + 4, coef, 0.0)
    return table.astype(np.float32)


def butterfly_sum(value, axis):
    count = lax.axis_size(axis)
    if count & (count - 1):
        return lax.psum(value, axis)
    stride = 1
    while stride < count:
        value = value + lax.ppermute(value, axis, [(i, i ^ stride) for i in range(count)])
        stride *= 2
    return value


def sum_steps(axes):
    steps = []
    for axis in axes:
        count = lax.axis_size(axis)
        if count & (count - 1):
            steps.append(lambda value, axis=axis: lax.psum(value, axis))
            continue
        stride = 1
        while stride < count:
            pairs = [(i, i ^ stride) for i in range(count)]
            steps.append(lambda value, axis=axis, pairs=pairs: value + lax.ppermute(value, axis, pairs))
            stride *= 2
    return steps


def global_sum(local_value):
    for step in sum_steps(("gx", "gy")):
        local_value = step(local_value)
    return local_value


def advance(carry, value, step=True):
    total, steps = carry
    if step and steps:
        total = steps[0](total)
        steps = steps[1:]
    total, value = lax.optimization_barrier((total, value))
    return (total, steps), value


def finish(carry):
    total, steps = carry
    for step in steps:
        total = step(total)
    return total


def with_rim(field, width=4):
    return extended(field, (("gx", 1), ("gy", 2)), width)


def lane_sum(values):
    return jnp.sum(values.reshape(-1, 128), axis=0)


def interior(field):
    return field[:, 4:-4, 4:-4]


def shards(right_side, prior_weight, jacobi_inverse, interaction, footprint):
    highest = lax.Precision.HIGH
    layers, tile_rows, tile_cols = right_side.shape
    sensors, rows_blocks, cols_blocks = (footprint.shape[0], footprint.shape[1], footprint.shape[2])
    block_rows = tile_rows // rows_blocks
    block_cols = tile_cols // cols_blocks
    owners = lax.axis_size("gy")
    layer_blocks_cols = cols_blocks * owners
    requests = sensors * rows_blocks * cols_blocks * layers
    capacity = requests // owners + 1
    own_blocks = layers * rows_blocks * cols_blocks
    synth_rows = synth_table(tile_rows)
    synth_cols = synth_table(tile_cols)
    analysis_rows = analysis_table(tile_rows + 8)
    analysis_cols = analysis_table(tile_cols + 8)
    flat_ids = footprint.reshape(requests)
    request_num = jnp.arange(requests, dtype=jnp.int32)
    layer_of = request_num % layers
    sensor_of = request_num // (requests // sensors)
    target = flat_ids % layer_blocks_cols // cols_blocks
    owned_index = (
        layer_of * (rows_blocks * cols_blocks)
        + flat_ids // layer_blocks_cols % rows_blocks * cols_blocks
        + flat_ids % layer_blocks_cols % cols_blocks
    )
    picks = (target[:, None] == jnp.arange(owners, dtype=jnp.int32)[None, :]).astype(jnp.int32)
    slot = jnp.sum(picks * (jnp.cumsum(picks, axis=0) - 1), axis=1)
    hit = (target[:, None, None] == jnp.arange(owners, dtype=jnp.int32)[None, :, None]) & (
        slot[:, None, None] == jnp.arange(capacity, dtype=jnp.int32)[None, None, :]
    )
    used = jnp.any(hit, axis=0)
    send_ids = jnp.where(
        used, jnp.sum(jnp.where(hit, owned_index[:, None, None], 0), axis=0), own_blocks
    )
    wanted_ids = lax.all_to_all(send_ids, "gy", split_axis=0, concat_axis=0, tiled=True)
    slot_source = jnp.where(
        used, jnp.sum(jnp.where(hit, request_num[:, None, None], 0), axis=0), requests
    )
    own_layer = wanted_ids // (rows_blocks * cols_blocks)
    own_row = wanted_ids % (rows_blocks * cols_blocks) // cols_blocks
    own_col = wanted_ids % cols_blocks
    gather_ids = jnp.where(
        wanted_ids < own_blocks,
        own_layer * (rows_blocks * cols_blocks) + own_col * rows_blocks + own_row,
        own_blocks,
    )
    picking = (
        (target * capacity + slot)[:, None]
        == jnp.arange(owners * capacity, dtype=jnp.int32)[None, :]
    ).astype(jnp.float32)
    landing = (
        gather_ids.reshape(-1)[None, :] == jnp.arange(own_blocks, dtype=jnp.int32)[:, None]
    ).astype(jnp.float32)
    def apply_op(direction, partials):
        along_rows = jnp.einsum("lab,ac->lcb", direction, synth_rows, precision=highest)
        blocks = jnp.einsum(
            "lab,bjc->ljac",
            along_rows,
            synth_cols.reshape(-1, cols_blocks, block_cols),
            precision=highest,
        ).reshape(own_blocks, block_rows, block_cols)
        outgoing = jnp.einsum(
            "bk,bxc->kxc", landing, blocks, precision=lax.Precision.HIGHEST
        ).reshape(owners, capacity, block_rows, block_cols)
        arrived = lax.all_to_all(outgoing, "gy", split_axis=0, concat_axis=0, tiled=True)
        seen = arrived[target, slot].reshape(
            sensors, rows_blocks * cols_blocks, layers, block_rows, block_cols
        )
        slopes = jnp.einsum("sklxy,slyz->skxz", seen, interaction, precision=highest)
        carry = (partials(slopes), sum_steps(("gx", "gy")))
        back = jnp.einsum("skxz,slyz->sklxy", slopes, interaction, precision=highest).reshape(
            requests, block_rows, block_cols
        )
        returning = jnp.einsum(
            "ek,exc->kxc", picking, back, precision=lax.Precision.HIGHEST
        ).reshape(owners, capacity, block_rows, block_cols)
        carry, returning = advance(carry, returning)
        landed = lax.all_to_all(returning, "gy", split_axis=0, concat_axis=0, tiled=True)
        carry, landed = advance(carry, landed, step=False)
        summed = jnp.einsum(
            "bk,kxc->bxc",
            landing,
            landed.reshape(owners * capacity, block_rows, block_cols),
            precision=highest,
        )
        carry, summed = advance(carry, summed)
        padded = extended(
            summed.reshape(layers, cols_blocks, tile_rows, block_cols), (("gx", 2),), 8
        )
        carry, padded = advance(carry, padded)
        count = lax.axis_size("gy")
        forward = [(i, i + 1) for i in range(count - 1)]
        backward = [(target, source) for source, target in forward]
        left = lax.ppermute(padded[:, cols_blocks - 1, :, block_cols - 8 :], "gy", forward)
        right = lax.ppermute(padded[:, 0, :, :8], "gy", backward)
        along_cols = (
            jnp.einsum(
                "ljac,jcd->lad",
                padded,
                analysis_cols[8 : 8 + tile_cols].reshape(cols_blocks, block_cols, -1),
                precision=highest,
            )
            + jnp.einsum("lab,bc->lac", left, analysis_cols[:8], precision=highest)
            + jnp.einsum("lab,bc->lac", right, analysis_cols[8 + tile_cols :], precision=highest)
        )
        carry, along_cols = advance(carry, along_cols)
        return (
            jnp.einsum("lab,ac->lcb", along_cols, analysis_rows, precision=highest)
            + prior_weight * direction
        ), slopes, jnp.sum(finish(carry), axis=1)

    rims = with_rim(jnp.concatenate([right_side, jacobi_inverse, prior_weight]))
    residual, jacobi_inverse, prior_weight = jnp.split(rims, 3)
    solution = jnp.zeros_like(right_side)
    prior_inner = interior(prior_weight)
    precond_res = jacobi_inverse * residual
    direction = interior(precond_res)
    image, direction_slopes, totals = apply_op(
        precond_res,
        lambda slopes: jnp.stack(
            [
                lane_sum(interior(residual) * direction),
                lane_sum(slopes * slopes),
                lane_sum(prior_inner * direction * direction),
            ]
        ),
    )
    rho_now = totals[0]
    step_size = rho_now / (totals[1] + totals[2])
    for step in range(ITERS):
        solution = solution + step_size * direction
        residual = residual - step_size * image
        if step + 1 < ITERS:
            precond_res = jacobi_inverse * residual
            inner = interior(precond_res)
            applied, slopes_now, totals = apply_op(
                precond_res,
                lambda slopes: jnp.stack(
                    [
                        lane_sum(interior(residual) * inner),
                        lane_sum(slopes * slopes),
                        lane_sum(slopes * direction_slopes),
                        lane_sum(direction_slopes * direction_slopes),
                        lane_sum(prior_inner * inner * inner),
                        lane_sum(prior_inner * inner * direction),
                        lane_sum(prior_inner * direction * direction),
                    ]
                ),
            )
            rho_next = totals[0]
            ratio = rho_next / rho_now
            curvature = (totals[1] + 2.0 * ratio * totals[2] + ratio * ratio * totals[3]) + (
                totals[4] + 2.0 * ratio * totals[5] + ratio * ratio * totals[6]
            )
            step_size = rho_next / curvature
            direction = inner + ratio * direction
            direction_slopes = slopes_now + ratio * direction_slopes
            image = applied + ratio * image
            rho_now = rho_next
    residual = interior(residual)
    return (solution, residual)


def solution(mesh):
    return jax.shard_map(
        shards,
        mesh=mesh,
        in_specs=(
            P(None, "gx", "gy"),
            P(None, "gx", "gy"),
            P(None, "gx", "gy"),
            P(),
            P(None, "gx", "gy", None),
        ),
        out_specs=(P(None, "gx", "gy"), P(None, "gx", "gy")),
        check_vma=False,
    )
```

```python
import jax
import numpy as np
import jax.numpy as jnp
from jax import lax
from jax.sharding import PartitionSpec as P

ITERS = 4


DAUB_LOW = (
    0.3326705529509569,
    0.8068915093133388,
    0.4598775021193313,
    -0.13501102001039084,
    -0.08544127388224149,
    0.035226291882100656,
)
DAUB_HIGH = tuple(((-1.0) ** tap_index * DAUB_LOW[5 - tap_index] for tap_index in range(6)))


def extended(block, sides, width):
    for axis, dim in sides:
        count = lax.axis_size(axis)
        forward = [(i, i + 1) for i in range(count - 1)]
        backward = [(target, source) for source, target in forward]
        low = lax.ppermute(
            lax.slice_in_dim(block, block.shape[dim] - width, None, axis=dim), axis, forward
        )
        high = lax.ppermute(lax.slice_in_dim(block, 0, width, axis=dim), axis, backward)
        block = jnp.concatenate([low, block, high], axis=dim)
    return block


def synth_table(length):
    inputs = np.arange(length + 8, dtype=np.int64)[:, None]
    outputs = np.arange(length, dtype=np.int64)[None, :]
    half = outputs // 2
    phase = outputs % 2
    table = np.zeros((length + 8, length), np.float64)
    for tap_num in range(3):
        low_coef = np.where(phase == 0, DAUB_LOW[2 * tap_num], DAUB_LOW[2 * tap_num + 1])
        high_coef = np.where(phase == 0, DAUB_HIGH[2 * tap_num], DAUB_HIGH[2 * tap_num + 1])
        table = table + np.where(inputs == 2 * (half - tap_num) + 4, low_coef, 0.0)
        table = table + np.where(inputs == 2 * (half - tap_num) + 5, high_coef, 0.0)
    return table.astype(np.float32)


def analysis_table(length):
    inputs = np.arange(length + 8, dtype=np.int64)[:, None]
    outputs = np.arange(length, dtype=np.int64)[None, :]
    half = outputs // 2
    phase = outputs % 2
    table = np.zeros((length + 8, length), np.float64)
    for tap_num in range(3):
        for offset in (0, 1):
            coef = np.where(
                phase == 0, DAUB_LOW[2 * tap_num + offset], DAUB_HIGH[2 * tap_num + offset]
            )
            table = table + np.where(inputs == 2 * (half + tap_num) + offset + 4, coef, 0.0)
    return table.astype(np.float32)


def butterfly_sum(value, axis):
    count = lax.axis_size(axis)
    if count & (count - 1):
        return lax.psum(value, axis)
    stride = 1
    while stride < count:
        value = value + lax.ppermute(value, axis, [(i, i ^ stride) for i in range(count)])
        stride *= 2
    return value


def sum_steps(axes):
    steps = []
    for axis in axes:
        count = lax.axis_size(axis)
        if count & (count - 1):
            steps.append(lambda value, axis=axis: lax.psum(value, axis))
            continue
        stride = 1
        while stride < count:
            pairs = [(i, i ^ stride) for i in range(count)]
            steps.append(lambda value, axis=axis, pairs=pairs: value + lax.ppermute(value, axis, pairs))
            stride *= 2
    return steps


def global_sum(local_value):
    for step in sum_steps(("gx", "gy")):
        local_value = step(local_value)
    return local_value


def advance(carry, value, step=True):
    total, steps = carry
    if step and steps:
        total = steps[0](total)
        steps = steps[1:]
    total, value = lax.optimization_barrier((total, value))
    return (total, steps), value


def finish(carry):
    total, steps = carry
    for step in steps:
        total = step(total)
    return total


def with_rim(field, width=4):
    return extended(field, (("gx", 1), ("gy", 2)), width)


def lane_sum(values):
    return jnp.sum(values.reshape(-1, 128), axis=0)


def interior(field):
    return field[:, 4:-4, 4:-4]


def shards(right_side, prior_weight, jacobi_inverse, interaction, footprint):
    highest = lax.Precision.HIGH
    layers, tile_rows, tile_cols = right_side.shape
    sensors, rows_blocks, cols_blocks = (footprint.shape[0], footprint.shape[1], footprint.shape[2])
    block_rows = tile_rows // rows_blocks
    block_cols = tile_cols // cols_blocks
    owners = lax.axis_size("gy")
    layer_blocks_cols = cols_blocks * owners
    requests = sensors * rows_blocks * cols_blocks * layers
    capacity = requests // owners + 1
    own_blocks = layers * rows_blocks * cols_blocks
    synth_rows = synth_table(tile_rows)
    synth_cols = synth_table(tile_cols)
    analysis_rows = analysis_table(tile_rows + 8)
    analysis_cols = analysis_table(tile_cols + 8)
    flat_ids = footprint.reshape(requests)
    request_num = jnp.arange(requests, dtype=jnp.int32)
    layer_of = request_num % layers
    sensor_of = request_num // (requests // sensors)
    target = flat_ids % layer_blocks_cols // cols_blocks
    owned_index = (
        layer_of * (rows_blocks * cols_blocks)
        + flat_ids // layer_blocks_cols % rows_blocks * cols_blocks
        + flat_ids % layer_blocks_cols % cols_blocks
    )
    picks = (target[:, None] == jnp.arange(owners, dtype=jnp.int32)[None, :]).astype(jnp.int32)
    slot = jnp.sum(picks * (jnp.cumsum(picks, axis=0) - 1), axis=1)
    hit = (target[:, None, None] == jnp.arange(owners, dtype=jnp.int32)[None, :, None]) & (
        slot[:, None, None] == jnp.arange(capacity, dtype=jnp.int32)[None, None, :]
    )
    used = jnp.any(hit, axis=0)
    send_ids = jnp.where(
        used, jnp.sum(jnp.where(hit, owned_index[:, None, None], 0), axis=0), own_blocks
    )
    wanted_ids = lax.all_to_all(send_ids, "gy", split_axis=0, concat_axis=0, tiled=True)
    slot_source = jnp.where(
        used, jnp.sum(jnp.where(hit, request_num[:, None, None], 0), axis=0), requests
    )
    own_layer = wanted_ids // (rows_blocks * cols_blocks)
    own_row = wanted_ids % (rows_blocks * cols_blocks) // cols_blocks
    own_col = wanted_ids % cols_blocks
    gather_ids = jnp.where(
        wanted_ids < own_blocks,
        own_layer * (rows_blocks * cols_blocks) + own_col * rows_blocks + own_row,
        own_blocks,
    )
    picking = (
        (target * capacity + slot)[:, None]
        == jnp.arange(owners * capacity, dtype=jnp.int32)[None, :]
    ).astype(jnp.float32)
    landing = (
        gather_ids.reshape(-1)[None, :] == jnp.arange(own_blocks, dtype=jnp.int32)[:, None]
    ).astype(jnp.float32)
    def apply_op(direction, partials):
        along_rows = jnp.einsum("lab,ac->lcb", direction, synth_rows, precision=highest)
        blocks = jnp.einsum(
            "lab,bjc->ljac",
            along_rows,
            synth_cols.reshape(-1, cols_blocks, block_cols),
            precision=highest,
        ).reshape(own_blocks, block_rows, block_cols)
        outgoing = jnp.einsum(
            "bk,bxc->kxc", landing, blocks, precision=lax.Precision.HIGHEST
        ).reshape(owners, capacity, block_rows, block_cols)
        arrived = lax.all_to_all(outgoing, "gy", split_axis=0, concat_axis=0, tiled=True)
        seen = jnp.einsum(
            "ek,kxc->exc",
            picking,
            arrived.reshape(owners * capacity, block_rows, block_cols),
            precision=lax.Precision.HIGHEST,
        ).reshape(sensors, rows_blocks * cols_blocks, layers, block_rows, block_cols)
        slopes = jnp.einsum("sklxy,slyz->skxz", seen, interaction, precision=highest)
        carry = (partials(slopes), sum_steps(("gx", "gy")))
        back = jnp.einsum("skxz,slyz->sklxy", slopes, interaction, precision=highest).reshape(
            requests, block_rows, block_cols
        )
        returning = jnp.einsum(
            "ek,exc->kxc", picking, back, precision=lax.Precision.HIGHEST
        ).reshape(owners, capacity, block_rows, block_cols)
        carry, returning = advance(carry, returning)
        landed = lax.all_to_all(returning, "gy", split_axis=0, concat_axis=0, tiled=True)
        carry, landed = advance(carry, landed, step=False)
        summed = jnp.einsum(
            "bk,kxc->bxc",
            landing,
            landed.reshape(owners * capacity, block_rows, block_cols),
            precision=highest,
        )
        carry, summed = advance(carry, summed)
        padded = extended(
            summed.reshape(layers, cols_blocks, tile_rows, block_cols), (("gx", 2),), 8
        )
        carry, padded = advance(carry, padded)
        count = lax.axis_size("gy")
        forward = [(i, i + 1) for i in range(count - 1)]
        backward = [(target, source) for source, target in forward]
        left = lax.ppermute(padded[:, cols_blocks - 1, :, block_cols - 8 :], "gy", forward)
        right = lax.ppermute(padded[:, 0, :, :8], "gy", backward)
        along_cols = (
            jnp.einsum(
                "ljac,jcd->lad",
                padded,
                analysis_cols[8 : 8 + tile_cols].reshape(cols_blocks, block_cols, -1),
                precision=highest,
            )
            + jnp.einsum("lab,bc->lac", left, analysis_cols[:8], precision=highest)
            + jnp.einsum("lab,bc->lac", right, analysis_cols[8 + tile_cols :], precision=highest)
        )
        carry, along_cols = advance(carry, along_cols)
        return (
            jnp.einsum("lab,ac->lcb", along_cols, analysis_rows, precision=highest)
            + prior_weight * direction
        ), slopes, jnp.sum(finish(carry), axis=1)

    rims = with_rim(jnp.concatenate([right_side, jacobi_inverse, prior_weight]))
    residual, jacobi_inverse, prior_weight = jnp.split(rims, 3)
    solution = jnp.zeros_like(right_side)
    prior_inner = interior(prior_weight)
    precond_res = jacobi_inverse * residual
    direction = interior(precond_res)
    image, direction_slopes, totals = apply_op(
        precond_res,
        lambda slopes: jnp.stack(
            [
                lane_sum(interior(residual) * direction),
                lane_sum(slopes * slopes),
                lane_sum(prior_inner * direction * direction),
            ]
        ),
    )
    rho_now = totals[0]
    step_size = rho_now / (totals[1] + totals[2])
    for step in range(ITERS):
        solution = solution + step_size * direction
        residual = residual - step_size * image
        if step + 1 < ITERS:
            precond_res = jacobi_inverse * residual
            inner = interior(precond_res)
            applied, slopes_now, totals = apply_op(
                precond_res,
                lambda slopes: jnp.stack(
                    [
                        lane_sum(interior(residual) * inner),
                        lane_sum(slopes * slopes),
                        lane_sum(slopes * direction_slopes),
                        lane_sum(direction_slopes * direction_slopes),
                        lane_sum(prior_inner * inner * inner),
                        lane_sum(prior_inner * inner * direction),
                        lane_sum(prior_inner * direction * direction),
                    ]
                ),
            )
            rho_next = totals[0]
            ratio = rho_next / rho_now
            curvature = (totals[1] + 2.0 * ratio * totals[2] + ratio * ratio * totals[3]) + (
                totals[4] + 2.0 * ratio * totals[5] + ratio * ratio * totals[6]
            )
            step_size = rho_next / curvature
            direction = inner + ratio * direction
            direction_slopes = slopes_now + ratio * direction_slopes
            image = applied + ratio * image
            rho_now = rho_next
    residual = interior(residual)
    return (solution, residual)


def solution(mesh):
    return jax.shard_map(
        shards,
        mesh=mesh,
        in_specs=(
            P(None, "gx", "gy"),
            P(None, "gx", "gy"),
            P(None, "gx", "gy"),
            P(),
            P(None, "gx", "gy", None),
        ),
        out_specs=(P(None, "gx", "gy"), P(None, "gx", "gy")),
        check_vma=False,
    )
```

```python
import jax
import numpy as np
import jax.numpy as jnp
from jax import lax
from jax.sharding import PartitionSpec as P

ITERS = 4


DAUB_LOW = (
    0.3326705529509569,
    0.8068915093133388,
    0.4598775021193313,
    -0.13501102001039084,
    -0.08544127388224149,
    0.035226291882100656,
)
DAUB_HIGH = tuple(((-1.0) ** tap_index * DAUB_LOW[5 - tap_index] for tap_index in range(6)))


def extended(block, sides, width):
    for axis, dim in sides:
        count = lax.axis_size(axis)
        forward = [(i, i + 1) for i in range(count - 1)]
        backward = [(target, source) for source, target in forward]
        low = lax.ppermute(
            lax.slice_in_dim(block, block.shape[dim] - width, None, axis=dim), axis, forward
        )
        high = lax.ppermute(lax.slice_in_dim(block, 0, width, axis=dim), axis, backward)
        block = jnp.concatenate([low, block, high], axis=dim)
    return block


def synth_table(length):
    inputs = np.arange(length + 8, dtype=np.int64)[:, None]
    outputs = np.arange(length, dtype=np.int64)[None, :]
    half = outputs // 2
    phase = outputs % 2
    table = np.zeros((length + 8, length), np.float64)
    for tap_num in range(3):
        low_coef = np.where(phase == 0, DAUB_LOW[2 * tap_num], DAUB_LOW[2 * tap_num + 1])
        high_coef = np.where(phase == 0, DAUB_HIGH[2 * tap_num], DAUB_HIGH[2 * tap_num + 1])
        table = table + np.where(inputs == 2 * (half - tap_num) + 4, low_coef, 0.0)
        table = table + np.where(inputs == 2 * (half - tap_num) + 5, high_coef, 0.0)
    return table.astype(np.float32)


def analysis_table(length):
    inputs = np.arange(length + 8, dtype=np.int64)[:, None]
    outputs = np.arange(length, dtype=np.int64)[None, :]
    half = outputs // 2
    phase = outputs % 2
    table = np.zeros((length + 8, length), np.float64)
    for tap_num in range(3):
        for offset in (0, 1):
            coef = np.where(
                phase == 0, DAUB_LOW[2 * tap_num + offset], DAUB_HIGH[2 * tap_num + offset]
            )
            table = table + np.where(inputs == 2 * (half + tap_num) + offset + 4, coef, 0.0)
    return table.astype(np.float32)


def butterfly_sum(value, axis):
    count = lax.axis_size(axis)
    if count & (count - 1):
        return lax.psum(value, axis)
    stride = 1
    while stride < count:
        value = value + lax.ppermute(value, axis, [(i, i ^ stride) for i in range(count)])
        stride *= 2
    return value


def sum_steps(axes):
    steps = []
    for axis in axes:
        count = lax.axis_size(axis)
        if count & (count - 1):
            steps.append(lambda value, axis=axis: lax.psum(value, axis))
            continue
        stride = 1
        while stride < count:
            pairs = [(i, i ^ stride) for i in range(count)]
            steps.append(lambda value, axis=axis, pairs=pairs: value + lax.ppermute(value, axis, pairs))
            stride *= 2
    return steps


def global_sum(local_value):
    for step in sum_steps(("gx", "gy")):
        local_value = step(local_value)
    return local_value


def advance(carry, value, step=True):
    total, steps = carry
    if step and steps:
        total = steps[0](total)
        steps = steps[1:]
    total, value = lax.optimization_barrier((total, value))
    return (total, steps), value


def finish(carry):
    total, steps = carry
    for step in steps:
        total = step(total)
    return total


def with_rim(field, width=4):
    return extended(field, (("gx", 1), ("gy", 2)), width)


def lane_sum(values):
    return jnp.sum(values.reshape(-1, 128), axis=0)


def interior(field):
    return field[:, 4:-4, 4:-4]


def shards(right_side, prior_weight, jacobi_inverse, interaction, footprint):
    highest = lax.Precision.HIGH
    layers, tile_rows, tile_cols = right_side.shape
    sensors, rows_blocks, cols_blocks = (footprint.shape[0], footprint.shape[1], footprint.shape[2])
    block_rows = tile_rows // rows_blocks
    block_cols = tile_cols // cols_blocks
    owners = lax.axis_size("gy")
    layer_blocks_cols = cols_blocks * owners
    requests = sensors * rows_blocks * cols_blocks * layers
    capacity = requests // owners + 1
    own_blocks = layers * rows_blocks * cols_blocks
    synth_rows = synth_table(tile_rows)
    synth_cols = synth_table(tile_cols)
    analysis_rows = analysis_table(tile_rows + 8)
    analysis_cols = analysis_table(tile_cols + 8)
    flat_ids = footprint.reshape(requests)
    request_num = jnp.arange(requests, dtype=jnp.int32)
    layer_of = request_num % layers
    sensor_of = request_num // (requests // sensors)
    target = flat_ids % layer_blocks_cols // cols_blocks
    owned_index = (
        layer_of * (rows_blocks * cols_blocks)
        + flat_ids // layer_blocks_cols % rows_blocks * cols_blocks
        + flat_ids % layer_blocks_cols % cols_blocks
    )
    picks = (target[:, None] == jnp.arange(owners, dtype=jnp.int32)[None, :]).astype(jnp.int32)
    slot = jnp.sum(picks * (jnp.cumsum(picks, axis=0) - 1), axis=1)
    hit = (target[:, None, None] == jnp.arange(owners, dtype=jnp.int32)[None, :, None]) & (
        slot[:, None, None] == jnp.arange(capacity, dtype=jnp.int32)[None, None, :]
    )
    used = jnp.any(hit, axis=0)
    send_ids = jnp.where(
        used, jnp.sum(jnp.where(hit, owned_index[:, None, None], 0), axis=0), own_blocks
    )
    wanted_ids = lax.all_to_all(send_ids, "gy", split_axis=0, concat_axis=0, tiled=True)
    slot_source = jnp.where(
        used, jnp.sum(jnp.where(hit, request_num[:, None, None], 0), axis=0), requests
    )
    own_layer = wanted_ids // (rows_blocks * cols_blocks)
    own_row = wanted_ids % (rows_blocks * cols_blocks) // cols_blocks
    own_col = wanted_ids % cols_blocks
    gather_ids = jnp.where(
        wanted_ids < own_blocks,
        own_layer * (rows_blocks * cols_blocks) + own_col * rows_blocks + own_row,
        own_blocks,
    )
    picking = (
        (target * capacity + slot)[:, None]
        == jnp.arange(owners * capacity, dtype=jnp.int32)[None, :]
    ).astype(jnp.float32)
    landing = (
        gather_ids.reshape(-1)[None, :] == jnp.arange(own_blocks, dtype=jnp.int32)[:, None]
    ).astype(jnp.float32)
    def apply_op(direction, partials):
        along_rows = jnp.einsum("lab,ac->lcb", direction, synth_rows, precision=highest)
        blocks = jnp.einsum(
            "lab,bjc->ljac",
            along_rows,
            synth_cols.reshape(-1, cols_blocks, block_cols),
            precision=highest,
        ).reshape(own_blocks, block_rows, block_cols)
        outgoing = jnp.einsum(
            "bk,bxc->kxc", landing, blocks, precision=lax.Precision.HIGHEST
        ).reshape(owners, capacity, block_rows, block_cols)
        arrived = lax.all_to_all(outgoing, "gy", split_axis=0, concat_axis=0, tiled=True)
        seen = jnp.einsum(
            "ek,kxc->exc",
            picking,
            arrived.reshape(owners * capacity, block_rows, block_cols),
            precision=lax.Precision.HIGHEST,
        ).reshape(sensors, rows_blocks * cols_blocks, layers, block_rows, block_cols)
        slopes = jnp.einsum("sklxy,slyz->skxz", seen, interaction, precision=highest)
        carry = (partials(slopes), sum_steps(("gx", "gy")))
        back = jnp.einsum("skxz,slyz->sklxy", slopes, interaction, precision=highest).reshape(
            requests, block_rows, block_cols
        )
        returning = jnp.einsum(
            "ek,exc->kxc", picking, back, precision=lax.Precision.HIGHEST
        ).reshape(owners, capacity, block_rows, block_cols)
        carry, returning = advance(carry, returning)
        landed = lax.all_to_all(returning, "gy", split_axis=0, concat_axis=0, tiled=True)
        carry, landed = advance(carry, landed, step=False)
        summed = jnp.einsum(
            "bk,kxc->bxc",
            landing,
            landed.reshape(owners * capacity, block_rows, block_cols),
            precision=highest,
        )
        carry, summed = advance(carry, summed)
        inner_part = summed.reshape(layers, cols_blocks, tile_rows, block_cols)
        gx_count = lax.axis_size("gx")
        gx_forward = [(i, i + 1) for i in range(gx_count - 1)]
        gx_backward = [(target, source) for source, target in gx_forward]
        top = lax.ppermute(inner_part[:, :, tile_rows - 8 :], "gx", gx_forward)
        bottom = lax.ppermute(inner_part[:, :, :8], "gx", gx_backward)
        carry, (top, bottom) = advance(carry, (top, bottom))
        count = lax.axis_size("gy")
        forward = [(i, i + 1) for i in range(count - 1)]
        backward = [(target, source) for source, target in forward]
        parts = (top, inner_part, bottom)
        left = lax.ppermute(
            jnp.concatenate([part[:, cols_blocks - 1, :, block_cols - 8 :] for part in parts], axis=1),
            "gy",
            forward,
        )
        right = lax.ppermute(
            jnp.concatenate([part[:, 0, :, :8] for part in parts], axis=1), "gy", backward
        )
        middle = analysis_cols[8 : 8 + tile_cols].reshape(cols_blocks, block_cols, -1)
        row_bounds = ((0, 8), (8, 8 + tile_rows), (8 + tile_rows, 16 + tile_rows))
        sides = jnp.einsum("lab,bc->lac", left, analysis_cols[:8], precision=highest) + jnp.einsum(
            "lab,bc->lac", right, analysis_cols[8 + tile_cols :], precision=highest
        )
        along_cols = jnp.einsum("lab,ac->lcb", sides, analysis_rows, precision=highest)
        for part, (low, high) in zip(parts, row_bounds):
            along_cols = along_cols + jnp.einsum(
                "lab,ac->lcb",
                jnp.einsum("ljac,jcd->lad", part, middle, precision=highest),
                analysis_rows[low:high],
                precision=highest,
            )
        carry, along_cols = advance(carry, along_cols)
        return (
            along_cols + prior_weight * direction
        ), slopes, jnp.sum(finish(carry), axis=1)

    rims = with_rim(jnp.concatenate([right_side, jacobi_inverse, prior_weight]))
    residual, jacobi_inverse, prior_weight = jnp.split(rims, 3)
    solution = jnp.zeros_like(right_side)
    prior_inner = interior(prior_weight)
    precond_res = jacobi_inverse * residual
    direction = interior(precond_res)
    image, direction_slopes, totals = apply_op(
        precond_res,
        lambda slopes: jnp.stack(
            [
                lane_sum(interior(residual) * direction),
                lane_sum(slopes * slopes),
                lane_sum(prior_inner * direction * direction),
            ]
        ),
    )
    rho_now = totals[0]
    step_size = rho_now / (totals[1] + totals[2])
    for step in range(ITERS):
        solution = solution + step_size * direction
        residual = residual - step_size * image
        if step + 1 < ITERS:
            precond_res = jacobi_inverse * residual
            inner = interior(precond_res)
            applied, slopes_now, totals = apply_op(
                precond_res,
                lambda slopes: jnp.stack(
                    [
                        lane_sum(interior(residual) * inner),
                        lane_sum(slopes * slopes),
                        lane_sum(slopes * direction_slopes),
                        lane_sum(direction_slopes * direction_slopes),
                        lane_sum(prior_inner * inner * inner),
                        lane_sum(prior_inner * inner * direction),
                        lane_sum(prior_inner * direction * direction),
                    ]
                ),
            )
            rho_next = totals[0]
            ratio = rho_next / rho_now
            curvature = (totals[1] + 2.0 * ratio * totals[2] + ratio * ratio * totals[3]) + (
                totals[4] + 2.0 * ratio * totals[5] + ratio * ratio * totals[6]
            )
            step_size = rho_next / curvature
            direction = inner + ratio * direction
            direction_slopes = slopes_now + ratio * direction_slopes
            image = applied + ratio * image
            rho_now = rho_next
    residual = interior(residual)
    return (solution, residual)


def solution(mesh):
    return jax.shard_map(
        shards,
        mesh=mesh,
        in_specs=(
            P(None, "gx", "gy"),
            P(None, "gx", "gy"),
            P(None, "gx", "gy"),
            P(),
            P(None, "gx", "gy", None),
        ),
        out_specs=(P(None, "gx", "gy"), P(None, "gx", "gy")),
        check_vma=False,
    )
```

```python
import jax
import numpy as np
import jax.numpy as jnp
from jax import lax
from jax.sharding import PartitionSpec as P

ITERS = 4


DAUB_LOW = (
    0.3326705529509569,
    0.8068915093133388,
    0.4598775021193313,
    -0.13501102001039084,
    -0.08544127388224149,
    0.035226291882100656,
)
DAUB_HIGH = tuple(((-1.0) ** tap_index * DAUB_LOW[5 - tap_index] for tap_index in range(6)))


def extended(block, sides, width):
    for axis, dim in sides:
        count = lax.axis_size(axis)
        forward = [(i, i + 1) for i in range(count - 1)]
        backward = [(target, source) for source, target in forward]
        low = lax.ppermute(
            lax.slice_in_dim(block, block.shape[dim] - width, None, axis=dim), axis, forward
        )
        high = lax.ppermute(lax.slice_in_dim(block, 0, width, axis=dim), axis, backward)
        block = jnp.concatenate([low, block, high], axis=dim)
    return block


def synth_table(length):
    inputs = np.arange(length + 8, dtype=np.int64)[:, None]
    outputs = np.arange(length, dtype=np.int64)[None, :]
    half = outputs // 2
    phase = outputs % 2
    table = np.zeros((length + 8, length), np.float64)
    for tap_num in range(3):
        low_coef = np.where(phase == 0, DAUB_LOW[2 * tap_num], DAUB_LOW[2 * tap_num + 1])
        high_coef = np.where(phase == 0, DAUB_HIGH[2 * tap_num], DAUB_HIGH[2 * tap_num + 1])
        table = table + np.where(inputs == 2 * (half - tap_num) + 4, low_coef, 0.0)
        table = table + np.where(inputs == 2 * (half - tap_num) + 5, high_coef, 0.0)
    return table.astype(np.float32)


def analysis_table(length):
    inputs = np.arange(length + 8, dtype=np.int64)[:, None]
    outputs = np.arange(length, dtype=np.int64)[None, :]
    half = outputs // 2
    phase = outputs % 2
    table = np.zeros((length + 8, length), np.float64)
    for tap_num in range(3):
        for offset in (0, 1):
            coef = np.where(
                phase == 0, DAUB_LOW[2 * tap_num + offset], DAUB_HIGH[2 * tap_num + offset]
            )
            table = table + np.where(inputs == 2 * (half + tap_num) + offset + 4, coef, 0.0)
    return table.astype(np.float32)


def butterfly_sum(value, axis):
    count = lax.axis_size(axis)
    if count & (count - 1):
        return lax.psum(value, axis)
    stride = 1
    while stride < count:
        value = value + lax.ppermute(value, axis, [(i, i ^ stride) for i in range(count)])
        stride *= 2
    return value


def sum_steps(axes):
    steps = []
    for axis in axes:
        count = lax.axis_size(axis)
        if count & (count - 1):
            steps.append(lambda value, axis=axis: lax.psum(value, axis))
            continue
        stride = 1
        while stride < count:
            pairs = [(i, i ^ stride) for i in range(count)]
            steps.append(lambda value, axis=axis, pairs=pairs: value + lax.ppermute(value, axis, pairs))
            stride *= 2
    return steps


def global_sum(local_value):
    for step in sum_steps(("gx", "gy")):
        local_value = step(local_value)
    return local_value


def advance(carry, value, step=True):
    total, steps = carry
    if step and steps:
        total = steps[0](total)
        steps = steps[1:]
    total, value = lax.optimization_barrier((total, value))
    return (total, steps), value


def finish(carry):
    total, steps = carry
    for step in steps:
        total = step(total)
    return total


def with_rim(field, width=4):
    return extended(field, (("gx", 1), ("gy", 2)), width)


def lane_sum(values):
    return jnp.sum(values.reshape(-1, 128), axis=0)


def interior(field):
    return field[:, 4:-4, 4:-4]


def shards(right_side, prior_weight, jacobi_inverse, interaction, footprint):
    highest = lax.Precision.HIGH
    layers, tile_rows, tile_cols = right_side.shape
    sensors, rows_blocks, cols_blocks = (footprint.shape[0], footprint.shape[1], footprint.shape[2])
    block_rows = tile_rows // rows_blocks
    block_cols = tile_cols // cols_blocks
    owners = lax.axis_size("gy")
    layer_blocks_cols = cols_blocks * owners
    requests = sensors * rows_blocks * cols_blocks * layers
    capacity = requests // owners + 1
    own_blocks = layers * rows_blocks * cols_blocks
    synth_rows = synth_table(tile_rows)
    synth_cols = synth_table(tile_cols)
    analysis_rows = analysis_table(tile_rows + 8)
    analysis_cols = analysis_table(tile_cols + 8)
    flat_ids = footprint.reshape(requests)
    request_num = jnp.arange(requests, dtype=jnp.int32)
    layer_of = request_num % layers
    sensor_of = request_num // (requests // sensors)
    target = flat_ids % layer_blocks_cols // cols_blocks
    owned_index = (
        layer_of * (rows_blocks * cols_blocks)
        + flat_ids // layer_blocks_cols % rows_blocks * cols_blocks
        + flat_ids % layer_blocks_cols % cols_blocks
    )
    picks = (target[:, None] == jnp.arange(owners, dtype=jnp.int32)[None, :]).astype(jnp.int32)
    slot = jnp.sum(picks * (jnp.cumsum(picks, axis=0) - 1), axis=1)
    hit = (target[:, None, None] == jnp.arange(owners, dtype=jnp.int32)[None, :, None]) & (
        slot[:, None, None] == jnp.arange(capacity, dtype=jnp.int32)[None, None, :]
    )
    used = jnp.any(hit, axis=0)
    send_ids = jnp.where(
        used, jnp.sum(jnp.where(hit, owned_index[:, None, None], 0), axis=0), own_blocks
    )
    wanted_ids = lax.all_to_all(send_ids, "gy", split_axis=0, concat_axis=0, tiled=True)
    slot_source = jnp.where(
        used, jnp.sum(jnp.where(hit, request_num[:, None, None], 0), axis=0), requests
    )
    own_layer = wanted_ids // (rows_blocks * cols_blocks)
    own_row = wanted_ids % (rows_blocks * cols_blocks) // cols_blocks
    own_col = wanted_ids % cols_blocks
    gather_ids = jnp.where(
        wanted_ids < own_blocks,
        own_layer * (rows_blocks * cols_blocks) + own_col * rows_blocks + own_row,
        own_blocks,
    )
    picking = (
        (target * capacity + slot)[:, None]
        == jnp.arange(owners * capacity, dtype=jnp.int32)[None, :]
    ).astype(jnp.float32)
    landing = (
        gather_ids.reshape(-1)[None, :] == jnp.arange(own_blocks, dtype=jnp.int32)[:, None]
    ).astype(jnp.float32)
    def apply_op(direction, partials):
        along_rows = jnp.einsum("lab,ac->lcb", direction, synth_rows, precision=highest)
        blocks = jnp.einsum(
            "lab,bjc->ljac",
            along_rows,
            synth_cols.reshape(-1, cols_blocks, block_cols),
            precision=highest,
        ).reshape(own_blocks, block_rows, block_cols)
        outgoing = jnp.einsum(
            "bk,bxc->kxc", landing, blocks, precision=lax.Precision.HIGHEST
        ).reshape(owners, capacity, block_rows, block_cols)
        arrived = lax.all_to_all(outgoing, "gy", split_axis=0, concat_axis=0, tiled=True)
        seen = jnp.einsum(
            "ek,kxc->exc",
            picking,
            arrived.reshape(owners * capacity, block_rows, block_cols),
            precision=highest,
        ).reshape(sensors, rows_blocks * cols_blocks, layers, block_rows, block_cols)
        slopes = jnp.einsum("sklxy,slyz->skxz", seen, interaction, precision=highest)
        carry = (partials(slopes), sum_steps(("gx", "gy")))
        back = jnp.einsum("skxz,slyz->sklxy", slopes, interaction, precision=highest).reshape(
            requests, block_rows, block_cols
        )
        returning = jnp.einsum(
            "ek,exc->kxc", picking, back, precision=highest
        ).reshape(owners, capacity, block_rows, block_cols)
        carry, returning = advance(carry, returning)
        landed = lax.all_to_all(returning, "gy", split_axis=0, concat_axis=0, tiled=True)
        carry, landed = advance(carry, landed, step=False)
        summed = jnp.einsum(
            "bk,kxc->bxc",
            landing,
            landed.reshape(owners * capacity, block_rows, block_cols),
            precision=highest,
        )
        carry, summed = advance(carry, summed)
        padded = extended(
            summed.reshape(layers, cols_blocks, tile_rows, block_cols), (("gx", 2),), 8
        )
        carry, padded = advance(carry, padded)
        count = lax.axis_size("gy")
        forward = [(i, i + 1) for i in range(count - 1)]
        backward = [(target, source) for source, target in forward]
        left = lax.ppermute(padded[:, cols_blocks - 1, :, block_cols - 8 :], "gy", forward)
        right = lax.ppermute(padded[:, 0, :, :8], "gy", backward)
        along_cols = (
            jnp.einsum(
                "ljac,jcd->lad",
                padded,
                analysis_cols[8 : 8 + tile_cols].reshape(cols_blocks, block_cols, -1),
                precision=highest,
            )
            + jnp.einsum("lab,bc->lac", left, analysis_cols[:8], precision=highest)
            + jnp.einsum("lab,bc->lac", right, analysis_cols[8 + tile_cols :], precision=highest)
        )
        carry, along_cols = advance(carry, along_cols)
        return (
            jnp.einsum("lab,ac->lcb", along_cols, analysis_rows, precision=highest)
            + prior_weight * direction
        ), slopes, jnp.sum(finish(carry), axis=1)

    rims = with_rim(jnp.concatenate([right_side, jacobi_inverse, prior_weight]))
    residual, jacobi_inverse, prior_weight = jnp.split(rims, 3)
    solution = jnp.zeros_like(right_side)
    prior_inner = interior(prior_weight)
    precond_res = jacobi_inverse * residual
    direction = interior(precond_res)
    image, direction_slopes, totals = apply_op(
        precond_res,
        lambda slopes: jnp.stack(
            [
                lane_sum(interior(residual) * direction),
                lane_sum(slopes * slopes),
                lane_sum(prior_inner * direction * direction),
            ]
        ),
    )
    rho_now = totals[0]
    step_size = rho_now / (totals[1] + totals[2])
    for step in range(ITERS):
        solution = solution + step_size * direction
        residual = residual - step_size * image
        if step + 1 < ITERS:
            precond_res = jacobi_inverse * residual
            inner = interior(precond_res)
            applied, slopes_now, totals = apply_op(
                precond_res,
                lambda slopes: jnp.stack(
                    [
                        lane_sum(interior(residual) * inner),
                        lane_sum(slopes * slopes),
                        lane_sum(slopes * direction_slopes),
                        lane_sum(direction_slopes * direction_slopes),
                        lane_sum(prior_inner * inner * inner),
                        lane_sum(prior_inner * inner * direction),
                        lane_sum(prior_inner * direction * direction),
                    ]
                ),
            )
            rho_next = totals[0]
            ratio = rho_next / rho_now
            curvature = (totals[1] + 2.0 * ratio * totals[2] + ratio * ratio * totals[3]) + (
                totals[4] + 2.0 * ratio * totals[5] + ratio * ratio * totals[6]
            )
            step_size = rho_next / curvature
            direction = inner + ratio * direction
            direction_slopes = slopes_now + ratio * direction_slopes
            image = applied + ratio * image
            rho_now = rho_next
    residual = interior(residual)
    return (solution, residual)


def solution(mesh):
    return jax.shard_map(
        shards,
        mesh=mesh,
        in_specs=(
            P(None, "gx", "gy"),
            P(None, "gx", "gy"),
            P(None, "gx", "gy"),
            P(),
            P(None, "gx", "gy", None),
        ),
        out_specs=(P(None, "gx", "gy"), P(None, "gx", "gy")),
        check_vma=False,
    )
```

```python
import jax
import numpy as np
import jax.numpy as jnp
from jax import lax
from jax.sharding import PartitionSpec as P

ITERS = 4


DAUB_LOW = (
    0.3326705529509569,
    0.8068915093133388,
    0.4598775021193313,
    -0.13501102001039084,
    -0.08544127388224149,
    0.035226291882100656,
)
DAUB_HIGH = tuple(((-1.0) ** tap_index * DAUB_LOW[5 - tap_index] for tap_index in range(6)))


def extended(block, sides, width):
    for axis, dim in sides:
        count = lax.axis_size(axis)
        forward = [(i, i + 1) for i in range(count - 1)]
        backward = [(target, source) for source, target in forward]
        low = lax.ppermute(
            lax.slice_in_dim(block, block.shape[dim] - width, None, axis=dim), axis, forward
        )
        high = lax.ppermute(lax.slice_in_dim(block, 0, width, axis=dim), axis, backward)
        block = jnp.concatenate([low, block, high], axis=dim)
    return block


def synth_table(length):
    inputs = np.arange(length + 8, dtype=np.int64)[:, None]
    outputs = np.arange(length, dtype=np.int64)[None, :]
    half = outputs // 2
    phase = outputs % 2
    table = np.zeros((length + 8, length), np.float64)
    for tap_num in range(3):
        low_coef = np.where(phase == 0, DAUB_LOW[2 * tap_num], DAUB_LOW[2 * tap_num + 1])
        high_coef = np.where(phase == 0, DAUB_HIGH[2 * tap_num], DAUB_HIGH[2 * tap_num + 1])
        table = table + np.where(inputs == 2 * (half - tap_num) + 4, low_coef, 0.0)
        table = table + np.where(inputs == 2 * (half - tap_num) + 5, high_coef, 0.0)
    return table.astype(np.float32)


def analysis_table(length):
    inputs = np.arange(length + 8, dtype=np.int64)[:, None]
    outputs = np.arange(length, dtype=np.int64)[None, :]
    half = outputs // 2
    phase = outputs % 2
    table = np.zeros((length + 8, length), np.float64)
    for tap_num in range(3):
        for offset in (0, 1):
            coef = np.where(
                phase == 0, DAUB_LOW[2 * tap_num + offset], DAUB_HIGH[2 * tap_num + offset]
            )
            table = table + np.where(inputs == 2 * (half + tap_num) + offset + 4, coef, 0.0)
    return table.astype(np.float32)


def butterfly_sum(value, axis):
    count = lax.axis_size(axis)
    if count & (count - 1):
        return lax.psum(value, axis)
    stride = 1
    while stride < count:
        value = value + lax.ppermute(value, axis, [(i, i ^ stride) for i in range(count)])
        stride *= 2
    return value


def sum_steps(axes):
    steps = []
    for axis in axes:
        count = lax.axis_size(axis)
        if count & (count - 1):
            steps.append(lambda value, axis=axis: lax.psum(value, axis))
            continue
        stride = 1
        while stride < count:
            pairs = [(i, i ^ stride) for i in range(count)]
            steps.append(lambda value, axis=axis, pairs=pairs: value + lax.ppermute(value, axis, pairs))
            stride *= 2
    return steps


def global_sum(local_value):
    for step in sum_steps(("gx", "gy")):
        local_value = step(local_value)
    return local_value


def advance(carry, value, step=True):
    total, steps = carry
    if step and steps:
        total = steps[0](total)
        steps = steps[1:]
    total, value = lax.optimization_barrier((total, value))
    return (total, steps), value


def finish(carry):
    total, steps = carry
    for step in steps:
        total = step(total)
    return total


def with_rim(field, width=4):
    return extended(field, (("gx", 1), ("gy", 2)), width)


def lane_sum(values):
    return jnp.sum(values.reshape(-1, 128), axis=0)


def interior(field):
    return field[:, 4:-4, 4:-4]


def shards(right_side, prior_weight, jacobi_inverse, interaction, footprint):
    highest = lax.Precision.HIGH
    layers, tile_rows, tile_cols = right_side.shape
    sensors, rows_blocks, cols_blocks = (footprint.shape[0], footprint.shape[1], footprint.shape[2])
    block_rows = tile_rows // rows_blocks
    block_cols = tile_cols // cols_blocks
    owners = lax.axis_size("gy")
    layer_blocks_cols = cols_blocks * owners
    requests = sensors * rows_blocks * cols_blocks * layers
    capacity = requests // owners + 1
    own_blocks = layers * rows_blocks * cols_blocks
    synth_rows = synth_table(tile_rows)
    synth_cols = synth_table(tile_cols)
    analysis_rows = analysis_table(tile_rows + 8)
    analysis_cols = analysis_table(tile_cols + 8)
    flat_ids = footprint.reshape(requests)
    request_num = jnp.arange(requests, dtype=jnp.int32)
    layer_of = request_num % layers
    sensor_of = request_num // (requests // sensors)
    target = flat_ids % layer_blocks_cols // cols_blocks
    owned_index = (
        layer_of * (rows_blocks * cols_blocks)
        + flat_ids // layer_blocks_cols % rows_blocks * cols_blocks
        + flat_ids % layer_blocks_cols % cols_blocks
    )
    picks = (target[:, None] == jnp.arange(owners, dtype=jnp.int32)[None, :]).astype(jnp.int32)
    slot = jnp.sum(picks * (jnp.cumsum(picks, axis=0) - 1), axis=1)
    hit = (target[:, None, None] == jnp.arange(owners, dtype=jnp.int32)[None, :, None]) & (
        slot[:, None, None] == jnp.arange(capacity, dtype=jnp.int32)[None, None, :]
    )
    used = jnp.any(hit, axis=0)
    send_ids = jnp.where(
        used, jnp.sum(jnp.where(hit, owned_index[:, None, None], 0), axis=0), own_blocks
    )
    wanted_ids = lax.all_to_all(send_ids, "gy", split_axis=0, concat_axis=0, tiled=True)
    slot_source = jnp.where(
        used, jnp.sum(jnp.where(hit, request_num[:, None, None], 0), axis=0), requests
    )
    own_layer = wanted_ids // (rows_blocks * cols_blocks)
    own_row = wanted_ids % (rows_blocks * cols_blocks) // cols_blocks
    own_col = wanted_ids % cols_blocks
    gather_ids = jnp.where(
        wanted_ids < own_blocks,
        own_layer * (rows_blocks * cols_blocks) + own_col * rows_blocks + own_row,
        own_blocks,
    )
    picking = (
        (target * capacity + slot)[:, None]
        == jnp.arange(owners * capacity, dtype=jnp.int32)[None, :]
    ).astype(jnp.float32)
    landing = (
        gather_ids.reshape(-1)[None, :] == jnp.arange(own_blocks, dtype=jnp.int32)[:, None]
    ).astype(jnp.float32)
    def apply_op(direction, partials):
        along_rows = jnp.einsum("lab,ac->lcb", direction, synth_rows, precision=highest)
        blocks = jnp.einsum(
            "lab,bjc->ljac",
            along_rows,
            synth_cols.reshape(-1, cols_blocks, block_cols),
            precision=highest,
        ).reshape(own_blocks, block_rows, block_cols)
        outgoing = jnp.einsum(
            "bk,bxc->kxc", landing, blocks, precision=highest
        ).reshape(owners, capacity, block_rows, block_cols)
        arrived = lax.all_to_all(outgoing, "gy", split_axis=0, concat_axis=0, tiled=True)
        seen = jnp.einsum(
            "ek,kxc->exc",
            picking,
            arrived.reshape(owners * capacity, block_rows, block_cols),
            precision=highest,
        ).reshape(sensors, rows_blocks * cols_blocks, layers, block_rows, block_cols)
        slopes = jnp.einsum("sklxy,slyz->skxz", seen, interaction, precision=highest)
        carry = (partials(slopes), sum_steps(("gx", "gy")))
        back = jnp.einsum("skxz,slyz->sklxy", slopes, interaction, precision=highest).reshape(
            requests, block_rows, block_cols
        )
        returning = jnp.einsum(
            "ek,exc->kxc", picking, back, precision=highest
        ).reshape(owners, capacity, block_rows, block_cols)
        carry, returning = advance(carry, returning)
        landed = lax.all_to_all(returning, "gy", split_axis=0, concat_axis=0, tiled=True)
        carry, landed = advance(carry, landed, step=False)
        summed = jnp.einsum(
            "bk,kxc->bxc",
            landing,
            landed.reshape(owners * capacity, block_rows, block_cols),
            precision=highest,
        )
        carry, summed = advance(carry, summed)
        padded = extended(
            summed.reshape(layers, cols_blocks, tile_rows, block_cols), (("gx", 2),), 8
        )
        carry, padded = advance(carry, padded)
        count = lax.axis_size("gy")
        forward = [(i, i + 1) for i in range(count - 1)]
        backward = [(target, source) for source, target in forward]
        left = lax.ppermute(padded[:, cols_blocks - 1, :, block_cols - 8 :], "gy", forward)
        right = lax.ppermute(padded[:, 0, :, :8], "gy", backward)
        along_cols = (
            jnp.einsum(
                "ljac,jcd->lad",
                padded,
                analysis_cols[8 : 8 + tile_cols].reshape(cols_blocks, block_cols, -1),
                precision=highest,
            )
            + jnp.einsum("lab,bc->lac", left, analysis_cols[:8], precision=highest)
            + jnp.einsum("lab,bc->lac", right, analysis_cols[8 + tile_cols :], precision=highest)
        )
        carry, along_cols = advance(carry, along_cols)
        return (
            jnp.einsum("lab,ac->lcb", along_cols, analysis_rows, precision=highest)
            + prior_weight * direction
        ), slopes, jnp.sum(finish(carry), axis=1)

    rims = with_rim(jnp.concatenate([right_side, jacobi_inverse, prior_weight]))
    residual, jacobi_inverse, prior_weight = jnp.split(rims, 3)
    solution = jnp.zeros_like(right_side)
    prior_inner = interior(prior_weight)
    precond_res = jacobi_inverse * residual
    direction = interior(precond_res)
    image, direction_slopes, totals = apply_op(
        precond_res,
        lambda slopes: jnp.stack(
            [
                lane_sum(interior(residual) * direction),
                lane_sum(slopes * slopes),
                lane_sum(prior_inner * direction * direction),
            ]
        ),
    )
    rho_now = totals[0]
    step_size = rho_now / (totals[1] + totals[2])
    for step in range(ITERS):
        solution = solution + step_size * direction
        residual = residual - step_size * image
        if step + 1 < ITERS:
            precond_res = jacobi_inverse * residual
            inner = interior(precond_res)
            applied, slopes_now, totals = apply_op(
                precond_res,
                lambda slopes: jnp.stack(
                    [
                        lane_sum(interior(residual) * inner),
                        lane_sum(slopes * slopes),
                        lane_sum(slopes * direction_slopes),
                        lane_sum(direction_slopes * direction_slopes),
                        lane_sum(prior_inner * inner * inner),
                        lane_sum(prior_inner * inner * direction),
                        lane_sum(prior_inner * direction * direction),
                    ]
                ),
            )
            rho_next = totals[0]
            ratio = rho_next / rho_now
            curvature = (totals[1] + 2.0 * ratio * totals[2] + ratio * ratio * totals[3]) + (
                totals[4] + 2.0 * ratio * totals[5] + ratio * ratio * totals[6]
            )
            step_size = rho_next / curvature
            direction = inner + ratio * direction
            direction_slopes = slopes_now + ratio * direction_slopes
            image = applied + ratio * image
            rho_now = rho_next
    residual = interior(residual)
    return (solution, residual)


def solution(mesh):
    return jax.shard_map(
        shards,
        mesh=mesh,
        in_specs=(
            P(None, "gx", "gy"),
            P(None, "gx", "gy"),
            P(None, "gx", "gy"),
            P(),
            P(None, "gx", "gy", None),
        ),
        out_specs=(P(None, "gx", "gy"), P(None, "gx", "gy")),
        check_vma=False,
    )
```
